512 devices in a mesh: req: 64 (over x, y, core), tp: 8 (over z).
Axes of the slice: x: 4, y: 8, z: 8, core: 2. Of those that a mesh axis runs over, the one named last changes fastest.
Arguments:
- queries: bfloat16 [16384, 2048], P('req', 'tp'), may hold values from -10 to 10
- new_kv: bfloat16 [16384, 2048], P('req', 'tp'), may hold values from -4 to 4
- kv_pool: bfloat16 [512, 4, 256, 2048], P('req', None, None, 'tp'), may hold values from -4 to 4
- cache_lens: int32 [512], P('req'), may hold values from 2 to 1024, as said below
- parents: int32 [512, 32], P('req'), may hold values from 0 to 31, as said below
- accepted: int32 [512], P('req'), may hold values from 0 to 31, as said below
- residual: bfloat16 [16384, 4096], P(('req', 'tp')), may hold values from -3 to 3
- w_out: bfloat16 [2048, 4096], P('tp'), may hold values from -0.125 to 0.125
- norm_gain: float32 [4096], replicated, may hold values from 0.25 to 1.75
Outputs:
- hidden_out: bfloat16 [16384, 4096], P(('req', 'tp'))
- normed: bfloat16 [16384, 4096], P(('req', 'tp'))
- accepted_kv: bfloat16 [512, 8, 2048], P('req', None, 'tp')
The draws below stay inside these ranges and needn't reach their ends.
Inputs may be any that keep to these rules, and one draw needn't show every extreme that they name: parents[r, 0] = 0 and parents[r, i] < i for i >= 1; every node lies at depth 7 or less; nodes 1 to 7 form a chain below the root. Some request's accepted node lies at depth 7. `cache_lens`: some request holds 1024 cached rows and some holds 2.
All inputs are finite; a program needn't handle non-finite values.
Results may differ from the reference program's by a relative error of at most 0.015.
Values may be sent and summed in bfloat16 or wider, within the bound.
No kernel may reach another device: no remote copies, remote signals or barrier semaphores. Data moves between devices by JAX's collectives and lax.ppermute only.
A program may use at most 64 MiB of HBM per device.

```python
from functools import reduce
import jax
import jax.numpy as jnp
from jax import lax

D = 4096
HEADS = 16
KVH = 8
HD = 128
TREE = 32
MAXD = 7
PAGE = 256
PAGES = 4
REQ_DEV = 8
PATH = 8
REQUESTS = 512
TOKENS = 16384
N_REQ = 64
N_TP = 8


def draw_queries(key, part):
    first_key = jax.random.fold_in(jax.random.fold_in(key, 11), 0)
    values = jnp.clip(2.5 * jax.random.normal(first_key, (TOKENS, HEADS * HD), jnp.float32), -10.0, 10.0)
    return values.astype(jnp.bfloat16)


def draw_kv_pool(key, part):
    shape = (REQUESTS, PAGES, PAGE, KVH * 2 * HD)
    pool_key = jax.random.fold_in(key, 21)
    values = jnp.clip(jax.random.normal(pool_key, shape, jnp.float32), -4.0, 4.0)
    return values.astype(jnp.bfloat16)


def draw_cache_lens(key, part):
    first_key, second_key, third_key, fourth_key = jax.random.split(jax.random.fold_in(key, 31), 4)
    lowest = PAGE * (PAGES - 1) // 2 + 2
    long_lengths = jax.random.randint(first_key, (REQUESTS,), lowest, PAGES * PAGE + 1)
    short_lengths = jax.random.randint(second_key, (REQUESTS,), 2, PAGE + 1)
    is_short = jax.random.randint(third_key, (REQUESTS,), 0, 16) == 0
    lengths = jnp.where(is_short, short_lengths, long_lengths)
    longest = jax.random.randint(fourth_key, (), 0, REQUESTS)
    shortest = (longest + REQUESTS // 2) % REQUESTS
    request_ids = jnp.arange(REQUESTS, dtype=jnp.int32)
    lengths = jnp.where(request_ids == shortest, 2, lengths)
    return jnp.where(request_ids == longest, PAGES * PAGE, lengths).astype(jnp.int32)


def draw_parents(key, part):

    def one_tree(tree_key):

        def add_node(node, carry):
            parent_ids, depths = carry
            picked = jax.random.randint(jax.random.fold_in(tree_key, node), (), 0, node)
            picked = jnp.where(node <= MAXD, node - 1, picked)
            picked = jnp.where(depths[picked] >= MAXD, parent_ids[picked], picked)
            parent_ids = parent_ids.at[node].set(picked)
            depths = depths.at[node].set(depths[picked] + 1)
            return (parent_ids, depths)
        start_ids = jnp.zeros((TREE,), jnp.int32)
        parent_ids, depths = lax.fori_loop(1, TREE, add_node, (start_ids, start_ids))
        return parent_ids
    tree_keys = jax.random.split(jax.random.fold_in(key, 41), REQUESTS)
    return jax.vmap(one_tree)(tree_keys).astype(jnp.int32)


def draw_accepted(key, part):
    first_key, second_key = jax.random.split(jax.random.fold_in(key, 51), 2)
    nodes_drawn = jax.random.randint(first_key, (REQUESTS,), 0, TREE)
    deepest = jax.random.randint(second_key, (), 0, REQUESTS)
    return jnp.where(jnp.arange(REQUESTS, dtype=jnp.int32) == deepest, MAXD, nodes_drawn).astype(jnp.int32)


def shard_levels(stream_key, dims, cuts, smallest, top_value):
    gain, own = 1.0, jax.random.fold_in(stream_key, 6)
    for position, shards_of in cuts:
        draws = jnp.exp(jax.random.uniform(jax.random.fold_in(own, position), (shards_of,), jnp.float32, smallest / len(cuts), top_value / len(cuts)))
        gain = gain * jnp.repeat(draws, dims[position] // shards_of).reshape([-1 if axis == position else 1 for axis in range(len(dims))])
    return gain


def gaussian(own_key, dims, spread, bound, shards=(), kind=jnp.bfloat16):
    drawn = jax.random.normal(own_key, dims, jnp.float32) * spread
    if len(shards) > 0:
        drawn = shard_levels(own_key, dims, shards, -0.22, 0.18) * drawn
    return jnp.clip(drawn, min=-bound, max=bound).astype(kind)


def setup_inputs(seed: int = 0) -> dict:
    arg_keys = jax.random.split(jax.random.key(seed), 10)
    return {
        "queries": draw_queries(jax.random.fold_in(arg_keys[9], 71), 0),
        "new_kv": gaussian(arg_keys[1], (TOKENS, KVH * 2 * HD), 1.0, 4.0, ((0, 64), (1, 8))),
        "kv_pool": draw_kv_pool(jax.random.fold_in(arg_keys[9], 71), 0),
        "cache_lens": draw_cache_lens(jax.random.fold_in(arg_keys[9], 71), 0),
        "parents": draw_parents(jax.random.fold_in(arg_keys[9], 71), 0),
        "accepted": draw_accepted(jax.random.fold_in(arg_keys[9], 71), 0),
        "residual": gaussian(arg_keys[6], (TOKENS, D), 0.5, 3.0, ((0, 512),)),
        "w_out": gaussian(arg_keys[7], (HEADS * HD, D), (HEADS * HD) ** -0.5, 0.125, ((0, 8),)),
        "norm_gain": jnp.clip(1.0 + 0.15 * jax.random.normal(arg_keys[8], (D,), jnp.float32), 0.25, 1.75),
    }


NEGATIVE = -1e+30

def ancestors(parents):
    node_ids = jnp.arange(TREE, dtype=jnp.int32)
    current = jnp.broadcast_to(node_ids, parents.shape)
    marked = jnp.zeros(parents.shape + (TREE,), jnp.int32)
    for depth_step in range(MAXD + 1):
        onehot_rows = (current[..., None] == node_ids).astype(jnp.int32)
        marked = jnp.maximum(marked, onehot_rows)
        current = lax.optimization_barrier(jnp.sum(onehot_rows * parents[..., None, :], axis=-1, dtype=jnp.int32))
    return marked

def block_partial(query_rows, key_rows, value_rows, allowed):
    scale_factor = HD ** (-0.5)
    scores = jnp.einsum('tkgd,ckd->tkgc', query_rows, key_rows) * scale_factor
    visible = allowed[:, None, None, :]
    largest = lax.optimization_barrier(jnp.max(jnp.where(visible, scores, NEGATIVE), axis=-1))
    weights = jnp.where(visible, jnp.exp(scores - largest[..., None]), 0.0)
    totals = lax.optimization_barrier(jnp.sum(weights, axis=-1))
    rounded = lax.optimization_barrier(weights.astype(jnp.bfloat16)).astype(jnp.float32)
    weighted = jnp.einsum('tkgc,ckd->tkgd', rounded, value_rows)
    return (largest, totals, weighted)

def merge_blocks(block_list):
    largest = reduce(jnp.maximum, [block_part[0] for block_part in block_list])
    factors = [jnp.exp(block_part[0] - largest) for block_part in block_list]
    denominator = reduce(jnp.add, [factor * block_part[1] for factor, block_part in zip(factors, block_list)])
    numerator = reduce(jnp.add, [factor[..., None] * block_part[2] for factor, block_part in zip(factors, block_list)])
    return (denominator, numerator)

def reference(queries, new_kv, kv_pool, cache_lens, parents, accepted, residual, w_out, norm_gain):
    group = HEADS // KVH
    row_width = KVH * 2 * HD
    marked_all = ancestors(parents)

    def attend(request):
        first_row = request * TREE
        query_rows = lax.dynamic_slice_in_dim(queries, first_row, TREE, 0).astype(jnp.float32).reshape(TREE, KVH, group, HD)
        fresh = lax.dynamic_slice_in_dim(new_kv, first_row, TREE, 0).astype(jnp.float32).reshape(TREE, KVH, 2, HD)
        length = cache_lens[request]
        marked = marked_all[request]
        block_list = [block_partial(query_rows, fresh[:, :, 0], fresh[:, :, 1], marked > 0)]
        home = request // REQ_DEV
        within = request % REQ_DEV
        for page_index in range(PAGES):
            holder = ((home + page_index) % N_REQ * REQ_DEV + within).astype(jnp.int32)
            page_rows = lax.dynamic_slice(kv_pool, (holder, jnp.int32(page_index), jnp.int32(0), jnp.int32(0)), (1, 1, PAGE, row_width))
            page_rows = page_rows.reshape(PAGE, KVH, 2, HD).astype(jnp.float32)
            positions = page_index * PAGE + jnp.arange(PAGE, dtype=jnp.int32)
            allowed = jnp.broadcast_to((positions < length)[None, :], (TREE, PAGE))
            block_list.append(block_partial(query_rows, page_rows[:, :, 0], page_rows[:, :, 1], allowed))
        denominator, numerator = merge_blocks(block_list)
        return (numerator / denominator[..., None]).reshape(TREE, HEADS * HD).astype(jnp.bfloat16)
    attention = lax.map(attend, jnp.arange(REQUESTS, dtype=jnp.int32)).reshape(TOKENS, HEADS * HD)
    group_width = HEADS * HD // N_TP
    summed = jnp.zeros((TOKENS, D), jnp.float32)
    for group_index in range(N_TP):
        low = group_index * group_width
        product = jnp.dot(attention[:, low:low + group_width], w_out[low:low + group_width], preferred_element_type=jnp.float32)
        summed = summed + lax.optimization_barrier(product.astype(jnp.bfloat16)).astype(jnp.float32)
    hidden_out = (residual.astype(jnp.float32) + summed).astype(jnp.bfloat16)
    widened = hidden_out.astype(jnp.float32)
    normed = (widened * lax.rsqrt(lax.optimization_barrier(jnp.mean(widened * widened, axis=-1, keepdims=True)) + 1e-05) * norm_gain).astype(jnp.bfloat16)
    node_ids = jnp.arange(TREE, dtype=jnp.int32)
    chosen = (accepted[:, None] == node_ids[None, :]).astype(jnp.int32)
    on_path = lax.optimization_barrier(jnp.sum(chosen[:, :, None] * marked_all, axis=1, dtype=jnp.int32))
    path_rank = jnp.cumsum(on_path, axis=1, dtype=jnp.int32) - 1
    path_slots = jnp.arange(PATH, dtype=jnp.int32)
    selector = ((path_rank[:, None, :] == path_slots[None, :, None]) & (on_path[:, None, :] > 0)).astype(jnp.float32)
    fresh_rows = new_kv.reshape(REQUESTS, TREE, row_width).astype(jnp.float32)
    accepted_kv = jnp.einsum('rku,ruc->rkc', selector, fresh_rows).astype(jnp.bfloat16)
    return (hidden_out, normed, accepted_kv)
```

```python
from functools import reduce

import jax
import jax.numpy as jnp
from jax import lax
from jax.sharding import PartitionSpec as P

HD = 128
TREE = 32
MAXD = 7
PATH = 8
EXTRA = 16


NEGATIVE = -1e30


def shifted(value, axis, steps):
    count = lax.axis_size(axis)
    pairs = [(source, (source + steps) % count) for source in range(count)]
    return lax.ppermute(value, axis, pairs)


def ancestors(parents):
    node_ids = jnp.arange(TREE, dtype=jnp.int32)
    current = jnp.broadcast_to(node_ids, parents.shape)
    marked = jnp.zeros(parents.shape + (TREE,), jnp.int32)
    for depth_step in range(MAXD + 1):
        onehot_rows = (current[..., None] == node_ids).astype(jnp.int32)
        marked = jnp.maximum(marked, onehot_rows)
        current = jnp.sum(onehot_rows * parents[..., None, :], axis=-1, dtype=jnp.int32)
    return marked


def block_partial(query_rows, key_rows, value_rows, allowed, round_max=False):
    scale_factor = HD ** (-0.5)
    scores = (
        jnp.einsum("rtkgd,rckd->rtkgc", query_rows, key_rows, preferred_element_type=jnp.float32)
        * scale_factor
    )
    visible = allowed[:, :, None, None, :]
    largest = jnp.max(jnp.where(visible, scores, NEGATIVE), axis=-1)
    if round_max:
        largest = largest.astype(jnp.bfloat16).astype(jnp.float32)
    weights = jnp.where(visible, jnp.exp(scores - largest[..., None]), 0.0)
    totals = jnp.sum(weights, axis=-1)
    weighted = jnp.einsum(
        "rtkgc,rckd->rtkgd",
        weights.astype(jnp.bfloat16),
        value_rows,
        preferred_element_type=jnp.float32,
    )
    return (largest, totals, weighted)


def page_term(query_rows, page_rows, lengths, page_index, round_max=False):
    req_count, row_count, row_width = page_rows.shape
    kv_local = row_width // (2 * HD)
    split_rows = page_rows.reshape(req_count, row_count, kv_local, 2, HD)
    positions = page_index * row_count + jnp.arange(row_count, dtype=jnp.int32)
    allowed = positions[None, None, :] < lengths[:, None, None]
    return block_partial(
        query_rows, split_rows[:, :, :, 0], split_rows[:, :, :, 1], allowed, round_max
    )


def merge_blocks(block_list):
    largest = reduce(jnp.maximum, [block_part[0] for block_part in block_list])
    factors = [jnp.exp(block_part[0] - largest) for block_part in block_list]
    denominator = reduce(
        jnp.add, [factor * block_part[1] for factor, block_part in zip(factors, block_list)]
    )
    numerator = reduce(
        jnp.add,
        [factor[..., None] * block_part[2] for factor, block_part in zip(factors, block_list)],
    )
    return (denominator, numerator)


def pack_queries(queries, lengths):
    width = queries.shape[1]
    count = lengths.shape[0]
    hi = (lengths // 16).astype(jnp.bfloat16)
    lo = (lengths % 16).astype(jnp.bfloat16)
    extra = jnp.zeros((EXTRA, width), jnp.bfloat16)
    extra = extra.at[0, :count].set(hi).at[1, :count].set(lo)
    return jnp.concatenate([queries, extra], axis=0)


def unpack_queries(packed, count):
    rows = packed.shape[0] - EXTRA
    extra = packed[rows:]
    hi = extra[0, :count].astype(jnp.int32)
    lo = extra[1, :count].astype(jnp.int32)
    return packed[:rows], hi * 16 + lo


def pack_partial(part):
    largest, totals, weighted = part
    req_count, tree, kv_local, group = largest.shape
    tokens = req_count * tree
    heads = kv_local * group
    body = weighted.reshape(tokens, heads * HD).astype(jnp.bfloat16)
    total_hi = totals.astype(jnp.bfloat16)
    total_lo = (totals - total_hi.astype(jnp.float32)).astype(jnp.bfloat16)
    stats = jnp.stack(
        [largest.astype(jnp.bfloat16), total_hi, total_lo], axis=0
    ).reshape(3, tokens, heads)
    stats = jnp.transpose(stats, (0, 2, 1)).reshape(3 * heads, tokens)
    width = heads * HD
    extra = jnp.zeros((EXTRA, width), jnp.bfloat16)
    extra = extra.at[: 3 * heads, :tokens].set(stats)
    return jnp.concatenate([body, extra], axis=0)


def unpack_partial(packed, shape):
    req_count, tree, kv_local, group = shape
    tokens = req_count * tree
    heads = kv_local * group
    body = packed[:tokens].astype(jnp.float32).reshape(req_count, tree, kv_local, group, HD)
    stats = packed[tokens : tokens + 3 * heads, :tokens].astype(jnp.float32)
    stats = jnp.transpose(stats.reshape(3, heads, tokens), (0, 2, 1)).reshape(
        3, req_count, tree, kv_local, group
    )
    return (stats[0], stats[1] + stats[2], body)


def per_device(queries, new_kv, kv_pool, cache_lens, parents, accepted, residual, w_out, norm_gain):
    req_count, page_count, page_size, row_width = kv_pool.shape
    kv_local = row_width // (2 * HD)
    q_local = queries.shape[1] // HD
    group = q_local // kv_local
    query_rows = queries.reshape(req_count, TREE, kv_local, group, HD)
    fresh = new_kv.reshape(req_count, TREE, kv_local, 2, HD)
    marked = ancestors(parents)

    packed_queries = pack_queries(queries, cache_lens)
    arrived = [shifted(packed_queries, "req", page_index) for page_index in range(1, page_count)]

    block_list = [block_partial(query_rows, fresh[:, :, :, 0], fresh[:, :, :, 1], marked > 0)]
    block_list.append(page_term(query_rows, kv_pool[:, 0], cache_lens, 0))

    returned = []
    for page_index in range(1, page_count):
        guest_queries, guest_lengths = unpack_queries(arrived[page_index - 1], req_count)
        guest_rows = guest_queries.reshape(req_count, TREE, kv_local, group, HD)
        part = page_term(guest_rows, kv_pool[:, page_index], guest_lengths, page_index, True)
        returned.append(shifted(pack_partial(part), "req", -page_index))
    stat_shape = (req_count, TREE, kv_local, group)
    for packed in returned:
        block_list.append(unpack_partial(packed, stat_shape))

    denominator, numerator = merge_blocks(block_list)
    attention = (
        (numerator / denominator[..., None])
        .astype(jnp.bfloat16)
        .reshape(req_count * TREE, q_local * HD)
    )
    product = jnp.dot(attention, w_out, preferred_element_type=jnp.float32)
    summed = lax.psum_scatter(
        lax.optimization_barrier(product.astype(jnp.bfloat16))
        .astype(jnp.float32)
        .astype(jnp.bfloat16),
        "tp",
        scatter_dimension=0,
        tiled=True,
    ).astype(jnp.float32)
    hidden_out = (residual.astype(jnp.float32) + summed).astype(jnp.bfloat16)
    widened = hidden_out.astype(jnp.float32)
    normed = (
        widened * lax.rsqrt(jnp.mean(widened * widened, axis=-1, keepdims=True) + 1e-05) * norm_gain
    ).astype(jnp.bfloat16)
    node_ids = jnp.arange(TREE, dtype=jnp.int32)
    chosen = (accepted[:, None] == node_ids[None, :]).astype(jnp.int32)
    on_path = jnp.sum(chosen[:, :, None] * marked, axis=1, dtype=jnp.int32)
    path_rank = jnp.cumsum(on_path, axis=1, dtype=jnp.int32) - 1
    path_slots = jnp.arange(PATH, dtype=jnp.int32)
    selector = (
        (path_rank[:, None, :] == path_slots[None, :, None]) & (on_path[:, None, :] > 0)
    ).astype(jnp.bfloat16)
    fresh_rows = new_kv.reshape(req_count, TREE, row_width)
    accepted_kv = jnp.einsum(
        "rku,ruc->rkc", selector, fresh_rows, preferred_element_type=jnp.float32
    ).astype(jnp.bfloat16)
    return (hidden_out, normed, accepted_kv)


def solution(mesh):
    placed = (
        P("req", "tp"),
        P("req", "tp"),
        P("req", None, None, "tp"),
        P("req"),
        P("req", None),
        P("req"),
        P(("req", "tp"), None),
        P("tp", None),
        P(),
    )
    return jax.shard_map(
        per_device,
        mesh=mesh,
        in_specs=placed,
        out_specs=(P(("req", "tp"), None), P(("req", "tp"), None), P("req", None, "tp")),
        check_vma=False,
    )
```

```python
import functools

import jax
import jax.numpy as jnp
from jax import lax
from jax.experimental import pallas as pl
from jax.experimental.pallas import tpu as pltpu
from jax.sharding import PartitionSpec as P

HD = 128
TREE = 32
MAXD = 7
PATH = 8
EXTRA = 16
STAT_LANES = 128


NEGATIVE = -1e30


def shifted(value, axis, steps):
    count = lax.axis_size(axis)
    pairs = [(source, (source + steps) % count) for source in range(count)]
    return lax.ppermute(value, axis, pairs)


def ancestors(parents):
    node_ids = jnp.arange(TREE, dtype=jnp.int32)
    current = jnp.broadcast_to(node_ids, parents.shape)
    marked = jnp.zeros(parents.shape + (TREE,), jnp.int32)
    for depth_step in range(MAXD + 1):
        onehot_rows = (current[..., None] == node_ids).astype(jnp.int32)
        marked = jnp.maximum(marked, onehot_rows)
        current = jnp.sum(onehot_rows * parents[..., None, :], axis=-1, dtype=jnp.int32)
    return marked


def attend(query, key, value, valid, round_max):
    scores = lax.dot_general(
        query, key, (((1,), (1,)), ((), ())), preferred_element_type=jnp.float32
    ) * (HD ** (-0.5))
    scores = jnp.where(valid, scores, NEGATIVE)
    largest = jnp.max(scores, axis=1, keepdims=True)
    if round_max:
        largest = largest.astype(jnp.bfloat16).astype(jnp.float32)
    weights = jnp.where(valid, jnp.exp(scores - largest), 0.0)
    totals = jnp.sum(weights, axis=1, keepdims=True)
    weighted = jnp.dot(
        weights.astype(jnp.bfloat16), value, preferred_element_type=jnp.float32
    )
    return largest, totals, weighted


def lane_pick(block, lane):
    lanes = lax.broadcasted_iota(jnp.int32, block.shape, 1)
    return jnp.sum(jnp.where(lanes == lane, block, 0.0), axis=1, keepdims=True)


def holder_kernel(page_index, group, q_ref, qx_ref, kv_ref, out_ref):
    request = pl.program_id(0)
    page_size = kv_ref.shape[0]
    extra = qx_ref[...].astype(jnp.float32)
    length_row = extra[0:1, :] * 16.0 + extra[1:2, :]
    length = lane_pick(length_row, request)
    positions = (
        lax.broadcasted_iota(jnp.int32, (1, page_size), 1) + page_index * page_size
    ).astype(jnp.float32)
    valid = positions < length
    key = kv_ref[:, 0:HD]
    value = kv_ref[:, HD : 2 * HD]
    rows = q_ref.shape[0]
    lanes = lax.broadcasted_iota(jnp.int32, (rows, STAT_LANES), 1)
    stats = jnp.zeros((rows, STAT_LANES), jnp.float32)
    for head in range(group):
        query = q_ref[:, head * HD : (head + 1) * HD]
        largest, totals, weighted = attend(query, key, value, valid, True)
        out_ref[:, head * HD : (head + 1) * HD] = weighted.astype(jnp.bfloat16)
        total_hi = totals.astype(jnp.bfloat16).astype(jnp.float32)
        total_lo = totals - total_hi
        stats = jnp.where(lanes == head, largest, stats)
        stats = jnp.where(lanes == group + head, total_hi, stats)
        stats = jnp.where(lanes == 2 * group + head, total_lo, stats)
    out_ref[:, group * HD : group * HD + STAT_LANES] = stats.astype(jnp.bfloat16)


def holder_partial(packed_queries, kv_pool, page_index, group):
    req_count, page_count, page_size, row_width = kv_pool.shape
    width = packed_queries.shape[1]
    rows = req_count * TREE
    return pl.pallas_call(
        functools.partial(holder_kernel, page_index, group),
        out_shape=jax.ShapeDtypeStruct((rows, width + STAT_LANES), jnp.bfloat16),
        grid=(req_count,),
        in_specs=[
            pl.BlockSpec((TREE, width), lambda r: (r, 0)),
            pl.BlockSpec((EXTRA, width), lambda r: (rows // EXTRA, 0)),
            pl.BlockSpec((None, None, page_size, row_width), lambda r: (r, page_index, 0, 0)),
        ],
        out_specs=pl.BlockSpec((TREE, width + STAT_LANES), lambda r: (r, 0)),
    )(packed_queries, packed_queries, kv_pool)


def home_kernel(group, lens_ref, q_ref, fresh_ref, kv_ref, marked_ref, *rest):
    returned = rest[:-1]
    out_ref = rest[-1]
    request = pl.program_id(0)
    page_size = kv_ref.shape[0]
    length = lens_ref[request]
    page_valid = lax.broadcasted_iota(jnp.int32, (1, page_size), 1) < length
    tree_valid = marked_ref[...] > 0
    for head in range(group):
        query = q_ref[:, head * HD : (head + 1) * HD]
        blocks = [
            attend(query, fresh_ref[:, 0:HD], fresh_ref[:, HD : 2 * HD], tree_valid, False),
            attend(query, kv_ref[:, 0:HD], kv_ref[:, HD : 2 * HD], page_valid, False),
        ]
        for part_ref in returned:
            stats = part_ref[:, group * HD : group * HD + STAT_LANES].astype(jnp.float32)
            largest = lane_pick(stats, head)
            totals = lane_pick(stats, group + head) + lane_pick(stats, 2 * group + head)
            weighted = part_ref[:, head * HD : (head + 1) * HD].astype(jnp.float32)
            blocks.append((largest, totals, weighted))
        top = blocks[0][0]
        for block in blocks[1:]:
            top = jnp.maximum(top, block[0])
        denominator = jnp.zeros_like(top)
        numerator = jnp.zeros(blocks[0][2].shape, jnp.float32)
        for largest, totals, weighted in blocks:
            factor = jnp.exp(largest - top)
            denominator = denominator + factor * totals
            numerator = numerator + factor * weighted
        out_ref[:, head * HD : (head + 1) * HD] = (numerator / denominator).astype(jnp.bfloat16)


def home_attention(cache_lens, queries, new_kv, kv_pool, marked, returned, group):
    req_count, page_count, page_size, row_width = kv_pool.shape
    rows, width = queries.shape
    part_width = returned[0].shape[1]
    in_specs = [
        pl.BlockSpec((TREE, width), lambda r, lens: (r, 0)),
        pl.BlockSpec((TREE, row_width), lambda r, lens: (r, 0)),
        pl.BlockSpec((None, None, page_size, row_width), lambda r, lens: (r, 0, 0, 0)),
        pl.BlockSpec((None, TREE, TREE), lambda r, lens: (r, 0, 0)),
    ] + [pl.BlockSpec((TREE, part_width), lambda r, lens: (r, 0)) for _ in returned]
    return pl.pallas_call(
        functools.partial(home_kernel, group),
        out_shape=jax.ShapeDtypeStruct((rows, width), jnp.bfloat16),
        grid_spec=pltpu.PrefetchScalarGridSpec(
            num_scalar_prefetch=1,
            grid=(req_count,),
            in_specs=in_specs,
            out_specs=pl.BlockSpec((TREE, width), lambda r, lens: (r, 0)),
        ),
    )(cache_lens, queries, new_kv, kv_pool, marked, *returned)


def pack_queries(queries, lengths):
    width = queries.shape[1]
    count = lengths.shape[0]
    pair = jnp.stack([lengths // 16, lengths % 16]).astype(jnp.bfloat16)
    extra = jnp.pad(pair, ((0, EXTRA - 2), (0, width - count)))
    return jnp.concatenate([queries, extra], axis=0)


def per_device(queries, new_kv, kv_pool, cache_lens, parents, accepted, residual, w_out, norm_gain):
    req_count, page_count, page_size, row_width = kv_pool.shape
    kv_local = row_width // (2 * HD)
    q_local = queries.shape[1] // HD
    group = q_local // kv_local
    marked = ancestors(parents)

    packed_queries = pack_queries(queries, cache_lens)
    returned = []
    for page_index in range(1, page_count):
        guest = shifted(packed_queries, "req", page_index)
        part = holder_partial(guest, kv_pool, page_index, group)
        returned.append(shifted(part, "req", -page_index))

    attention = home_attention(cache_lens, queries, new_kv, kv_pool, marked, returned, group)
    product = jnp.dot(attention, w_out, preferred_element_type=jnp.float32)
    summed = lax.psum_scatter(
        lax.optimization_barrier(product.astype(jnp.bfloat16))
        .astype(jnp.float32)
        .astype(jnp.bfloat16),
        "tp",
        scatter_dimension=0,
        tiled=True,
    ).astype(jnp.float32)
    hidden_out = (residual.astype(jnp.float32) + summed).astype(jnp.bfloat16)
    widened = hidden_out.astype(jnp.float32)
    normed = (
        widened * lax.rsqrt(jnp.mean(widened * widened, axis=-1, keepdims=True) + 1e-05) * norm_gain
    ).astype(jnp.bfloat16)
    node_ids = jnp.arange(TREE, dtype=jnp.int32)
    chosen = (accepted[:, None] == node_ids[None, :]).astype(jnp.int32)
    on_path = jnp.sum(chosen[:, :, None] * marked, axis=1, dtype=jnp.int32)
    path_rank = jnp.cumsum(on_path, axis=1, dtype=jnp.int32) - 1
    path_slots = jnp.arange(PATH, dtype=jnp.int32)
    selector = (
        (path_rank[:, None, :] == path_slots[None, :, None]) & (on_path[:, None, :] > 0)
    ).astype(jnp.bfloat16)
    fresh_rows = new_kv.reshape(req_count, TREE, row_width)
    accepted_kv = jnp.einsum(
        "rku,ruc->rkc", selector, fresh_rows, preferred_element_type=jnp.float32
    ).astype(jnp.bfloat16)
    return (hidden_out, normed, accepted_kv)


def solution(mesh):
    placed = (
        P("req", "tp"),
        P("req", "tp"),
        P("req", None, None, "tp"),
        P("req"),
        P("req", None),
        P("req"),
        P(("req", "tp"), None),
        P("tp", None),
        P(),
    )
    return jax.shard_map(
        per_device,
        mesh=mesh,
        in_specs=placed,
        out_specs=(P(("req", "tp"), None), P(("req", "tp"), None), P("req", None, "tp")),
        check_vma=False,
    )
```

```python
import functools

import jax
import jax.numpy as jnp
from jax import lax
from jax.experimental import pallas as pl
from jax.experimental.pallas import tpu as pltpu
from jax.sharding import PartitionSpec as P

HD = 128
TREE = 32
MAXD = 7
PATH = 8
EXTRA = 16
STAT_LANES = 128


NEGATIVE = -1e30


def shifted(value, axis, steps):
    count = lax.axis_size(axis)
    pairs = [(source, (source + steps) % count) for source in range(count)]
    return lax.ppermute(value, axis, pairs)


def attend(query, key, value, valid, round_max):
    scores = lax.dot_general(
        query, key, (((1,), (1,)), ((), ())), preferred_element_type=jnp.float32
    ) * (HD ** (-0.5))
    scores = jnp.where(valid, scores, NEGATIVE)
    largest = jnp.max(scores, axis=1, keepdims=True)
    if round_max:
        largest = largest.astype(jnp.bfloat16).astype(jnp.float32)
    weights = jnp.where(valid, jnp.exp(scores - largest), 0.0)
    totals = jnp.sum(weights, axis=1, keepdims=True)
    weighted = jnp.dot(
        weights.astype(jnp.bfloat16), value, preferred_element_type=jnp.float32
    )
    return largest, totals, weighted


def lane_pick(block, lane):
    lanes = lax.broadcasted_iota(jnp.int32, block.shape, 1)
    return jnp.sum(jnp.where(lanes == lane, block, 0.0), axis=1, keepdims=True)


def stacked_heads(rows_ref, row0, group):
    parts = [rows_ref[row0 : row0 + TREE, g * HD : (g + 1) * HD] for g in range(group)]
    return jnp.concatenate(parts, axis=0)


def local_kernel(group, lens_ref, acc_ref, q_ref, fresh_ref, kv_ref, parents_ref,
                 sum_ref, stat_ref, path_ref):
    req_count, page_size = kv_ref.shape[0], kv_ref.shape[1]
    sub = lax.broadcasted_iota(jnp.int32, (TREE, TREE), 0)
    lane = lax.broadcasted_iota(jnp.int32, (TREE, TREE), 1)
    identity = (sub == lane).astype(jnp.float32)
    inclusive = (sub <= lane).astype(jnp.bfloat16)
    parent_cols = parents_ref[...].astype(jnp.float32)
    stat_lanes = lax.broadcasted_iota(jnp.int32, (TREE, STAT_LANES), 1)
    for r in range(req_count):
        row0 = r * TREE
        parent = lane_pick(parent_cols, r)
        reach = jnp.maximum((parent == lane.astype(jnp.float32)).astype(jnp.float32), identity)
        for _ in range(3):
            square = jnp.dot(reach.astype(jnp.bfloat16), reach.astype(jnp.bfloat16),
                             preferred_element_type=jnp.float32)
            reach = jnp.minimum(square, 1.0)
        on_path = jnp.sum(jnp.where(sub == acc_ref[r], reach, 0.0), axis=0, keepdims=True)
        rank = jnp.dot(jnp.broadcast_to(on_path, (8, TREE)).astype(jnp.bfloat16), inclusive,
                       preferred_element_type=jnp.float32)[0:1]
        slot = lax.broadcasted_iota(jnp.int32, (PATH, TREE), 0).astype(jnp.float32)
        selector = jnp.where((rank - 1.0 == slot) & (on_path > 0.5), 1.0, 0.0)
        fresh = fresh_ref[row0 : row0 + TREE, :]
        path_ref[r] = jnp.dot(selector.astype(jnp.bfloat16), fresh,
                              preferred_element_type=jnp.float32).astype(path_ref.dtype)

        query = stacked_heads(q_ref, row0, group)
        tree_valid = jnp.concatenate([reach] * group, axis=0) > 0.5
        length = lens_ref[r]
        page_valid = lax.broadcasted_iota(jnp.int32, (1, page_size), 1) < length
        m1, l1, a1 = attend(query, fresh[:, 0:HD], fresh[:, HD : 2 * HD], tree_valid, False)
        m2, l2, a2 = attend(query, kv_ref[r, :, 0:HD], kv_ref[r, :, HD : 2 * HD], page_valid, False)
        top = jnp.maximum(m1, m2)
        f1 = jnp.exp(m1 - top)
        f2 = jnp.exp(m2 - top)
        totals = f1 * l1 + f2 * l2
        weighted = f1 * a1 + f2 * a2
        stats = jnp.zeros((TREE, STAT_LANES), jnp.float32)
        for g in range(group):
            rows = slice(g * TREE, (g + 1) * TREE)
            sum_ref[row0 : row0 + TREE, g * HD : (g + 1) * HD] = weighted[rows]
            stats = jnp.where(stat_lanes == g, top[rows], stats)
            stats = jnp.where(stat_lanes == group + g, totals[rows], stats)
        stat_ref[row0 : row0 + TREE, :] = stats


def local_partial(cache_lens, accepted, queries, new_kv, kv_pool, parents, group):
    req_count, page_count, page_size, row_width = kv_pool.shape
    rows, width = queries.shape
    vmem = pltpu.MemorySpace.VMEM
    return pl.pallas_call(
        functools.partial(local_kernel, group),
        out_shape=(
            jax.ShapeDtypeStruct((rows, width), jnp.float32),
            jax.ShapeDtypeStruct((rows, STAT_LANES), jnp.float32),
            jax.ShapeDtypeStruct((req_count, PATH, row_width), jnp.bfloat16),
        ),
        grid_spec=pltpu.PrefetchScalarGridSpec(
            num_scalar_prefetch=2,
            grid=(1,),
            in_specs=[
                pl.BlockSpec((rows, width), lambda i, a, b: (0, 0)),
                pl.BlockSpec((rows, row_width), lambda i, a, b: (0, 0)),
                pl.BlockSpec((req_count, None, page_size, row_width), lambda i, a, b: (0, 0, 0, 0)),
                pl.BlockSpec((TREE, req_count), lambda i, a, b: (0, 0)),
            ],
            out_specs=(
                pl.BlockSpec((rows, width), lambda i, a, b: (0, 0)),
                pl.BlockSpec((rows, STAT_LANES), lambda i, a, b: (0, 0)),
                pl.BlockSpec((req_count, PATH, row_width), lambda i, a, b: (0, 0, 0)),
            ),
        ),
    )(cache_lens, accepted, queries, new_kv, kv_pool, parents.T)


def holder_kernel(page_index, group, q_ref, kv_ref, out_ref):
    req_count, page_size = kv_ref.shape[0], kv_ref.shape[1]
    rows = req_count * TREE
    extra = q_ref[rows : rows + EXTRA, :].astype(jnp.float32)
    length_row = extra[0:1, :] * 16.0 + extra[1:2, :]
    positions = (
        lax.broadcasted_iota(jnp.int32, (1, page_size), 1) + page_index * page_size
    ).astype(jnp.float32)
    stat_lanes = lax.broadcasted_iota(jnp.int32, (TREE, STAT_LANES), 1)
    for r in range(req_count):
        row0 = r * TREE
        valid = positions < lane_pick(length_row, r)
        query = stacked_heads(q_ref, row0, group)
        largest, totals, weighted = attend(
            query, kv_ref[r, :, 0:HD], kv_ref[r, :, HD : 2 * HD], valid, True
        )
        total_hi = totals.astype(jnp.bfloat16).astype(jnp.float32)
        total_lo = totals - total_hi
        stats = jnp.zeros((TREE, STAT_LANES), jnp.float32)
        for g in range(group):
            part = slice(g * TREE, (g + 1) * TREE)
            out_ref[row0 : row0 + TREE, g * HD : (g + 1) * HD] = weighted[part].astype(jnp.bfloat16)
            stats = jnp.where(stat_lanes == g, largest[part], stats)
            stats = jnp.where(stat_lanes == group + g, total_hi[part], stats)
            stats = jnp.where(stat_lanes == 2 * group + g, total_lo[part], stats)
        out_ref[row0 : row0 + TREE, group * HD : group * HD + STAT_LANES] = stats.astype(jnp.bfloat16)


def holder_partial(packed_queries, kv_pool, page_index, group):
    req_count, page_count, page_size, row_width = kv_pool.shape
    packed_rows, width = packed_queries.shape
    rows = req_count * TREE
    return pl.pallas_call(
        functools.partial(holder_kernel, page_index, group),
        out_shape=jax.ShapeDtypeStruct((rows, width + STAT_LANES), jnp.bfloat16),
        grid=(1,),
        in_specs=[
            pl.BlockSpec((packed_rows, width), lambda i: (0, 0)),
            pl.BlockSpec((req_count, None, page_size, row_width), lambda i: (0, page_index, 0, 0)),
        ],
        out_specs=pl.BlockSpec((rows, width + STAT_LANES), lambda i: (0, 0)),
    )(packed_queries, kv_pool)


def merge_kernel(group, sum_ref, stat_ref, *rest):
    returned = rest[:-2]
    w_ref = rest[-2]
    out_ref = rest[-1]
    rows = sum_ref.shape[0]
    for r in range(rows // TREE):
        row0 = r * TREE
        local_stats = stat_ref[row0 : row0 + TREE, :]
        heads = []
        for g in range(group):
            cols = slice(g * HD, (g + 1) * HD)
            blocks = [(lane_pick(local_stats, g), lane_pick(local_stats, group + g),
                       sum_ref[row0 : row0 + TREE, cols])]
            for part_ref in returned:
                stats = part_ref[row0 : row0 + TREE, group * HD : group * HD + STAT_LANES].astype(jnp.float32)
                totals = lane_pick(stats, group + g) + lane_pick(stats, 2 * group + g)
                blocks.append((lane_pick(stats, g), totals,
                               part_ref[row0 : row0 + TREE, cols].astype(jnp.float32)))
            top = blocks[0][0]
            for block in blocks[1:]:
                top = jnp.maximum(top, block[0])
            denominator = jnp.zeros_like(top)
            numerator = jnp.zeros((TREE, HD), jnp.float32)
            for largest, totals, weighted in blocks:
                factor = jnp.exp(largest - top)
                denominator = denominator + factor * totals
                numerator = numerator + factor * weighted
            heads.append((numerator / denominator).astype(jnp.bfloat16))
        attention = jnp.concatenate(heads, axis=1)
        out_ref[row0 : row0 + TREE, :] = jnp.dot(
            attention, w_ref[...], preferred_element_type=jnp.float32
        ).astype(out_ref.dtype)


def merge_project(sums, stats, returned, w_out, group):
    rows, width = sums.shape
    part_width = returned[0].shape[1]
    model = w_out.shape[1]
    full = lambda shape: pl.BlockSpec(shape, lambda i: (0, 0))
    return pl.pallas_call(
        functools.partial(merge_kernel, group),
        out_shape=jax.ShapeDtypeStruct((rows, model), jnp.bfloat16),
        grid=(1,),
        in_specs=[full((rows, width)), full((rows, STAT_LANES))]
        + [full((rows, part_width)) for _ in returned]
        + [full(w_out.shape)],
        out_specs=full((rows, model)),
        compiler_params=pltpu.CompilerParams(vmem_limit_bytes=48 * 1024 * 1024),
    )(sums, stats, *returned, w_out)


def pack_queries(queries, lengths):
    width = queries.shape[1]
    count = lengths.shape[0]
    pair = jnp.stack([lengths // 16, lengths % 16]).astype(jnp.bfloat16)
    extra = jnp.pad(pair, ((0, EXTRA - 2), (0, width - count)))
    return jnp.concatenate([queries, extra], axis=0)


def per_device(queries, new_kv, kv_pool, cache_lens, parents, accepted, residual, w_out, norm_gain):
    req_count, page_count, page_size, row_width = kv_pool.shape
    kv_local = row_width // (2 * HD)
    q_local = queries.shape[1] // HD
    group = q_local // kv_local

    packed_queries = pack_queries(queries, cache_lens)
    guests = [shifted(packed_queries, "req", p) for p in range(1, page_count)]
    sums, stats, accepted_kv = local_partial(
        cache_lens, accepted, queries, new_kv, kv_pool, parents, group
    )
    returned = []
    for page_index in range(1, page_count):
        part = holder_partial(guests[page_index - 1], kv_pool, page_index, group)
        returned.append(shifted(part, "req", -page_index))

    product = merge_project(sums, stats, returned, w_out, group)
    summed = lax.psum_scatter(product, "tp", scatter_dimension=0, tiled=True).astype(jnp.float32)
    hidden_out = (residual.astype(jnp.float32) + summed).astype(jnp.bfloat16)
    widened = hidden_out.astype(jnp.float32)
    normed = (
        widened * lax.rsqrt(jnp.mean(widened * widened, axis=-1, keepdims=True) + 1e-05) * norm_gain
    ).astype(jnp.bfloat16)
    return (hidden_out, normed, accepted_kv)


def solution(mesh):
    placed = (
        P("req", "tp"),
        P("req", "tp"),
        P("req", None, None, "tp"),
        P("req"),
        P("req", None),
        P("req"),
        P(("req", "tp"), None),
        P("tp", None),
        P(),
    )
    return jax.shard_map(
        per_device,
        mesh=mesh,
        in_specs=placed,
        out_specs=(P(("req", "tp"), None), P(("req", "tp"), None), P("req", None, "tp")),
        check_vma=False,
    )
```

```python
import functools

import jax
import jax.numpy as jnp
from jax import lax
from jax.experimental import pallas as pl
from jax.experimental.pallas import tpu as pltpu
from jax.sharding import PartitionSpec as P

HD = 128
TREE = 32
MAXD = 7
PATH = 8
EXTRA = 16
STAT_LANES = 128


NEGATIVE = -1e30


def shifted(value, axis, steps):
    count = lax.axis_size(axis)
    pairs = [(source, (source + steps) % count) for source in range(count)]
    return lax.ppermute(value, axis, pairs)


def attend(query, key, value, valid, round_max):
    scores = lax.dot_general(
        query, key, (((1,), (1,)), ((), ())), preferred_element_type=jnp.float32
    ) * (HD ** (-0.5))
    scores = jnp.where(valid, scores, NEGATIVE)
    largest = jnp.max(scores, axis=1, keepdims=True)
    if round_max:
        largest = largest.astype(jnp.bfloat16).astype(jnp.float32)
    weights = jnp.where(valid, jnp.exp(scores - largest), 0.0)
    totals = jnp.sum(weights, axis=1, keepdims=True)
    weighted = jnp.dot(
        weights.astype(jnp.bfloat16), value, preferred_element_type=jnp.float32
    )
    return largest, totals, weighted


def lane_pick(block, lane):
    lanes = lax.broadcasted_iota(jnp.int32, block.shape, 1)
    return jnp.sum(jnp.where(lanes == lane, block, 0.0), axis=1, keepdims=True)


def stacked_heads(rows_ref, row0, group):
    parts = [rows_ref[row0 : row0 + TREE, g * HD : (g + 1) * HD] for g in range(group)]
    return jnp.concatenate(parts, axis=0)


def local_kernel(group, lens_ref, acc_ref, q_ref, fresh_ref, kv_ref, parents_ref,
                 sum_ref, stat_ref, path_ref):
    req_count, page_size = kv_ref.shape[0], kv_ref.shape[1]
    sub = lax.broadcasted_iota(jnp.int32, (TREE, TREE), 0)
    lane = lax.broadcasted_iota(jnp.int32, (TREE, TREE), 1)
    identity = (sub == lane).astype(jnp.float32)
    inclusive = (sub <= lane).astype(jnp.bfloat16)
    parent_cols = parents_ref[...].astype(jnp.float32)
    stat_lanes = lax.broadcasted_iota(jnp.int32, (TREE, STAT_LANES), 1)
    for r in range(req_count):
        row0 = r * TREE
        parent = lane_pick(parent_cols, r)
        reach = jnp.maximum((parent == lane.astype(jnp.float32)).astype(jnp.float32), identity)
        for _ in range(3):
            square = jnp.dot(reach.astype(jnp.bfloat16), reach.astype(jnp.bfloat16),
                             preferred_element_type=jnp.float32)
            reach = jnp.minimum(square, 1.0)
        on_path = jnp.sum(jnp.where(sub == acc_ref[r], reach, 0.0), axis=0, keepdims=True)
        rank = jnp.dot(jnp.broadcast_to(on_path, (8, TREE)).astype(jnp.bfloat16), inclusive,
                       preferred_element_type=jnp.float32)[0:1]
        slot = lax.broadcasted_iota(jnp.int32, (PATH, TREE), 0).astype(jnp.float32)
        selector = jnp.where((rank - 1.0 == slot) & (on_path > 0.5), 1.0, 0.0)
        fresh = fresh_ref[row0 : row0 + TREE, :]
        path_ref[r] = jnp.dot(selector.astype(jnp.bfloat16), fresh,
                              preferred_element_type=jnp.float32).astype(path_ref.dtype)

        query = stacked_heads(q_ref, row0, group)
        tree_valid = jnp.concatenate([reach] * group, axis=0) > 0.5
        length = lens_ref[r]
        page_valid = lax.broadcasted_iota(jnp.int32, (1, page_size), 1) < length
        m1, l1, a1 = attend(query, fresh[:, 0:HD], fresh[:, HD : 2 * HD], tree_valid, False)
        m2, l2, a2 = attend(query, kv_ref[r, :, 0:HD], kv_ref[r, :, HD : 2 * HD], page_valid, False)
        top = jnp.maximum(m1, m2)
        f1 = jnp.exp(m1 - top)
        f2 = jnp.exp(m2 - top)
        totals = f1 * l1 + f2 * l2
        weighted = f1 * a1 + f2 * a2
        stats = jnp.zeros((TREE, STAT_LANES), jnp.float32)
        for g in range(group):
            rows = slice(g * TREE, (g + 1) * TREE)
            sum_ref[row0 : row0 + TREE, g * HD : (g + 1) * HD] = weighted[rows]
            stats = jnp.where(stat_lanes == g, top[rows], stats)
            stats = jnp.where(stat_lanes == group + g, totals[rows], stats)
        stat_ref[row0 : row0 + TREE, :] = stats


def local_partial(cache_lens, accepted, queries, new_kv, kv_pool, parents, group):
    req_count, page_count, page_size, row_width = kv_pool.shape
    rows, width = queries.shape
    vmem = pltpu.MemorySpace.VMEM
    return pl.pallas_call(
        functools.partial(local_kernel, group),
        out_shape=(
            jax.ShapeDtypeStruct((rows, width), jnp.float32),
            jax.ShapeDtypeStruct((rows, STAT_LANES), jnp.float32),
            jax.ShapeDtypeStruct((req_count, PATH, row_width), jnp.bfloat16),
        ),
        grid_spec=pltpu.PrefetchScalarGridSpec(
            num_scalar_prefetch=2,
            grid=(1,),
            in_specs=[
                pl.BlockSpec((rows, width), lambda i, a, b: (0, 0)),
                pl.BlockSpec((rows, row_width), lambda i, a, b: (0, 0)),
                pl.BlockSpec((req_count, None, page_size, row_width), lambda i, a, b: (0, 0, 0, 0)),
                pl.BlockSpec((TREE, req_count), lambda i, a, b: (0, 0)),
            ],
            out_specs=(
                pl.BlockSpec((rows, width), lambda i, a, b: (0, 0)),
                pl.BlockSpec((rows, STAT_LANES), lambda i, a, b: (0, 0)),
                pl.BlockSpec((req_count, PATH, row_width), lambda i, a, b: (0, 0, 0)),
            ),
        ),
    )(cache_lens, accepted, queries, new_kv, kv_pool, parents.T)


def holder_kernel(page_index, group, q_ref, kv_ref, out_ref):
    req_count, page_size = kv_ref.shape[0], kv_ref.shape[1]
    rows = req_count * TREE
    extra = q_ref[rows : rows + EXTRA, :].astype(jnp.float32)
    length_row = extra[0:1, :] * 16.0 + extra[1:2, :]
    positions = (
        lax.broadcasted_iota(jnp.int32, (1, page_size), 1) + page_index * page_size
    ).astype(jnp.float32)
    stat_lanes = lax.broadcasted_iota(jnp.int32, (TREE, STAT_LANES), 1)
    for r in range(req_count):
        row0 = r * TREE
        valid = positions < lane_pick(length_row, r)
        query = stacked_heads(q_ref, row0, group)
        largest, totals, weighted = attend(
            query, kv_ref[r, :, 0:HD], kv_ref[r, :, HD : 2 * HD], valid, True
        )
        total_hi = totals.astype(jnp.bfloat16).astype(jnp.float32)
        total_lo = totals - total_hi
        stats = jnp.zeros((TREE, STAT_LANES), jnp.float32)
        for g in range(group):
            part = slice(g * TREE, (g + 1) * TREE)
            out_ref[row0 : row0 + TREE, g * HD : (g + 1) * HD] = weighted[part].astype(jnp.bfloat16)
            stats = jnp.where(stat_lanes == g, largest[part], stats)
            stats = jnp.where(stat_lanes == group + g, total_hi[part], stats)
            stats = jnp.where(stat_lanes == 2 * group + g, total_lo[part], stats)
        out_ref[row0 : row0 + TREE, group * HD : group * HD + STAT_LANES] = stats.astype(jnp.bfloat16)


def holder_partial(packed_queries, kv_pool, page_index, group):
    req_count, page_count, page_size, row_width = kv_pool.shape
    packed_rows, width = packed_queries.shape
    rows = req_count * TREE
    return pl.pallas_call(
        functools.partial(holder_kernel, page_index, group),
        out_shape=jax.ShapeDtypeStruct((rows, width + STAT_LANES), jnp.bfloat16),
        grid=(1,),
        in_specs=[
            pl.BlockSpec((packed_rows, width), lambda i: (0, 0)),
            pl.BlockSpec((req_count, None, page_size, row_width), lambda i: (0, page_index, 0, 0)),
        ],
        out_specs=pl.BlockSpec((rows, width + STAT_LANES), lambda i: (0, 0)),
    )(packed_queries, kv_pool)


def merge_kernel(group, sum_ref, stat_ref, *rest):
    returned = rest[:-2]
    w_ref = rest[-2]
    out_ref = rest[-1]
    rows = sum_ref.shape[0]
    for r in range(rows // TREE):
        row0 = r * TREE
        local_stats = stat_ref[row0 : row0 + TREE, :]
        heads = []
        for g in range(group):
            cols = slice(g * HD, (g + 1) * HD)
            blocks = [(lane_pick(local_stats, g), lane_pick(local_stats, group + g),
                       sum_ref[row0 : row0 + TREE, cols])]
            for part_ref in returned:
                stats = part_ref[row0 : row0 + TREE, group * HD : group * HD + STAT_LANES].astype(jnp.float32)
                totals = lane_pick(stats, group + g) + lane_pick(stats, 2 * group + g)
                blocks.append((lane_pick(stats, g), totals,
                               part_ref[row0 : row0 + TREE, cols].astype(jnp.float32)))
            top = blocks[0][0]
            for block in blocks[1:]:
                top = jnp.maximum(top, block[0])
            denominator = jnp.zeros_like(top)
            numerator = jnp.zeros((TREE, HD), jnp.float32)
            for largest, totals, weighted in blocks:
                factor = jnp.exp(largest - top)
                denominator = denominator + factor * totals
                numerator = numerator + factor * weighted
            heads.append((numerator / denominator).astype(jnp.bfloat16))
        attention = jnp.concatenate(heads, axis=1)
        out_ref[row0 : row0 + TREE, :] = jnp.dot(
            attention, w_ref[...], preferred_element_type=jnp.float32
        ).astype(out_ref.dtype)


def merge_project(sums, stats, returned, w_out, group):
    rows, width = sums.shape
    part_width = returned[0].shape[1]
    model = w_out.shape[1]
    full = lambda shape: pl.BlockSpec(shape, lambda i: (0, 0))
    return pl.pallas_call(
        functools.partial(merge_kernel, group),
        out_shape=jax.ShapeDtypeStruct((rows, model), jnp.bfloat16),
        grid=(1,),
        in_specs=[full((rows, width)), full((rows, STAT_LANES))]
        + [full((rows, part_width)) for _ in returned]
        + [full(w_out.shape)],
        out_specs=full((rows, model)),
        compiler_params=pltpu.CompilerParams(vmem_limit_bytes=48 * 1024 * 1024),
    )(sums, stats, *returned, w_out)


def pack_queries(queries, lengths):
    width = queries.shape[1]
    count = lengths.shape[0]
    pair = jnp.stack([lengths // 16, lengths % 16]).astype(jnp.bfloat16)
    extra = jnp.pad(pair, ((0, EXTRA - 2), (0, width - count)))
    return jnp.concatenate([queries, extra], axis=0)


def per_device(queries, new_kv, kv_pool, cache_lens, parents, accepted, residual, w_out, norm_gain):
    req_count, page_count, page_size, row_width = kv_pool.shape
    kv_local = row_width // (2 * HD)
    q_local = queries.shape[1] // HD
    group = q_local // kv_local

    packed_queries = pack_queries(queries, cache_lens)
    guests = [shifted(packed_queries, "req", p) for p in range(1, page_count)]
    sums, stats, accepted_kv = local_partial(
        cache_lens, accepted, queries, new_kv, kv_pool, parents, group
    )
    returned = []
    for page_index in range(1, page_count):
        part = holder_partial(guests[page_index - 1], kv_pool, page_index, group)
        returned.append(shifted(part, "req", -page_index))

    product = merge_project(sums, stats, returned, w_out, group)
    tp_count = lax.axis_size("tp")
    pieces = product.reshape(tp_count, product.shape[0] // tp_count, product.shape[1])
    gathered = lax.all_to_all(pieces, "tp", 0, 0, tiled=False)
    summed = jnp.sum(gathered.astype(jnp.float32), axis=0)
    hidden_out = (residual.astype(jnp.float32) + summed).astype(jnp.bfloat16)
    widened = hidden_out.astype(jnp.float32)
    normed = (
        widened * lax.rsqrt(jnp.mean(widened * widened, axis=-1, keepdims=True) + 1e-05) * norm_gain
    ).astype(jnp.bfloat16)
    return (hidden_out, normed, accepted_kv)


def solution(mesh):
    placed = (
        P("req", "tp"),
        P("req", "tp"),
        P("req", None, None, "tp"),
        P("req"),
        P("req", None),
        P("req"),
        P(("req", "tp"), None),
        P("tp", None),
        P(),
    )
    return jax.shard_map(
        per_device,
        mesh=mesh,
        in_specs=placed,
        out_specs=(P(("req", "tp"), None), P(("req", "tp"), None), P("req", None, "tp")),
        check_vma=False,
    )
```

```python
import functools

import jax
import jax.numpy as jnp
from jax import lax
from jax.experimental import pallas as pl
from jax.experimental.pallas import tpu as pltpu
from jax.sharding import PartitionSpec as P

HD = 128
TREE = 32
MAXD = 7
PATH = 8
EXTRA = 16
STAT_LANES = 128


NEGATIVE = -1e30


def shifted(value, axis, steps):
    count = lax.axis_size(axis)
    pairs = [(source, (source + steps) % count) for source in range(count)]
    return lax.ppermute(value, axis, pairs)


def attend(query, key, value, valid, round_max):
    scores = lax.dot_general(
        query, key, (((1,), (1,)), ((), ())), preferred_element_type=jnp.float32
    ) * (HD ** (-0.5))
    scores = jnp.where(valid, scores, NEGATIVE)
    largest = jnp.max(scores, axis=1, keepdims=True)
    if round_max:
        largest = largest.astype(jnp.bfloat16).astype(jnp.float32)
    weights = jnp.where(valid, jnp.exp(scores - largest), 0.0)
    totals = jnp.sum(weights, axis=1, keepdims=True)
    weighted = jnp.dot(
        weights.astype(jnp.bfloat16), value, preferred_element_type=jnp.float32
    )
    return largest, totals, weighted


def lane_pick(block, lane):
    lanes = lax.broadcasted_iota(jnp.int32, block.shape, 1)
    return jnp.sum(jnp.where(lanes == lane, block, 0.0), axis=1, keepdims=True)


def stacked_heads(rows_ref, row0, group):
    parts = [rows_ref[row0 : row0 + TREE, g * HD : (g + 1) * HD] for g in range(group)]
    return jnp.concatenate(parts, axis=0)


def tree_kernel(group, acc_ref, q_ref, fresh_ref, parent_ref, part_ref, path_ref):
    rows = fresh_ref.shape[0]
    req_count = rows // TREE
    sub = lax.broadcasted_iota(jnp.int32, (rows, rows), 0)
    lane = lax.broadcasted_iota(jnp.int32, (rows, rows), 1)
    same_block = (sub // TREE) == (lane // TREE)
    reach = jnp.where((parent_ref[...] == lane) | (sub == lane), 1.0, 0.0)
    for _ in range(3):
        square = jnp.dot(reach.astype(jnp.bfloat16), reach.astype(jnp.bfloat16),
                         preferred_element_type=jnp.float32)
        reach = jnp.minimum(square, 1.0)
    inclusive = jnp.where(same_block & (sub <= lane), 1.0, 0.0).astype(jnp.bfloat16)
    sel_sub = lax.broadcasted_iota(jnp.int32, (req_count * PATH, rows), 0)
    sel_lane = lax.broadcasted_iota(jnp.int32, (req_count * PATH, rows), 1)
    chosen = jnp.zeros((req_count * PATH, rows), jnp.float32)
    for r in range(req_count):
        target = r * TREE + acc_ref[r]
        chosen = jnp.where((sel_sub // PATH == r) & (sel_lane == target), 1.0, chosen)
    on_path = jnp.dot(chosen.astype(jnp.bfloat16), reach.astype(jnp.bfloat16),
                      preferred_element_type=jnp.float32)
    rank = jnp.dot(on_path.astype(jnp.bfloat16), inclusive, preferred_element_type=jnp.float32)
    slot = (sel_sub % PATH).astype(jnp.float32)
    selector = jnp.where((rank - 1.0 == slot) & (on_path > 0.5), 1.0, 0.0)
    path = jnp.dot(selector.astype(jnp.bfloat16), fresh_ref[...],
                   preferred_element_type=jnp.float32).astype(path_ref.dtype)
    for r in range(req_count):
        path_ref[r] = path[r * PATH : (r + 1) * PATH]

    valid = jnp.concatenate([reach > 0.5] * group, axis=0)
    query = jnp.concatenate([q_ref[:, g * HD : (g + 1) * HD] for g in range(group)], axis=0)
    largest, totals, weighted = attend(query, fresh_ref[:, 0:HD], fresh_ref[:, HD : 2 * HD], valid, False)
    stat_lanes = lax.broadcasted_iota(jnp.int32, (rows, STAT_LANES), 1)
    stats = jnp.zeros((rows, STAT_LANES), jnp.float32)
    for g in range(group):
        part = slice(g * rows, (g + 1) * rows)
        stats = jnp.where(stat_lanes == g, largest[part], stats)
        stats = jnp.where(stat_lanes == group + g, totals[part], stats)
        part_ref[:, g * HD : (g + 1) * HD] = weighted[part]
    part_ref[:, group * HD : group * HD + STAT_LANES] = stats


def tree_partial(accepted, queries, new_kv, parents, group):
    rows, width = queries.shape
    req_count = parents.shape[0]
    row_width = new_kv.shape[1]
    offsets = TREE * jnp.arange(req_count, dtype=jnp.int32)[:, None]
    parent_rows = (parents + offsets).reshape(rows, 1)
    full = lambda shape: pl.BlockSpec(shape, lambda i, a: (0,) * len(shape))
    return pl.pallas_call(
        functools.partial(tree_kernel, group),
        out_shape=(
            jax.ShapeDtypeStruct((rows, width + STAT_LANES), jnp.float32),
            jax.ShapeDtypeStruct((req_count, PATH, row_width), jnp.bfloat16),
        ),
        grid_spec=pltpu.PrefetchScalarGridSpec(
            num_scalar_prefetch=1,
            grid=(1,),
            in_specs=[full((rows, width)), full((rows, row_width)), full((rows, 1))],
            out_specs=(full((rows, width + STAT_LANES)), full((req_count, PATH, row_width))),
        ),
    )(accepted, queries, new_kv, parent_rows)


def local_kernel(group, lens_ref, q_ref, kv_ref, tree_ref, sum_ref, stat_ref):
    req_count, page_size = kv_ref.shape[0], kv_ref.shape[1]
    stat_lanes = lax.broadcasted_iota(jnp.int32, (TREE, STAT_LANES), 1)
    for r in range(req_count):
        row0 = r * TREE
        query = stacked_heads(q_ref, row0, group)
        length = lens_ref[r]
        page_valid = lax.broadcasted_iota(jnp.int32, (1, page_size), 1) < length
        m2, l2, a2 = attend(query, kv_ref[r, :, 0:HD], kv_ref[r, :, HD : 2 * HD], page_valid, False)
        tree_stats = tree_ref[row0 : row0 + TREE, group * HD : group * HD + STAT_LANES]
        m1 = jnp.concatenate([lane_pick(tree_stats, g) for g in range(group)], axis=0)
        l1 = jnp.concatenate([lane_pick(tree_stats, group + g) for g in range(group)], axis=0)
        a1 = stacked_heads(tree_ref, row0, group)
        top = jnp.maximum(m1, m2)
        f1 = jnp.exp(m1 - top)
        f2 = jnp.exp(m2 - top)
        totals = f1 * l1 + f2 * l2
        weighted = f1 * a1 + f2 * a2
        stats = jnp.zeros((TREE, STAT_LANES), jnp.float32)
        for g in range(group):
            rows = slice(g * TREE, (g + 1) * TREE)
            sum_ref[row0 : row0 + TREE, g * HD : (g + 1) * HD] = weighted[rows]
            stats = jnp.where(stat_lanes == g, top[rows], stats)
            stats = jnp.where(stat_lanes == group + g, totals[rows], stats)
        stat_ref[row0 : row0 + TREE, :] = stats


def local_partial(cache_lens, queries, kv_pool, tree_part, group):
    req_count, page_count, page_size, row_width = kv_pool.shape
    rows, width = queries.shape
    return pl.pallas_call(
        functools.partial(local_kernel, group),
        out_shape=(
            jax.ShapeDtypeStruct((rows, width), jnp.float32),
            jax.ShapeDtypeStruct((rows, STAT_LANES), jnp.float32),
        ),
        grid_spec=pltpu.PrefetchScalarGridSpec(
            num_scalar_prefetch=1,
            grid=(1,),
            in_specs=[
                pl.BlockSpec((rows, width), lambda i, a: (0, 0)),
                pl.BlockSpec((req_count, None, page_size, row_width), lambda i, a: (0, 0, 0, 0)),
                pl.BlockSpec(tree_part.shape, lambda i, a: (0, 0)),
            ],
            out_specs=(
                pl.BlockSpec((rows, width), lambda i, a: (0, 0)),
                pl.BlockSpec((rows, STAT_LANES), lambda i, a: (0, 0)),
            ),
        ),
    )(cache_lens, queries, kv_pool, tree_part)


def holder_kernel(page_index, group, q_ref, kv_ref, order_ref, out_ref):
    req_count, page_size = kv_ref.shape[0], kv_ref.shape[1]
    rows = req_count * TREE
    extra = q_ref[rows : rows + EXTRA, :].astype(jnp.float32)
    length_row = extra[0:1, :] * 16.0 + extra[1:2, :]
    positions = (
        lax.broadcasted_iota(jnp.int32, (1, page_size), 1) + page_index * page_size
    ).astype(jnp.float32)
    stat_lanes = lax.broadcasted_iota(jnp.int32, (TREE, STAT_LANES), 1)
    for r in range(req_count):
        row0 = r * TREE
        valid = positions < lane_pick(length_row, r)
        query = stacked_heads(q_ref, row0, group)
        largest, totals, weighted = attend(
            query, kv_ref[r, :, 0:HD], kv_ref[r, :, HD : 2 * HD], valid, True
        )
        total_hi = totals.astype(jnp.bfloat16).astype(jnp.float32)
        total_lo = totals - total_hi
        stats = jnp.zeros((TREE, STAT_LANES), jnp.float32)
        for g in range(group):
            part = slice(g * TREE, (g + 1) * TREE)
            out_ref[row0 : row0 + TREE, g * HD : (g + 1) * HD] = weighted[part].astype(jnp.bfloat16)
            stats = jnp.where(stat_lanes == g, largest[part], stats)
            stats = jnp.where(stat_lanes == group + g, total_hi[part], stats)
            stats = jnp.where(stat_lanes == 2 * group + g, total_lo[part], stats)
        out_ref[row0 : row0 + TREE, group * HD : group * HD + STAT_LANES] = stats.astype(jnp.bfloat16)


def holder_partial(packed_queries, kv_pool, page_index, group, order_after):
    req_count, page_count, page_size, row_width = kv_pool.shape
    packed_rows, width = packed_queries.shape
    rows = req_count * TREE
    return pl.pallas_call(
        functools.partial(holder_kernel, page_index, group),
        out_shape=jax.ShapeDtypeStruct((rows, width + STAT_LANES), jnp.bfloat16),
        grid=(1,),
        in_specs=[
            pl.BlockSpec((packed_rows, width), lambda i: (0, 0)),
            pl.BlockSpec((req_count, None, page_size, row_width), lambda i: (0, page_index, 0, 0)),
            pl.BlockSpec((8, STAT_LANES), lambda i: (0, 0)),
        ],
        out_specs=pl.BlockSpec((rows, width + STAT_LANES), lambda i: (0, 0)),
    )(packed_queries, kv_pool, order_after)


def merge_kernel(group, sum_ref, stat_ref, *rest):
    returned = rest[:-2]
    w_ref = rest[-2]
    out_ref = rest[-1]
    rows = sum_ref.shape[0]
    for r in range(rows // TREE):
        row0 = r * TREE
        local_stats = stat_ref[row0 : row0 + TREE, :]
        heads = []
        for g in range(group):
            cols = slice(g * HD, (g + 1) * HD)
            blocks = [(lane_pick(local_stats, g), lane_pick(local_stats, group + g),
                       sum_ref[row0 : row0 + TREE, cols])]
            for part_ref in returned:
                stats = part_ref[row0 : row0 + TREE, group * HD : group * HD + STAT_LANES].astype(jnp.float32)
                totals = lane_pick(stats, group + g) + lane_pick(stats, 2 * group + g)
                blocks.append((lane_pick(stats, g), totals,
                               part_ref[row0 : row0 + TREE, cols].astype(jnp.float32)))
            top = blocks[0][0]
            for block in blocks[1:]:
                top = jnp.maximum(top, block[0])
            denominator = jnp.zeros_like(top)
            numerator = jnp.zeros((TREE, HD), jnp.float32)
            for largest, totals, weighted in blocks:
                factor = jnp.exp(largest - top)
                denominator = denominator + factor * totals
                numerator = numerator + factor * weighted
            heads.append((numerator / denominator).astype(jnp.bfloat16))
        attention = jnp.concatenate(heads, axis=1)
        out_ref[row0 : row0 + TREE, :] = jnp.dot(
            attention, w_ref[...], preferred_element_type=jnp.float32
        ).astype(out_ref.dtype)


def merge_project(sums, stats, returned, w_out, group):
    rows, width = sums.shape
    part_width = returned[0].shape[1]
    model = w_out.shape[1]
    full = lambda shape: pl.BlockSpec(shape, lambda i: (0, 0))
    return pl.pallas_call(
        functools.partial(merge_kernel, group),
        out_shape=jax.ShapeDtypeStruct((rows, model), jnp.bfloat16),
        grid=(1,),
        in_specs=[full((rows, width)), full((rows, STAT_LANES))]
        + [full((rows, part_width)) for _ in returned]
        + [full(w_out.shape)],
        out_specs=full((rows, model)),
        compiler_params=pltpu.CompilerParams(vmem_limit_bytes=48 * 1024 * 1024),
    )(sums, stats, *returned, w_out)


def pack_queries(queries, lengths):
    width = queries.shape[1]
    count = lengths.shape[0]
    pair = jnp.stack([lengths // 16, lengths % 16]).astype(jnp.bfloat16)
    extra = jnp.pad(pair, ((0, EXTRA - 2), (0, width - count)))
    return jnp.concatenate([queries, extra], axis=0)


def per_device(queries, new_kv, kv_pool, cache_lens, parents, accepted, residual, w_out, norm_gain):
    req_count, page_count, page_size, row_width = kv_pool.shape
    kv_local = row_width // (2 * HD)
    q_local = queries.shape[1] // HD
    group = q_local // kv_local

    packed_queries = pack_queries(queries, cache_lens)
    guests = [shifted(packed_queries, "req", p) for p in range(1, page_count)]
    tree_part, accepted_kv = tree_partial(accepted, queries, new_kv, parents, group)
    returned = []
    for page_index in range(1, page_count):
        part = holder_partial(guests[page_index - 1], kv_pool, page_index, group, tree_part)
        returned.append(shifted(part, "req", -page_index))
    sums, stats = local_partial(cache_lens, queries, kv_pool, tree_part, group)

    product = merge_project(sums, stats, returned, w_out, group)
    tp_count = lax.axis_size("tp")
    pieces = product.reshape(tp_count, product.shape[0] // tp_count, product.shape[1])
    gathered = lax.all_to_all(pieces, "tp", 0, 0, tiled=False)
    summed = jnp.sum(gathered.astype(jnp.float32), axis=0)
    hidden_out = (residual.astype(jnp.float32) + summed).astype(jnp.bfloat16)
    widened = hidden_out.astype(jnp.float32)
    normed = (
        widened * lax.rsqrt(jnp.mean(widened * widened, axis=-1, keepdims=True) + 1e-05) * norm_gain
    ).astype(jnp.bfloat16)
    return (hidden_out, normed, accepted_kv)


def solution(mesh):
    placed = (
        P("req", "tp"),
        P("req", "tp"),
        P("req", None, None, "tp"),
        P("req"),
        P("req", None),
        P("req"),
        P(("req", "tp"), None),
        P("tp", None),
        P(),
    )
    return jax.shard_map(
        per_device,
        mesh=mesh,
        in_specs=placed,
        out_specs=(P(("req", "tp"), None), P(("req", "tp"), None), P("req", None, "tp")),
        check_vma=False,
    )
```

```python
import functools

import jax
import jax.numpy as jnp
from jax import lax
from jax.experimental import pallas as pl
from jax.experimental.pallas import tpu as pltpu
from jax.sharding import PartitionSpec as P

HD = 128
TREE = 32
MAXD = 7
PATH = 8
EXTRA = 16
STAT_LANES = 128
SHIPPED_PAGES = (1, 2)


NEGATIVE = -1e30


def shifted(value, axis, steps):
    count = lax.axis_size(axis)
    pairs = [(source, (source + steps) % count) for source in range(count)]
    return lax.ppermute(value, axis, pairs)


def attend(query, key, value, valid, round_max):
    scores = lax.dot_general(
        query, key, (((1,), (1,)), ((), ())), preferred_element_type=jnp.float32
    ) * (HD ** (-0.5))
    scores = jnp.where(valid, scores, NEGATIVE)
    largest = jnp.max(scores, axis=1, keepdims=True)
    if round_max:
        largest = largest.astype(jnp.bfloat16).astype(jnp.float32)
    weights = jnp.where(valid, jnp.exp(scores - largest), 0.0)
    totals = jnp.sum(weights, axis=1, keepdims=True)
    weighted = jnp.dot(
        weights.astype(jnp.bfloat16), value, preferred_element_type=jnp.float32
    )
    return largest, totals, weighted


def lane_pick(block, lane):
    lanes = lax.broadcasted_iota(jnp.int32, block.shape, 1)
    return jnp.sum(jnp.where(lanes == lane, block, 0.0), axis=1, keepdims=True)


def stacked_heads(rows_ref, row0, group):
    parts = [rows_ref[row0 : row0 + TREE, g * HD : (g + 1) * HD] for g in range(group)]
    return jnp.concatenate(parts, axis=0)


def tree_kernel(group, acc_ref, q_ref, fresh_ref, parent_ref, part_ref, path_ref):
    rows = fresh_ref.shape[0]
    req_count = rows // TREE
    sub = lax.broadcasted_iota(jnp.int32, (rows, rows), 0)
    lane = lax.broadcasted_iota(jnp.int32, (rows, rows), 1)
    same_block = (sub // TREE) == (lane // TREE)
    reach = jnp.where((parent_ref[...] == lane) | (sub == lane), 1.0, 0.0)
    for _ in range(3):
        square = jnp.dot(reach.astype(jnp.bfloat16), reach.astype(jnp.bfloat16),
                         preferred_element_type=jnp.float32)
        reach = jnp.minimum(square, 1.0)
    inclusive = jnp.where(same_block & (sub <= lane), 1.0, 0.0).astype(jnp.bfloat16)
    sel_sub = lax.broadcasted_iota(jnp.int32, (req_count * PATH, rows), 0)
    sel_lane = lax.broadcasted_iota(jnp.int32, (req_count * PATH, rows), 1)
    chosen = jnp.zeros((req_count * PATH, rows), jnp.float32)
    for r in range(req_count):
        target = r * TREE + acc_ref[r]
        chosen = jnp.where((sel_sub // PATH == r) & (sel_lane == target), 1.0, chosen)
    on_path = jnp.dot(chosen.astype(jnp.bfloat16), reach.astype(jnp.bfloat16),
                      preferred_element_type=jnp.float32)
    rank = jnp.dot(on_path.astype(jnp.bfloat16), inclusive, preferred_element_type=jnp.float32)
    slot = (sel_sub % PATH).astype(jnp.float32)
    selector = jnp.where((rank - 1.0 == slot) & (on_path > 0.5), 1.0, 0.0)
    path = jnp.dot(selector.astype(jnp.bfloat16), fresh_ref[...],
                   preferred_element_type=jnp.float32).astype(path_ref.dtype)
    for r in range(req_count):
        path_ref[r] = path[r * PATH : (r + 1) * PATH]

    valid = jnp.concatenate([reach > 0.5] * group, axis=0)
    query = jnp.concatenate([q_ref[:, g * HD : (g + 1) * HD] for g in range(group)], axis=0)
    largest, totals, weighted = attend(query, fresh_ref[:, 0:HD], fresh_ref[:, HD : 2 * HD], valid, False)
    stat_lanes = lax.broadcasted_iota(jnp.int32, (rows, STAT_LANES), 1)
    stats = jnp.zeros((rows, STAT_LANES), jnp.float32)
    for g in range(group):
        part = slice(g * rows, (g + 1) * rows)
        stats = jnp.where(stat_lanes == g, largest[part], stats)
        stats = jnp.where(stat_lanes == group + g, totals[part], stats)
        part_ref[:, g * HD : (g + 1) * HD] = weighted[part]
    part_ref[:, group * HD : group * HD + STAT_LANES] = stats


def tree_partial(accepted, queries, new_kv, parents, group):
    rows, width = queries.shape
    req_count = parents.shape[0]
    row_width = new_kv.shape[1]
    offsets = TREE * jnp.arange(req_count, dtype=jnp.int32)[:, None]
    parent_rows = (parents + offsets).reshape(rows, 1)
    full = lambda shape: pl.BlockSpec(shape, lambda i, a: (0,) * len(shape))
    return pl.pallas_call(
        functools.partial(tree_kernel, group),
        out_shape=(
            jax.ShapeDtypeStruct((rows, width + STAT_LANES), jnp.float32),
            jax.ShapeDtypeStruct((req_count, PATH, row_width), jnp.bfloat16),
        ),
        grid_spec=pltpu.PrefetchScalarGridSpec(
            num_scalar_prefetch=1,
            grid=(1,),
            in_specs=[full((rows, width)), full((rows, row_width)), full((rows, 1))],
            out_specs=(full((rows, width + STAT_LANES)), full((req_count, PATH, row_width))),
        ),
    )(accepted, queries, new_kv, parent_rows)


def local_kernel(group, page_ids, lens_ref, q_ref, kv_ref, tree_ref, *rest):
    pages = rest[: len(page_ids) - 1]
    sum_ref, stat_ref = rest[-2:]
    req_count, page_size = kv_ref.shape[0], kv_ref.shape[1]
    stat_lanes = lax.broadcasted_iota(jnp.int32, (TREE, STAT_LANES), 1)
    for r in range(req_count):
        row0 = r * TREE
        query = stacked_heads(q_ref, row0, group)
        length = lens_ref[r]
        tree_stats = tree_ref[row0 : row0 + TREE, group * HD : group * HD + STAT_LANES]
        blocks = [(
            jnp.concatenate([lane_pick(tree_stats, g) for g in range(group)], axis=0),
            jnp.concatenate([lane_pick(tree_stats, group + g) for g in range(group)], axis=0),
            stacked_heads(tree_ref, row0, group),
        )]
        for page_index, page_ref in zip(page_ids, (kv_ref,) + tuple(pages)):
            positions = lax.broadcasted_iota(jnp.int32, (1, page_size), 1) + page_index * page_size
            blocks.append(attend(query, page_ref[r, :, 0:HD], page_ref[r, :, HD : 2 * HD],
                                 positions < length, False))
        top = blocks[0][0]
        for block in blocks[1:]:
            top = jnp.maximum(top, block[0])
        totals = jnp.zeros_like(top)
        weighted = jnp.zeros(blocks[0][2].shape, jnp.float32)
        for largest, part_totals, part_weighted in blocks:
            factor = jnp.exp(largest - top)
            totals = totals + factor * part_totals
            weighted = weighted + factor * part_weighted
        stats = jnp.zeros((TREE, STAT_LANES), jnp.float32)
        for g in range(group):
            rows = slice(g * TREE, (g + 1) * TREE)
            sum_ref[row0 : row0 + TREE, g * HD : (g + 1) * HD] = weighted[rows]
            stats = jnp.where(stat_lanes == g, top[rows], stats)
            stats = jnp.where(stat_lanes == group + g, totals[rows], stats)
        stat_ref[row0 : row0 + TREE, :] = stats


def local_partial(cache_lens, queries, kv_pool, tree_part, shipped, group):
    req_count, page_count, page_size, row_width = kv_pool.shape
    rows, width = queries.shape
    page_ids = (0,) + tuple(index for index, _ in shipped)
    page_spec = pl.BlockSpec((req_count, page_size, row_width), lambda i, a: (0, 0, 0))
    return pl.pallas_call(
        functools.partial(local_kernel, group, page_ids),
        out_shape=(
            jax.ShapeDtypeStruct((rows, width), jnp.float32),
            jax.ShapeDtypeStruct((rows, STAT_LANES), jnp.float32),
        ),
        grid_spec=pltpu.PrefetchScalarGridSpec(
            num_scalar_prefetch=1,
            grid=(1,),
            in_specs=[
                pl.BlockSpec((rows, width), lambda i, a: (0, 0)),
                pl.BlockSpec((req_count, None, page_size, row_width), lambda i, a: (0, 0, 0, 0)),
                pl.BlockSpec(tree_part.shape, lambda i, a: (0, 0)),
            ] + [page_spec for _ in shipped],
            out_specs=(
                pl.BlockSpec((rows, width), lambda i, a: (0, 0)),
                pl.BlockSpec((rows, STAT_LANES), lambda i, a: (0, 0)),
            ),
        ),
    )(cache_lens, queries, kv_pool, tree_part, *[page for _, page in shipped])


def holder_kernel(page_index, group, q_ref, kv_ref, order_ref, out_ref):
    req_count, page_size = kv_ref.shape[0], kv_ref.shape[1]
    rows = req_count * TREE
    extra = q_ref[rows : rows + EXTRA, :].astype(jnp.float32)
    length_row = extra[0:1, :] * 16.0 + extra[1:2, :]
    positions = (
        lax.broadcasted_iota(jnp.int32, (1, page_size), 1) + page_index * page_size
    ).astype(jnp.float32)
    stat_lanes = lax.broadcasted_iota(jnp.int32, (TREE, STAT_LANES), 1)
    for r in range(req_count):
        row0 = r * TREE
        valid = positions < lane_pick(length_row, r)
        query = stacked_heads(q_ref, row0, group)
        largest, totals, weighted = attend(
            query, kv_ref[r, :, 0:HD], kv_ref[r, :, HD : 2 * HD], valid, True
        )
        total_hi = totals.astype(jnp.bfloat16).astype(jnp.float32)
        total_lo = totals - total_hi
        stats = jnp.zeros((TREE, STAT_LANES), jnp.float32)
        for g in range(group):
            part = slice(g * TREE, (g + 1) * TREE)
            out_ref[row0 : row0 + TREE, g * HD : (g + 1) * HD] = weighted[part].astype(jnp.bfloat16)
            stats = jnp.where(stat_lanes == g, largest[part], stats)
            stats = jnp.where(stat_lanes == group + g, total_hi[part], stats)
            stats = jnp.where(stat_lanes == 2 * group + g, total_lo[part], stats)
        out_ref[row0 : row0 + TREE, group * HD : group * HD + STAT_LANES] = stats.astype(jnp.bfloat16)


def holder_partial(packed_queries, kv_pool, page_index, group, order_after):
    req_count, page_count, page_size, row_width = kv_pool.shape
    packed_rows, width = packed_queries.shape
    rows = req_count * TREE
    return pl.pallas_call(
        functools.partial(holder_kernel, page_index, group),
        out_shape=jax.ShapeDtypeStruct((rows, width + STAT_LANES), jnp.bfloat16),
        grid=(1,),
        in_specs=[
            pl.BlockSpec((packed_rows, width), lambda i: (0, 0)),
            pl.BlockSpec((req_count, None, page_size, row_width), lambda i: (0, page_index, 0, 0)),
            pl.BlockSpec((8, STAT_LANES), lambda i: (0, 0)),
        ],
        out_specs=pl.BlockSpec((rows, width + STAT_LANES), lambda i: (0, 0)),
    )(packed_queries, kv_pool, order_after)


def merge_kernel(group, sum_ref, stat_ref, *rest):
    returned = rest[:-2]
    w_ref = rest[-2]
    out_ref = rest[-1]
    rows = sum_ref.shape[0]
    for r in range(rows // TREE):
        row0 = r * TREE
        local_stats = stat_ref[row0 : row0 + TREE, :]
        heads = []
        for g in range(group):
            cols = slice(g * HD, (g + 1) * HD)
            blocks = [(lane_pick(local_stats, g), lane_pick(local_stats, group + g),
                       sum_ref[row0 : row0 + TREE, cols])]
            for part_ref in returned:
                stats = part_ref[row0 : row0 + TREE, group * HD : group * HD + STAT_LANES].astype(jnp.float32)
                totals = lane_pick(stats, group + g) + lane_pick(stats, 2 * group + g)
                blocks.append((lane_pick(stats, g), totals,
                               part_ref[row0 : row0 + TREE, cols].astype(jnp.float32)))
            top = blocks[0][0]
            for block in blocks[1:]:
                top = jnp.maximum(top, block[0])
            denominator = jnp.zeros_like(top)
            numerator = jnp.zeros((TREE, HD), jnp.float32)
            for largest, totals, weighted in blocks:
                factor = jnp.exp(largest - top)
                denominator = denominator + factor * totals
                numerator = numerator + factor * weighted
            heads.append((numerator / denominator).astype(jnp.bfloat16))
        attention = jnp.concatenate(heads, axis=1)
        out_ref[row0 : row0 + TREE, :] = jnp.dot(
            attention, w_ref[...], preferred_element_type=jnp.float32
        ).astype(out_ref.dtype)


def merge_project(sums, stats, returned, w_out, group):
    rows, width = sums.shape
    part_width = returned[0].shape[1]
    model = w_out.shape[1]
    full = lambda shape: pl.BlockSpec(shape, lambda i: (0, 0))
    return pl.pallas_call(
        functools.partial(merge_kernel, group),
        out_shape=jax.ShapeDtypeStruct((rows, model), jnp.bfloat16),
        grid=(1,),
        in_specs=[full((rows, width)), full((rows, STAT_LANES))]
        + [full((rows, part_width)) for _ in returned]
        + [full(w_out.shape)],
        out_specs=full((rows, model)),
        compiler_params=pltpu.CompilerParams(vmem_limit_bytes=48 * 1024 * 1024),
    )(sums, stats, *returned, w_out)


def pack_queries(queries, lengths):
    width = queries.shape[1]
    count = lengths.shape[0]
    pair = jnp.stack([lengths // 16, lengths % 16]).astype(jnp.bfloat16)
    extra = jnp.pad(pair, ((0, EXTRA - 2), (0, width - count)))
    return jnp.concatenate([queries, extra], axis=0)


def per_device(queries, new_kv, kv_pool, cache_lens, parents, accepted, residual, w_out, norm_gain):
    req_count, page_count, page_size, row_width = kv_pool.shape
    kv_local = row_width // (2 * HD)
    q_local = queries.shape[1] // HD
    group = q_local // kv_local

    shipped = [(p, shifted(kv_pool[:, p], "req", -p)) for p in SHIPPED_PAGES]
    visited = [p for p in range(1, page_count) if p not in SHIPPED_PAGES]
    packed_queries = pack_queries(queries, cache_lens)
    guests = [shifted(packed_queries, "req", p) for p in visited]
    tree_part, accepted_kv = tree_partial(accepted, queries, new_kv, parents, group)
    returned = []
    for page_index, guest in zip(visited, guests):
        part = holder_partial(guest, kv_pool, page_index, group, tree_part)
        returned.append(shifted(part, "req", -page_index))
    sums, stats = local_partial(cache_lens, queries, kv_pool, tree_part, shipped, group)

    product = merge_project(sums, stats, returned, w_out, group)
    tp_count = lax.axis_size("tp")
    pieces = product.reshape(tp_count, product.shape[0] // tp_count, product.shape[1])
    gathered = lax.all_to_all(pieces, "tp", 0, 0, tiled=False)
    summed = jnp.sum(gathered.astype(jnp.float32), axis=0)
    hidden_out = (residual.astype(jnp.float32) + summed).astype(jnp.bfloat16)
    widened = hidden_out.astype(jnp.float32)
    normed = (
        widened * lax.rsqrt(jnp.mean(widened * widened, axis=-1, keepdims=True) + 1e-05) * norm_gain
    ).astype(jnp.bfloat16)
    return (hidden_out, normed, accepted_kv)


def solution(mesh):
    placed = (
        P("req", "tp"),
        P("req", "tp"),
        P("req", None, None, "tp"),
        P("req"),
        P("req", None),
        P("req"),
        P(("req", "tp"), None),
        P("tp", None),
        P(),
    )
    return jax.shard_map(
        per_device,
        mesh=mesh,
        in_specs=placed,
        out_specs=(P(("req", "tp"), None), P(("req", "tp"), None), P("req", None, "tp")),
        check_vma=False,
    )
```

```python
import functools

import jax
import jax.numpy as jnp
from jax import lax
from jax.experimental import pallas as pl
from jax.experimental.pallas import tpu as pltpu
from jax.sharding import PartitionSpec as P

HD = 128
TREE = 32
MAXD = 7
PATH = 8
EXTRA = 16
STAT_LANES = 128
SHIPPED_PAGES = (1,)


NEGATIVE = -1e30


def shifted(value, axis, steps):
    count = lax.axis_size(axis)
    pairs = [(source, (source + steps) % count) for source in range(count)]
    return lax.ppermute(value, axis, pairs)


def attend(query, key, value, valid, round_max):
    scores = lax.dot_general(
        query, key, (((1,), (1,)), ((), ())), preferred_element_type=jnp.float32
    ) * (HD ** (-0.5))
    scores = jnp.where(valid, scores, NEGATIVE)
    largest = jnp.max(scores, axis=1, keepdims=True)
    if round_max:
        largest = largest.astype(jnp.bfloat16).astype(jnp.float32)
    weights = jnp.where(valid, jnp.exp(scores - largest), 0.0)
    totals = jnp.sum(weights, axis=1, keepdims=True)
    weighted = jnp.dot(
        weights.astype(jnp.bfloat16), value, preferred_element_type=jnp.float32
    )
    return largest, totals, weighted


def lane_pick(block, lane):
    lanes = lax.broadcasted_iota(jnp.int32, block.shape, 1)
    return jnp.sum(jnp.where(lanes == lane, block, 0.0), axis=1, keepdims=True)


def stacked_heads(rows_ref, row0, group):
    parts = [rows_ref[row0 : row0 + TREE, g * HD : (g + 1) * HD] for g in range(group)]
    return jnp.concatenate(parts, axis=0)


def tree_kernel(group, acc_ref, q_ref, fresh_ref, parent_ref, part_ref, path_ref):
    rows = fresh_ref.shape[0]
    req_count = rows // TREE
    sub = lax.broadcasted_iota(jnp.int32, (rows, rows), 0)
    lane = lax.broadcasted_iota(jnp.int32, (rows, rows), 1)
    same_block = (sub // TREE) == (lane // TREE)
    reach = jnp.where((parent_ref[...] == lane) | (sub == lane), 1.0, 0.0)
    for _ in range(3):
        square = jnp.dot(reach.astype(jnp.bfloat16), reach.astype(jnp.bfloat16),
                         preferred_element_type=jnp.float32)
        reach = jnp.minimum(square, 1.0)
    inclusive = jnp.where(same_block & (sub <= lane), 1.0, 0.0).astype(jnp.bfloat16)
    sel_sub = lax.broadcasted_iota(jnp.int32, (req_count * PATH, rows), 0)
    sel_lane = lax.broadcasted_iota(jnp.int32, (req_count * PATH, rows), 1)
    chosen = jnp.zeros((req_count * PATH, rows), jnp.float32)
    for r in range(req_count):
        target = r * TREE + acc_ref[r]
        chosen = jnp.where((sel_sub // PATH == r) & (sel_lane == target), 1.0, chosen)
    on_path = jnp.dot(chosen.astype(jnp.bfloat16), reach.astype(jnp.bfloat16),
                      preferred_element_type=jnp.float32)
    rank = jnp.dot(on_path.astype(jnp.bfloat16), inclusive, preferred_element_type=jnp.float32)
    slot = (sel_sub % PATH).astype(jnp.float32)
    selector = jnp.where((rank - 1.0 == slot) & (on_path > 0.5), 1.0, 0.0)
    path = jnp.dot(selector.astype(jnp.bfloat16), fresh_ref[...],
                   preferred_element_type=jnp.float32).astype(path_ref.dtype)
    for r in range(req_count):
        path_ref[r] = path[r * PATH : (r + 1) * PATH]

    valid = jnp.concatenate([reach > 0.5] * group, axis=0)
    query = jnp.concatenate([q_ref[:, g * HD : (g + 1) * HD] for g in range(group)], axis=0)
    largest, totals, weighted = attend(query, fresh_ref[:, 0:HD], fresh_ref[:, HD : 2 * HD], valid, False)
    stat_lanes = lax.broadcasted_iota(jnp.int32, (rows, STAT_LANES), 1)
    stats = jnp.zeros((rows, STAT_LANES), jnp.float32)
    for g in range(group):
        part = slice(g * rows, (g + 1) * rows)
        stats = jnp.where(stat_lanes == g, largest[part], stats)
        stats = jnp.where(stat_lanes == group + g, totals[part], stats)
        part_ref[:, g * HD : (g + 1) * HD] = weighted[part]
    part_ref[:, group * HD : group * HD + STAT_LANES] = stats


def tree_partial(accepted, queries, new_kv, parents, group):
    rows, width = queries.shape
    req_count = parents.shape[0]
    row_width = new_kv.shape[1]
    offsets = TREE * jnp.arange(req_count, dtype=jnp.int32)[:, None]
    parent_rows = (parents + offsets).reshape(rows, 1)
    full = lambda shape: pl.BlockSpec(shape, lambda i, a: (0,) * len(shape))
    return pl.pallas_call(
        functools.partial(tree_kernel, group),
        out_shape=(
            jax.ShapeDtypeStruct((rows, width + STAT_LANES), jnp.float32),
            jax.ShapeDtypeStruct((req_count, PATH, row_width), jnp.bfloat16),
        ),
        grid_spec=pltpu.PrefetchScalarGridSpec(
            num_scalar_prefetch=1,
            grid=(1,),
            in_specs=[full((rows, width)), full((rows, row_width)), full((rows, 1))],
            out_specs=(full((rows, width + STAT_LANES)), full((req_count, PATH, row_width))),
        ),
    )(accepted, queries, new_kv, parent_rows)


def local_kernel(group, page_ids, lens_ref, q_ref, kv_ref, tree_ref, *rest):
    pages = rest[: len(page_ids) - 1]
    sum_ref, stat_ref = rest[-2:]
    req_count, page_size = kv_ref.shape[0], kv_ref.shape[1]
    stat_lanes = lax.broadcasted_iota(jnp.int32, (TREE, STAT_LANES), 1)
    for r in range(req_count):
        row0 = r * TREE
        query = stacked_heads(q_ref, row0, group)
        length = lens_ref[r]
        tree_stats = tree_ref[row0 : row0 + TREE, group * HD : group * HD + STAT_LANES]
        blocks = [(
            jnp.concatenate([lane_pick(tree_stats, g) for g in range(group)], axis=0),
            jnp.concatenate([lane_pick(tree_stats, group + g) for g in range(group)], axis=0),
            stacked_heads(tree_ref, row0, group),
        )]
        for page_index, page_ref in zip(page_ids, (kv_ref,) + tuple(pages)):
            positions = lax.broadcasted_iota(jnp.int32, (1, page_size), 1) + page_index * page_size
            blocks.append(attend(query, page_ref[r, :, 0:HD], page_ref[r, :, HD : 2 * HD],
                                 positions < length, False))
        top = blocks[0][0]
        for block in blocks[1:]:
            top = jnp.maximum(top, block[0])
        totals = jnp.zeros_like(top)
        weighted = jnp.zeros(blocks[0][2].shape, jnp.float32)
        for largest, part_totals, part_weighted in blocks:
            factor = jnp.exp(largest - top)
            totals = totals + factor * part_totals
            weighted = weighted + factor * part_weighted
        stats = jnp.zeros((TREE, STAT_LANES), jnp.float32)
        for g in range(group):
            rows = slice(g * TREE, (g + 1) * TREE)
            sum_ref[row0 : row0 + TREE, g * HD : (g + 1) * HD] = weighted[rows]
            stats = jnp.where(stat_lanes == g, top[rows], stats)
            stats = jnp.where(stat_lanes == group + g, totals[rows], stats)
        stat_ref[row0 : row0 + TREE, :] = stats


def local_partial(cache_lens, queries, kv_pool, tree_part, shipped, group):
    req_count, page_count, page_size, row_width = kv_pool.shape
    rows, width = queries.shape
    page_ids = (0,) + tuple(index for index, _ in shipped)
    page_spec = pl.BlockSpec((req_count, page_size, row_width), lambda i, a: (0, 0, 0))
    return pl.pallas_call(
        functools.partial(local_kernel, group, page_ids),
        out_shape=(
            jax.ShapeDtypeStruct((rows, width), jnp.float32),
            jax.ShapeDtypeStruct((rows, STAT_LANES), jnp.float32),
        ),
        grid_spec=pltpu.PrefetchScalarGridSpec(
            num_scalar_prefetch=1,
            grid=(1,),
            in_specs=[
                pl.BlockSpec((rows, width), lambda i, a: (0, 0)),
                pl.BlockSpec((req_count, None, page_size, row_width), lambda i, a: (0, 0, 0, 0)),
                pl.BlockSpec(tree_part.shape, lambda i, a: (0, 0)),
            ] + [page_spec for _ in shipped],
            out_specs=(
                pl.BlockSpec((rows, width), lambda i, a: (0, 0)),
                pl.BlockSpec((rows, STAT_LANES), lambda i, a: (0, 0)),
            ),
        ),
    )(cache_lens, queries, kv_pool, tree_part, *[page for _, page in shipped])


def holder_kernel(page_index, group, q_ref, kv_ref, order_ref, out_ref):
    req_count, page_size = kv_ref.shape[0], kv_ref.shape[1]
    rows = req_count * TREE
    extra = q_ref[rows : rows + EXTRA, :].astype(jnp.float32)
    length_row = extra[0:1, :] * 16.0 + extra[1:2, :]
    positions = (
        lax.broadcasted_iota(jnp.int32, (1, page_size), 1) + page_index * page_size
    ).astype(jnp.float32)
    stat_lanes = lax.broadcasted_iota(jnp.int32, (TREE, STAT_LANES), 1)
    for r in range(req_count):
        row0 = r * TREE
        valid = positions < lane_pick(length_row, r)
        query = stacked_heads(q_ref, row0, group)
        largest, totals, weighted = attend(
            query, kv_ref[r, :, 0:HD], kv_ref[r, :, HD : 2 * HD], valid, True
        )
        total_hi = totals.astype(jnp.bfloat16).astype(jnp.float32)
        total_lo = totals - total_hi
        stats = jnp.zeros((TREE, STAT_LANES), jnp.float32)
        for g in range(group):
            part = slice(g * TREE, (g + 1) * TREE)
            out_ref[row0 : row0 + TREE, g * HD : (g + 1) * HD] = weighted[part].astype(jnp.bfloat16)
            stats = jnp.where(stat_lanes == g, largest[part], stats)
            stats = jnp.where(stat_lanes == group + g, total_hi[part], stats)
            stats = jnp.where(stat_lanes == 2 * group + g, total_lo[part], stats)
        out_ref[row0 : row0 + TREE, group * HD : group * HD + STAT_LANES] = stats.astype(jnp.bfloat16)


def holder_partial(packed_queries, kv_pool, page_index, group, order_after):
    req_count, page_count, page_size, row_width = kv_pool.shape
    packed_rows, width = packed_queries.shape
    rows = req_count * TREE
    return pl.pallas_call(
        functools.partial(holder_kernel, page_index, group),
        out_shape=jax.ShapeDtypeStruct((rows, width + STAT_LANES), jnp.bfloat16),
        grid=(1,),
        in_specs=[
            pl.BlockSpec((packed_rows, width), lambda i: (0, 0)),
            pl.BlockSpec((req_count, None, page_size, row_width), lambda i: (0, page_index, 0, 0)),
            pl.BlockSpec((8, STAT_LANES), lambda i: (0, 0)),
        ],
        out_specs=pl.BlockSpec((rows, width + STAT_LANES), lambda i: (0, 0)),
    )(packed_queries, kv_pool, order_after)


def merge_kernel(group, sum_ref, stat_ref, *rest):
    returned = rest[:-2]
    w_ref = rest[-2]
    out_ref = rest[-1]
    rows = sum_ref.shape[0]
    for r in range(rows // TREE):
        row0 = r * TREE
        local_stats = stat_ref[row0 : row0 + TREE, :]
        heads = []
        for g in range(group):
            cols = slice(g * HD, (g + 1) * HD)
            blocks = [(lane_pick(local_stats, g), lane_pick(local_stats, group + g),
                       sum_ref[row0 : row0 + TREE, cols])]
            for part_ref in returned:
                stats = part_ref[row0 : row0 + TREE, group * HD : group * HD + STAT_LANES].astype(jnp.float32)
                totals = lane_pick(stats, group + g) + lane_pick(stats, 2 * group + g)
                blocks.append((lane_pick(stats, g), totals,
                               part_ref[row0 : row0 + TREE, cols].astype(jnp.float32)))
            top = blocks[0][0]
            for block in blocks[1:]:
                top = jnp.maximum(top, block[0])
            denominator = jnp.zeros_like(top)
            numerator = jnp.zeros((TREE, HD), jnp.float32)
            for largest, totals, weighted in blocks:
                factor = jnp.exp(largest - top)
                denominator = denominator + factor * totals
                numerator = numerator + factor * weighted
            heads.append((numerator / denominator).astype(jnp.bfloat16))
        attention = jnp.concatenate(heads, axis=1)
        out_ref[row0 : row0 + TREE, :] = jnp.dot(
            attention, w_ref[...], preferred_element_type=jnp.float32
        ).astype(out_ref.dtype)


def merge_project(sums, stats, returned, w_out, group):
    rows, width = sums.shape
    part_width = returned[0].shape[1]
    model = w_out.shape[1]
    full = lambda shape: pl.BlockSpec(shape, lambda i: (0, 0))
    return pl.pallas_call(
        functools.partial(merge_kernel, group),
        out_shape=jax.ShapeDtypeStruct((rows, model), jnp.bfloat16),
        grid=(1,),
        in_specs=[full((rows, width)), full((rows, STAT_LANES))]
        + [full((rows, part_width)) for _ in returned]
        + [full(w_out.shape)],
        out_specs=full((rows, model)),
        compiler_params=pltpu.CompilerParams(vmem_limit_bytes=48 * 1024 * 1024),
    )(sums, stats, *returned, w_out)


def pack_queries(queries, lengths):
    width = queries.shape[1]
    count = lengths.shape[0]
    pair = jnp.stack([lengths // 16, lengths % 16]).astype(jnp.bfloat16)
    extra = jnp.pad(pair, ((0, EXTRA - 2), (0, width - count)))
    return jnp.concatenate([queries, extra], axis=0)


def per_device(queries, new_kv, kv_pool, cache_lens, parents, accepted, residual, w_out, norm_gain):
    req_count, page_count, page_size, row_width = kv_pool.shape
    kv_local = row_width // (2 * HD)
    q_local = queries.shape[1] // HD
    group = q_local // kv_local

    shipped = [(p, shifted(kv_pool[:, p], "req", -p)) for p in SHIPPED_PAGES]
    visited = [p for p in range(1, page_count) if p not in SHIPPED_PAGES]
    packed_queries = pack_queries(queries, cache_lens)
    guests = [shifted(packed_queries, "req", p) for p in visited]
    tree_part, accepted_kv = tree_partial(accepted, queries, new_kv, parents, group)
    returned = []
    for page_index, guest in zip(visited, guests):
        part = holder_partial(guest, kv_pool, page_index, group, tree_part)
        returned.append(shifted(part, "req", -page_index))
    sums, stats = local_partial(cache_lens, queries, kv_pool, tree_part, shipped, group)

    product = merge_project(sums, stats, returned, w_out, group)
    tp_count = lax.axis_size("tp")
    pieces = product.reshape(tp_count, product.shape[0] // tp_count, product.shape[1])
    gathered = lax.all_to_all(pieces, "tp", 0, 0, tiled=False)
    summed = jnp.sum(gathered.astype(jnp.float32), axis=0)
    hidden_out = (residual.astype(jnp.float32) + summed).astype(jnp.bfloat16)
    widened = hidden_out.astype(jnp.float32)
    normed = (
        widened * lax.rsqrt(jnp.mean(widened * widened, axis=-1, keepdims=True) + 1e-05) * norm_gain
    ).astype(jnp.bfloat16)
    return (hidden_out, normed, accepted_kv)


def solution(mesh):
    placed = (
        P("req", "tp"),
        P("req", "tp"),
        P("req", None, None, "tp"),
        P("req"),
        P("req", None),
        P("req"),
        P(("req", "tp"), None),
        P("tp", None),
        P(),
    )
    return jax.shard_map(
        per_device,
        mesh=mesh,
        in_specs=placed,
        out_specs=(P(("req", "tp"), None), P(("req", "tp"), None), P("req", None, "tp")),
        check_vma=False,
    )
```

```python
import functools

import jax
import jax.numpy as jnp
from jax import lax
from jax.experimental import pallas as pl
from jax.experimental.pallas import tpu as pltpu
from jax.sharding import PartitionSpec as P

HD = 128
TREE = 32
MAXD = 7
PATH = 8
EXTRA = 16
STAT_LANES = 128
SHIPPED_PAGES = (1,)


NEGATIVE = -1e30


def shifted(value, axis, steps):
    count = lax.axis_size(axis)
    pairs = [(source, (source + steps) % count) for source in range(count)]
    return lax.ppermute(value, axis, pairs)


def attend(query, key, value, valid, round_max):
    scores = lax.dot_general(
        query, key, (((1,), (1,)), ((), ())), preferred_element_type=jnp.float32
    ) * (HD ** (-0.5))
    scores = jnp.where(valid, scores, NEGATIVE)
    largest = jnp.max(scores, axis=1, keepdims=True)
    if round_max:
        largest = largest.astype(jnp.bfloat16).astype(jnp.float32)
    weights = jnp.where(valid, jnp.exp(scores - largest), 0.0)
    totals = jnp.sum(weights, axis=1, keepdims=True)
    weighted = jnp.dot(
        weights.astype(jnp.bfloat16), value, preferred_element_type=jnp.float32
    )
    return largest, totals, weighted


def lane_pick(block, lane):
    lanes = lax.broadcasted_iota(jnp.int32, block.shape, 1)
    return jnp.sum(jnp.where(lanes == lane, block, 0.0), axis=1, keepdims=True)


def stacked_heads(rows_ref, row0, group):
    parts = [rows_ref[row0 : row0 + TREE, g * HD : (g + 1) * HD] for g in range(group)]
    return jnp.concatenate(parts, axis=0)


def tree_kernel(group, acc_ref, q_ref, fresh_ref, parent_ref, part_ref, path_ref):
    rows = fresh_ref.shape[0]
    req_count = rows // TREE
    sub = lax.broadcasted_iota(jnp.int32, (rows, rows), 0)
    lane = lax.broadcasted_iota(jnp.int32, (rows, rows), 1)
    same_block = (sub // TREE) == (lane // TREE)
    reach = jnp.where((parent_ref[...] == lane) | (sub == lane), 1.0, 0.0)
    for _ in range(3):
        square = jnp.dot(reach.astype(jnp.bfloat16), reach.astype(jnp.bfloat16),
                         preferred_element_type=jnp.float32)
        reach = jnp.minimum(square, 1.0)
    inclusive = jnp.where(same_block & (sub <= lane), 1.0, 0.0).astype(jnp.bfloat16)
    sel_sub = lax.broadcasted_iota(jnp.int32, (req_count * PATH, rows), 0)
    sel_lane = lax.broadcasted_iota(jnp.int32, (req_count * PATH, rows), 1)
    chosen = jnp.zeros((req_count * PATH, rows), jnp.float32)
    for r in range(req_count):
        target = r * TREE + acc_ref[r]
        chosen = jnp.where((sel_sub // PATH == r) & (sel_lane == target), 1.0, chosen)
    on_path = jnp.dot(chosen.astype(jnp.bfloat16), reach.astype(jnp.bfloat16),
                      preferred_element_type=jnp.float32)
    rank = jnp.dot(on_path.astype(jnp.bfloat16), inclusive, preferred_element_type=jnp.float32)
    slot = (sel_sub % PATH).astype(jnp.float32)
    selector = jnp.where((rank - 1.0 == slot) & (on_path > 0.5), 1.0, 0.0)
    path = jnp.dot(selector.astype(jnp.bfloat16), fresh_ref[...],
                   preferred_element_type=jnp.float32).astype(path_ref.dtype)
    for r in range(req_count):
        path_ref[r] = path[r * PATH : (r + 1) * PATH]

    valid = jnp.concatenate([reach > 0.5] * group, axis=0)
    query = jnp.concatenate([q_ref[:, g * HD : (g + 1) * HD] for g in range(group)], axis=0)
    largest, totals, weighted = attend(query, fresh_ref[:, 0:HD], fresh_ref[:, HD : 2 * HD], valid, False)
    stat_lanes = lax.broadcasted_iota(jnp.int32, (rows, STAT_LANES), 1)
    stats = jnp.zeros((rows, STAT_LANES), jnp.float32)
    for g in range(group):
        part = slice(g * rows, (g + 1) * rows)
        stats = jnp.where(stat_lanes == g, largest[part], stats)
        stats = jnp.where(stat_lanes == group + g, totals[part], stats)
        part_ref[:, g * HD : (g + 1) * HD] = weighted[part]
    part_ref[:, group * HD : group * HD + STAT_LANES] = stats


def tree_partial(accepted, queries, new_kv, parents, group):
    rows, width = queries.shape
    req_count = parents.shape[0]
    row_width = new_kv.shape[1]
    offsets = TREE * jnp.arange(req_count, dtype=jnp.int32)[:, None]
    parent_rows = (parents + offsets).reshape(rows, 1)
    full = lambda shape: pl.BlockSpec(shape, lambda i, a: (0,) * len(shape))
    return pl.pallas_call(
        functools.partial(tree_kernel, group),
        out_shape=(
            jax.ShapeDtypeStruct((rows, width + STAT_LANES), jnp.float32),
            jax.ShapeDtypeStruct((req_count, PATH, row_width), jnp.bfloat16),
        ),
        grid_spec=pltpu.PrefetchScalarGridSpec(
            num_scalar_prefetch=1,
            grid=(1,),
            in_specs=[full((rows, width)), full((rows, row_width)), full((rows, 1))],
            out_specs=(full((rows, width + STAT_LANES)), full((req_count, PATH, row_width))),
        ),
    )(accepted, queries, new_kv, parent_rows)


def local_kernel(group, page_ids, lens_ref, q_ref, kv_ref, tree_ref, *rest):
    pages = rest[: len(page_ids) - 1]
    sum_ref, stat_ref = rest[-2:]
    req_count, page_size = kv_ref.shape[0], kv_ref.shape[1]
    stat_lanes = lax.broadcasted_iota(jnp.int32, (TREE, STAT_LANES), 1)
    for r in range(req_count):
        row0 = r * TREE
        query = stacked_heads(q_ref, row0, group)
        length = lens_ref[r]
        tree_stats = tree_ref[row0 : row0 + TREE, group * HD : group * HD + STAT_LANES]
        blocks = [(
            jnp.concatenate([lane_pick(tree_stats, g) for g in range(group)], axis=0),
            jnp.concatenate([lane_pick(tree_stats, group + g) for g in range(group)], axis=0),
            stacked_heads(tree_ref, row0, group),
        )]
        for page_index, page_ref in zip(page_ids, (kv_ref,) + tuple(pages)):
            positions = lax.broadcasted_iota(jnp.int32, (1, page_size), 1) + page_index * page_size
            blocks.append(attend(query, page_ref[r, :, 0:HD], page_ref[r, :, HD : 2 * HD],
                                 positions < length, False))
        top = blocks[0][0]
        for block in blocks[1:]:
            top = jnp.maximum(top, block[0])
        totals = jnp.zeros_like(top)
        weighted = jnp.zeros(blocks[0][2].shape, jnp.float32)
        for largest, part_totals, part_weighted in blocks:
            factor = jnp.exp(largest - top)
            totals = totals + factor * part_totals
            weighted = weighted + factor * part_weighted
        stats = jnp.zeros((TREE, STAT_LANES), jnp.float32)
        for g in range(group):
            rows = slice(g * TREE, (g + 1) * TREE)
            sum_ref[row0 : row0 + TREE, g * HD : (g + 1) * HD] = weighted[rows]
            stats = jnp.where(stat_lanes == g, top[rows], stats)
            stats = jnp.where(stat_lanes == group + g, totals[rows], stats)
        stat_ref[row0 : row0 + TREE, :] = stats


def local_partial(cache_lens, queries, kv_pool, tree_part, shipped, group):
    req_count, page_count, page_size, row_width = kv_pool.shape
    rows, width = queries.shape
    page_ids = (0,) + tuple(index for index, _ in shipped)
    page_spec = pl.BlockSpec((req_count, page_size, row_width), lambda i, a: (0, 0, 0))
    return pl.pallas_call(
        functools.partial(local_kernel, group, page_ids),
        out_shape=(
            jax.ShapeDtypeStruct((rows, width), jnp.float32),
            jax.ShapeDtypeStruct((rows, STAT_LANES), jnp.float32),
        ),
        grid_spec=pltpu.PrefetchScalarGridSpec(
            num_scalar_prefetch=1,
            grid=(1,),
            in_specs=[
                pl.BlockSpec((rows, width), lambda i, a: (0, 0)),
                pl.BlockSpec((req_count, None, page_size, row_width), lambda i, a: (0, 0, 0, 0)),
                pl.BlockSpec(tree_part.shape, lambda i, a: (0, 0)),
            ] + [page_spec for _ in shipped],
            out_specs=(
                pl.BlockSpec((rows, width), lambda i, a: (0, 0)),
                pl.BlockSpec((rows, STAT_LANES), lambda i, a: (0, 0)),
            ),
        ),
    )(cache_lens, queries, kv_pool, tree_part, *[page for _, page in shipped])


def holder_kernel(page_index, group, q_ref, kv_ref, order_ref, out_ref):
    req_count, page_size = kv_ref.shape[0], kv_ref.shape[1]
    rows = req_count * TREE
    extra = q_ref[rows : rows + EXTRA, :].astype(jnp.float32)
    length_row = extra[0:1, :] * 16.0 + extra[1:2, :]
    positions = (
        lax.broadcasted_iota(jnp.int32, (1, page_size), 1) + page_index * page_size
    ).astype(jnp.float32)
    stat_lanes = lax.broadcasted_iota(jnp.int32, (TREE, STAT_LANES), 1)
    for r in range(req_count):
        row0 = r * TREE
        valid = positions < lane_pick(length_row, r)
        query = stacked_heads(q_ref, row0, group)
        largest, totals, weighted = attend(
            query, kv_ref[r, :, 0:HD], kv_ref[r, :, HD : 2 * HD], valid, True
        )
        total_hi = totals.astype(jnp.bfloat16).astype(jnp.float32)
        total_lo = totals - total_hi
        stats = jnp.zeros((TREE, STAT_LANES), jnp.float32)
        for g in range(group):
            part = slice(g * TREE, (g + 1) * TREE)
            out_ref[row0 : row0 + TREE, g * HD : (g + 1) * HD] = weighted[part].astype(jnp.bfloat16)
            stats = jnp.where(stat_lanes == g, largest[part], stats)
            stats = jnp.where(stat_lanes == group + g, total_hi[part], stats)
            stats = jnp.where(stat_lanes == 2 * group + g, total_lo[part], stats)
        out_ref[row0 : row0 + TREE, group * HD : group * HD + STAT_LANES] = stats.astype(jnp.bfloat16)


def holder_partial(packed_queries, kv_pool, page_index, group, order_after):
    req_count, page_count, page_size, row_width = kv_pool.shape
    packed_rows, width = packed_queries.shape
    rows = req_count * TREE
    return pl.pallas_call(
        functools.partial(holder_kernel, page_index, group),
        out_shape=jax.ShapeDtypeStruct((rows, width + STAT_LANES), jnp.bfloat16),
        grid=(1,),
        in_specs=[
            pl.BlockSpec((packed_rows, width), lambda i: (0, 0)),
            pl.BlockSpec((req_count, None, page_size, row_width), lambda i: (0, page_index, 0, 0)),
            pl.BlockSpec((8, STAT_LANES), lambda i: (0, 0)),
        ],
        out_specs=pl.BlockSpec((rows, width + STAT_LANES), lambda i: (0, 0)),
    )(packed_queries, kv_pool, order_after)


def merge_kernel(group, sum_ref, stat_ref, *rest):
    returned = rest[:-2]
    w_ref = rest[-2]
    out_ref = rest[-1]
    rows = sum_ref.shape[0]
    for r in range(rows // TREE):
        row0 = r * TREE
        local_stats = stat_ref[row0 : row0 + TREE, :]
        heads = []
        for g in range(group):
            cols = slice(g * HD, (g + 1) * HD)
            blocks = [(lane_pick(local_stats, g), lane_pick(local_stats, group + g),
                       sum_ref[row0 : row0 + TREE, cols])]
            for part_ref in returned:
                stats = part_ref[row0 : row0 + TREE, group * HD : group * HD + STAT_LANES].astype(jnp.float32)
                totals = lane_pick(stats, group + g) + lane_pick(stats, 2 * group + g)
                blocks.append((lane_pick(stats, g), totals,
                               part_ref[row0 : row0 + TREE, cols].astype(jnp.float32)))
            top = blocks[0][0]
            for block in blocks[1:]:
                top = jnp.maximum(top, block[0])
            denominator = jnp.zeros_like(top)
            numerator = jnp.zeros((TREE, HD), jnp.float32)
            for largest, totals, weighted in blocks:
                factor = jnp.exp(largest - top)
                denominator = denominator + factor * totals
                numerator = numerator + factor * weighted
            heads.append((numerator / denominator).astype(jnp.bfloat16))
        attention = jnp.concatenate(heads, axis=1)
        out_ref[row0 : row0 + TREE, :] = jnp.dot(
            attention, w_ref[...], preferred_element_type=jnp.float32
        ).astype(out_ref.dtype)


def merge_project(sums, stats, returned, w_out, group):
    rows, width = sums.shape
    part_width = returned[0].shape[1]
    model = w_out.shape[1]
    full = lambda shape: pl.BlockSpec(shape, lambda i: (0, 0))
    return pl.pallas_call(
        functools.partial(merge_kernel, group),
        out_shape=jax.ShapeDtypeStruct((rows, model), jnp.bfloat16),
        grid=(1,),
        in_specs=[full((rows, width)), full((rows, STAT_LANES))]
        + [full((rows, part_width)) for _ in returned]
        + [full(w_out.shape)],
        out_specs=full((rows, model)),
        compiler_params=pltpu.CompilerParams(vmem_limit_bytes=48 * 1024 * 1024),
    )(sums, stats, *returned, w_out)


def chain_reduce_scatter(product, axis):
    count = lax.axis_size(axis)
    me = lax.axis_index(axis)
    chunk = product.shape[0] // count
    pieces = product.reshape(count, chunk, product.shape[1])

    def piece(offset):
        return lax.dynamic_index_in_dim(pieces, (me + offset) % count, 0, keepdims=False)

    forward_hops = count // 2
    backward_hops = count - 1 - forward_hops
    forward = piece(forward_hops)
    backward = piece(-backward_hops) if backward_hops > 0 else None
    for step in range(1, forward_hops + 1):
        forward = shifted(forward, axis, 1)
        if backward is not None and step <= backward_hops:
            backward = shifted(backward, axis, -1)
        if step < forward_hops:
            forward = (forward.astype(jnp.float32)
                       + piece(forward_hops - step).astype(jnp.float32)).astype(jnp.bfloat16)
        if backward is not None and step < backward_hops:
            backward = (backward.astype(jnp.float32)
                        + piece(step - backward_hops).astype(jnp.float32)).astype(jnp.bfloat16)
    total = piece(0).astype(jnp.float32) + forward.astype(jnp.float32)
    if backward is not None:
        total = total + backward.astype(jnp.float32)
    return total


def pack_queries(queries, lengths):
    width = queries.shape[1]
    count = lengths.shape[0]
    pair = jnp.stack([lengths // 16, lengths % 16]).astype(jnp.bfloat16)
    extra = jnp.pad(pair, ((0, EXTRA - 2), (0, width - count)))
    return jnp.concatenate([queries, extra], axis=0)


def per_device(queries, new_kv, kv_pool, cache_lens, parents, accepted, residual, w_out, norm_gain):
    req_count, page_count, page_size, row_width = kv_pool.shape
    kv_local = row_width // (2 * HD)
    q_local = queries.shape[1] // HD
    group = q_local // kv_local

    shipped = [(p, shifted(kv_pool[:, p], "req", -p)) for p in SHIPPED_PAGES]
    visited = [p for p in range(1, page_count) if p not in SHIPPED_PAGES]
    packed_queries = pack_queries(queries, cache_lens)
    guests = [shifted(packed_queries, "req", p) for p in visited]
    tree_part, accepted_kv = tree_partial(accepted, queries, new_kv, parents, group)
    returned = []
    for page_index, guest in zip(visited, guests):
        part = holder_partial(guest, kv_pool, page_index, group, tree_part)
        returned.append(shifted(part, "req", -page_index))
    sums, stats = local_partial(cache_lens, queries, kv_pool, tree_part, shipped, group)

    product = merge_project(sums, stats, returned, w_out, group)
    summed = chain_reduce_scatter(product, "tp")
    hidden_out = (residual.astype(jnp.float32) + summed).astype(jnp.bfloat16)
    widened = hidden_out.astype(jnp.float32)
    normed = (
        widened * lax.rsqrt(jnp.mean(widened * widened, axis=-1, keepdims=True) + 1e-05) * norm_gain
    ).astype(jnp.bfloat16)
    return (hidden_out, normed, accepted_kv)


def solution(mesh):
    placed = (
        P("req", "tp"),
        P("req", "tp"),
        P("req", None, None, "tp"),
        P("req"),
        P("req", None),
        P("req"),
        P(("req", "tp"), None),
        P("tp", None),
        P(),
    )
    return jax.shard_map(
        per_device,
        mesh=mesh,
        in_specs=placed,
        out_specs=(P(("req", "tp"), None), P(("req", "tp"), None), P("req", None, "tp")),
        check_vma=False,
    )
```

```python
import functools

import jax
import jax.numpy as jnp
from jax import lax
from jax.experimental import pallas as pl
from jax.experimental.pallas import tpu as pltpu
from jax.sharding import PartitionSpec as P

HD = 128
TREE = 32
MAXD = 7
PATH = 8
EXTRA = 16
STAT_LANES = 128
SHIPPED_PAGES = (1,)


NEGATIVE = -1e30


def shifted(value, axis, steps):
    count = lax.axis_size(axis)
    pairs = [(source, (source + steps) % count) for source in range(count)]
    return lax.ppermute(value, axis, pairs)


def attend(query, key, value, valid, round_max):
    scores = lax.dot_general(
        query, key, (((1,), (1,)), ((), ())), preferred_element_type=jnp.float32
    ) * (HD ** (-0.5))
    scores = jnp.where(valid, scores, NEGATIVE)
    largest = jnp.max(scores, axis=1, keepdims=True)
    if round_max:
        largest = largest.astype(jnp.bfloat16).astype(jnp.float32)
    weights = jnp.where(valid, jnp.exp(scores - largest), 0.0)
    totals = jnp.sum(weights, axis=1, keepdims=True)
    weighted = jnp.dot(
        weights.astype(jnp.bfloat16), value, preferred_element_type=jnp.float32
    )
    return largest, totals, weighted


def lane_pick(block, lane):
    lanes = lax.broadcasted_iota(jnp.int32, block.shape, 1)
    return jnp.sum(jnp.where(lanes == lane, block, 0.0), axis=1, keepdims=True)


def stacked_heads(rows_ref, row0, group):
    parts = [rows_ref[row0 : row0 + TREE, g * HD : (g + 1) * HD] for g in range(group)]
    return jnp.concatenate(parts, axis=0)


def tree_kernel(group, acc_ref, q_ref, fresh_ref, parent_ref, part_ref, path_ref):
    rows = fresh_ref.shape[0]
    req_count = rows // TREE
    sub = lax.broadcasted_iota(jnp.int32, (rows, rows), 0)
    lane = lax.broadcasted_iota(jnp.int32, (rows, rows), 1)
    same_block = (sub // TREE) == (lane // TREE)
    reach = jnp.where((parent_ref[...] == lane) | (sub == lane), 1.0, 0.0)
    for _ in range(3):
        square = jnp.dot(reach.astype(jnp.bfloat16), reach.astype(jnp.bfloat16),
                         preferred_element_type=jnp.float32)
        reach = jnp.minimum(square, 1.0)
    inclusive = jnp.where(same_block & (sub <= lane), 1.0, 0.0).astype(jnp.bfloat16)
    sel_sub = lax.broadcasted_iota(jnp.int32, (req_count * PATH, rows), 0)
    sel_lane = lax.broadcasted_iota(jnp.int32, (req_count * PATH, rows), 1)
    chosen = jnp.zeros((req_count * PATH, rows), jnp.float32)
    for r in range(req_count):
        target = r * TREE + acc_ref[r]
        chosen = jnp.where((sel_sub // PATH == r) & (sel_lane == target), 1.0, chosen)
    on_path = jnp.dot(chosen.astype(jnp.bfloat16), reach.astype(jnp.bfloat16),
                      preferred_element_type=jnp.float32)
    rank = jnp.dot(on_path.astype(jnp.bfloat16), inclusive, preferred_element_type=jnp.float32)
    slot = (sel_sub % PATH).astype(jnp.float32)
    selector = jnp.where((rank - 1.0 == slot) & (on_path > 0.5), 1.0, 0.0)
    path = jnp.dot(selector.astype(jnp.bfloat16), fresh_ref[...],
                   preferred_element_type=jnp.float32).astype(path_ref.dtype)
    for r in range(req_count):
        path_ref[r] = path[r * PATH : (r + 1) * PATH]

    valid = jnp.concatenate([reach > 0.5] * group, axis=0)
    query = jnp.concatenate([q_ref[:, g * HD : (g + 1) * HD] for g in range(group)], axis=0)
    largest, totals, weighted = attend(query, fresh_ref[:, 0:HD], fresh_ref[:, HD : 2 * HD], valid, False)
    stat_lanes = lax.broadcasted_iota(jnp.int32, (rows, STAT_LANES), 1)
    stats = jnp.zeros((rows, STAT_LANES), jnp.float32)
    for g in range(group):
        part = slice(g * rows, (g + 1) * rows)
        stats = jnp.where(stat_lanes == g, largest[part], stats)
        stats = jnp.where(stat_lanes == group + g, totals[part], stats)
        part_ref[:, g * HD : (g + 1) * HD] = weighted[part]
    part_ref[:, group * HD : group * HD + STAT_LANES] = stats


def tree_partial(accepted, queries, new_kv, parents, group):
    rows, width = queries.shape
    req_count = parents.shape[0]
    row_width = new_kv.shape[1]
    offsets = TREE * jnp.arange(req_count, dtype=jnp.int32)[:, None]
    parent_rows = (parents + offsets).reshape(rows, 1)
    full = lambda shape: pl.BlockSpec(shape, lambda i, a: (0,) * len(shape))
    return pl.pallas_call(
        functools.partial(tree_kernel, group),
        out_shape=(
            jax.ShapeDtypeStruct((rows, width + STAT_LANES), jnp.float32),
            jax.ShapeDtypeStruct((req_count, PATH, row_width), jnp.bfloat16),
        ),
        grid_spec=pltpu.PrefetchScalarGridSpec(
            num_scalar_prefetch=1,
            grid=(1,),
            in_specs=[full((rows, width)), full((rows, row_width)), full((rows, 1))],
            out_specs=(full((rows, width + STAT_LANES)), full((req_count, PATH, row_width))),
        ),
    )(accepted, queries, new_kv, parent_rows)


def local_kernel(group, page_ids, lens_ref, q_ref, kv_ref, tree_ref, *rest):
    pages = rest[: len(page_ids) - 1]
    sum_ref, stat_ref = rest[-2:]
    req_count, page_size = kv_ref.shape[0], kv_ref.shape[1]
    stat_lanes = lax.broadcasted_iota(jnp.int32, (TREE, STAT_LANES), 1)
    for r in range(req_count):
        row0 = r * TREE
        query = stacked_heads(q_ref, row0, group)
        length = lens_ref[r]
        tree_stats = tree_ref[row0 : row0 + TREE, group * HD : group * HD + STAT_LANES]
        blocks = [(
            jnp.concatenate([lane_pick(tree_stats, g) for g in range(group)], axis=0),
            jnp.concatenate([lane_pick(tree_stats, group + g) for g in range(group)], axis=0),
            stacked_heads(tree_ref, row0, group),
        )]
        for page_index, page_ref in zip(page_ids, (kv_ref,) + tuple(pages)):
            positions = lax.broadcasted_iota(jnp.int32, (1, page_size), 1) + page_index * page_size
            blocks.append(attend(query, page_ref[r, :, 0:HD], page_ref[r, :, HD : 2 * HD],
                                 positions < length, False))
        top = blocks[0][0]
        for block in blocks[1:]:
            top = jnp.maximum(top, block[0])
        totals = jnp.zeros_like(top)
        weighted = jnp.zeros(blocks[0][2].shape, jnp.float32)
        for largest, part_totals, part_weighted in blocks:
            factor = jnp.exp(largest - top)
            totals = totals + factor * part_totals
            weighted = weighted + factor * part_weighted
        stats = jnp.zeros((TREE, STAT_LANES), jnp.float32)
        for g in range(group):
            rows = slice(g * TREE, (g + 1) * TREE)
            sum_ref[row0 : row0 + TREE, g * HD : (g + 1) * HD] = weighted[rows]
            stats = jnp.where(stat_lanes == g, top[rows], stats)
            stats = jnp.where(stat_lanes == group + g, totals[rows], stats)
        stat_ref[row0 : row0 + TREE, :] = stats


def local_partial(cache_lens, queries, kv_pool, tree_part, shipped, group):
    req_count, page_count, page_size, row_width = kv_pool.shape
    rows, width = queries.shape
    page_ids = (0,) + tuple(index for index, _ in shipped)
    page_spec = pl.BlockSpec((req_count, page_size, row_width), lambda i, a: (0, 0, 0))
    return pl.pallas_call(
        functools.partial(local_kernel, group, page_ids),
        out_shape=(
            jax.ShapeDtypeStruct((rows, width), jnp.float32),
            jax.ShapeDtypeStruct((rows, STAT_LANES), jnp.float32),
        ),
        grid_spec=pltpu.PrefetchScalarGridSpec(
            num_scalar_prefetch=1,
            grid=(1,),
            in_specs=[
                pl.BlockSpec((rows, width), lambda i, a: (0, 0)),
                pl.BlockSpec((req_count, None, page_size, row_width), lambda i, a: (0, 0, 0, 0)),
                pl.BlockSpec(tree_part.shape, lambda i, a: (0, 0)),
            ] + [page_spec for _ in shipped],
            out_specs=(
                pl.BlockSpec((rows, width), lambda i, a: (0, 0)),
                pl.BlockSpec((rows, STAT_LANES), lambda i, a: (0, 0)),
            ),
        ),
    )(cache_lens, queries, kv_pool, tree_part, *[page for _, page in shipped])


def holder_kernel(page_index, group, q_ref, kv_ref, order_ref, out_ref):
    req_count, page_size = kv_ref.shape[0], kv_ref.shape[1]
    rows = req_count * TREE
    extra = q_ref[rows : rows + EXTRA, :].astype(jnp.float32)
    length_row = extra[0:1, :] * 16.0 + extra[1:2, :]
    positions = (
        lax.broadcasted_iota(jnp.int32, (1, page_size), 1) + page_index * page_size
    ).astype(jnp.float32)
    stat_lanes = lax.broadcasted_iota(jnp.int32, (TREE, STAT_LANES), 1)
    for r in range(req_count):
        row0 = r * TREE
        valid = positions < lane_pick(length_row, r)
        query = stacked_heads(q_ref, row0, group)
        largest, totals, weighted = attend(
            query, kv_ref[r, :, 0:HD], kv_ref[r, :, HD : 2 * HD], valid, True
        )
        total_hi = totals.astype(jnp.bfloat16).astype(jnp.float32)
        total_lo = totals - total_hi
        stats = jnp.zeros((TREE, STAT_LANES), jnp.float32)
        for g in range(group):
            part = slice(g * TREE, (g + 1) * TREE)
            out_ref[row0 : row0 + TREE, g * HD : (g + 1) * HD] = weighted[part].astype(jnp.bfloat16)
            stats = jnp.where(stat_lanes == g, largest[part], stats)
            stats = jnp.where(stat_lanes == group + g, total_hi[part], stats)
            stats = jnp.where(stat_lanes == 2 * group + g, total_lo[part], stats)
        out_ref[row0 : row0 + TREE, group * HD : group * HD + STAT_LANES] = stats.astype(jnp.bfloat16)


def holder_partial(packed_queries, kv_pool, page_index, group, order_after):
    req_count, page_count, page_size, row_width = kv_pool.shape
    packed_rows, width = packed_queries.shape
    rows = req_count * TREE
    return pl.pallas_call(
        functools.partial(holder_kernel, page_index, group),
        out_shape=jax.ShapeDtypeStruct((rows, width + STAT_LANES), jnp.bfloat16),
        grid=(1,),
        in_specs=[
            pl.BlockSpec((packed_rows, width), lambda i: (0, 0)),
            pl.BlockSpec((req_count, None, page_size, row_width), lambda i: (0, page_index, 0, 0)),
            pl.BlockSpec((8, STAT_LANES), lambda i: (0, 0)),
        ],
        out_specs=pl.BlockSpec((rows, width + STAT_LANES), lambda i: (0, 0)),
    )(packed_queries, kv_pool, order_after)


def merge_kernel(group, sum_ref, stat_ref, *rest):
    returned = rest[:-2]
    w_ref = rest[-2]
    out_ref = rest[-1]
    rows = sum_ref.shape[0]
    for r in range(rows // TREE):
        row0 = r * TREE
        local_stats = stat_ref[row0 : row0 + TREE, :]
        heads = []
        for g in range(group):
            cols = slice(g * HD, (g + 1) * HD)
            blocks = [(lane_pick(local_stats, g), lane_pick(local_stats, group + g),
                       sum_ref[row0 : row0 + TREE, cols])]
            for part_ref in returned:
                stats = part_ref[row0 : row0 + TREE, group * HD : group * HD + STAT_LANES].astype(jnp.float32)
                totals = lane_pick(stats, group + g) + lane_pick(stats, 2 * group + g)
                blocks.append((lane_pick(stats, g), totals,
                               part_ref[row0 : row0 + TREE, cols].astype(jnp.float32)))
            top = blocks[0][0]
            for block in blocks[1:]:
                top = jnp.maximum(top, block[0])
            denominator = jnp.zeros_like(top)
            numerator = jnp.zeros((TREE, HD), jnp.float32)
            for largest, totals, weighted in blocks:
                factor = jnp.exp(largest - top)
                denominator = denominator + factor * totals
                numerator = numerator + factor * weighted
            heads.append((numerator / denominator).astype(jnp.bfloat16))
        attention = jnp.concatenate(heads, axis=1)
        out_ref[row0 : row0 + TREE, :] = jnp.dot(
            attention, w_ref[...], preferred_element_type=jnp.float32
        ).astype(out_ref.dtype)


def merge_project(sums, stats, returned, w_out, group):
    rows, width = sums.shape
    part_width = returned[0].shape[1]
    model = w_out.shape[1]
    full = lambda shape: pl.BlockSpec(shape, lambda i: (0, 0))
    return pl.pallas_call(
        functools.partial(merge_kernel, group),
        out_shape=jax.ShapeDtypeStruct((rows, model), jnp.bfloat16),
        grid=(1,),
        in_specs=[full((rows, width)), full((rows, STAT_LANES))]
        + [full((rows, part_width)) for _ in returned]
        + [full(w_out.shape)],
        out_specs=full((rows, model)),
        compiler_params=pltpu.CompilerParams(vmem_limit_bytes=48 * 1024 * 1024),
    )(sums, stats, *returned, w_out)


def chain_reduce_scatter(product, axis):
    count = lax.axis_size(axis)
    me = lax.axis_index(axis)
    chunk = product.shape[0] // count
    pieces = product.reshape(count, chunk, product.shape[1])

    def piece(offset):
        return lax.dynamic_index_in_dim(pieces, (me + offset) % count, 0, keepdims=False)

    hops = (count - 1) // 2
    opposite = None
    if count % 2 == 0:
        opposite = shifted(piece(count // 2), axis, count // 2)
    forward = piece(hops) if hops > 0 else None
    backward = piece(-hops) if hops > 0 else None
    for step in range(1, hops + 1):
        forward = shifted(forward, axis, 1)
        backward = shifted(backward, axis, -1)
        if step < hops:
            forward = (forward.astype(jnp.float32)
                       + piece(hops - step).astype(jnp.float32)).astype(jnp.bfloat16)
            backward = (backward.astype(jnp.float32)
                        + piece(step - hops).astype(jnp.float32)).astype(jnp.bfloat16)
    total = piece(0).astype(jnp.float32)
    if hops > 0:
        total = total + forward.astype(jnp.float32) + backward.astype(jnp.float32)
    if opposite is not None:
        total = total + opposite.astype(jnp.float32)
    return total


def pack_queries(queries, lengths):
    width = queries.shape[1]
    count = lengths.shape[0]
    pair = jnp.stack([lengths // 16, lengths % 16]).astype(jnp.bfloat16)
    extra = jnp.pad(pair, ((0, EXTRA - 2), (0, width - count)))
    return jnp.concatenate([queries, extra], axis=0)


def per_device(queries, new_kv, kv_pool, cache_lens, parents, accepted, residual, w_out, norm_gain):
    req_count, page_count, page_size, row_width = kv_pool.shape
    kv_local = row_width // (2 * HD)
    q_local = queries.shape[1] // HD
    group = q_local // kv_local

    shipped = [(p, shifted(kv_pool[:, p], "req", -p)) for p in SHIPPED_PAGES]
    visited = [p for p in range(1, page_count) if p not in SHIPPED_PAGES]
    packed_queries = pack_queries(queries, cache_lens)
    guests = [shifted(packed_queries, "req", p) for p in visited]
    tree_part, accepted_kv = tree_partial(accepted, queries, new_kv, parents, group)
    returned = []
    for page_index, guest in zip(visited, guests):
        part = holder_partial(guest, kv_pool, page_index, group, tree_part)
        returned.append(shifted(part, "req", -page_index))
    sums, stats = local_partial(cache_lens, queries, kv_pool, tree_part, shipped, group)

    product = merge_project(sums, stats, returned, w_out, group)
    summed = chain_reduce_scatter(product, "tp")
    hidden_out = (residual.astype(jnp.float32) + summed).astype(jnp.bfloat16)
    widened = hidden_out.astype(jnp.float32)
    normed = (
        widened * lax.rsqrt(jnp.mean(widened * widened, axis=-1, keepdims=True) + 1e-05) * norm_gain
    ).astype(jnp.bfloat16)
    return (hidden_out, normed, accepted_kv)


def solution(mesh):
    placed = (
        P("req", "tp"),
        P("req", "tp"),
        P("req", None, None, "tp"),
        P("req"),
        P("req", None),
        P("req"),
        P(("req", "tp"), None),
        P("tp", None),
        P(),
    )
    return jax.shard_map(
        per_device,
        mesh=mesh,
        in_specs=placed,
        out_specs=(P(("req", "tp"), None), P(("req", "tp"), None), P("req", None, "tp")),
        check_vma=False,
    )
```

```python
import functools

import jax
import jax.numpy as jnp
from jax import lax
from jax.experimental import pallas as pl
from jax.experimental.pallas import tpu as pltpu
from jax.sharding import PartitionSpec as P

HD = 128
TREE = 32
MAXD = 7
PATH = 8
EXTRA = 16
STAT_LANES = 128
SHIPPED_PAGES = (1,)


NEGATIVE = -1e30


def shifted(value, axis, steps):
    count = lax.axis_size(axis)
    pairs = [(source, (source + steps) % count) for source in range(count)]
    return lax.ppermute(value, axis, pairs)


def attend(query, key, value, valid, round_max):
    scores = lax.dot_general(
        query, key, (((1,), (1,)), ((), ())), preferred_element_type=jnp.float32
    ) * (HD ** (-0.5))
    scores = jnp.where(valid, scores, NEGATIVE)
    largest = jnp.max(scores, axis=1, keepdims=True)
    if round_max:
        largest = largest.astype(jnp.bfloat16).astype(jnp.float32)
    weights = jnp.where(valid, jnp.exp(scores - largest), 0.0)
    totals = jnp.sum(weights, axis=1, keepdims=True)
    weighted = jnp.dot(
        weights.astype(jnp.bfloat16), value, preferred_element_type=jnp.float32
    )
    return largest, totals, weighted


def lane_pick(block, lane):
    lanes = lax.broadcasted_iota(jnp.int32, block.shape, 1)
    return jnp.sum(jnp.where(lanes == lane, block, 0.0), axis=1, keepdims=True)


def stacked_heads(rows_ref, row0, group):
    parts = [rows_ref[row0 : row0 + TREE, g * HD : (g + 1) * HD] for g in range(group)]
    return jnp.concatenate(parts, axis=0)


def tree_kernel(group, acc_ref, q_ref, fresh_ref, parent_ref, part_ref, path_ref):
    rows = fresh_ref.shape[0]
    req_count = rows // TREE
    sub = lax.broadcasted_iota(jnp.int32, (rows, rows), 0)
    lane = lax.broadcasted_iota(jnp.int32, (rows, rows), 1)
    same_block = (sub // TREE) == (lane // TREE)
    reach = jnp.where((parent_ref[...] == lane) | (sub == lane), 1.0, 0.0)
    for _ in range(3):
        square = jnp.dot(reach.astype(jnp.bfloat16), reach.astype(jnp.bfloat16),
                         preferred_element_type=jnp.float32)
        reach = jnp.minimum(square, 1.0)
    inclusive = jnp.where(same_block & (sub <= lane), 1.0, 0.0).astype(jnp.bfloat16)
    sel_sub = lax.broadcasted_iota(jnp.int32, (req_count * PATH, rows), 0)
    sel_lane = lax.broadcasted_iota(jnp.int32, (req_count * PATH, rows), 1)
    chosen = jnp.zeros((req_count * PATH, rows), jnp.float32)
    for r in range(req_count):
        target = r * TREE + acc_ref[r]
        chosen = jnp.where((sel_sub // PATH == r) & (sel_lane == target), 1.0, chosen)
    on_path = jnp.dot(chosen.astype(jnp.bfloat16), reach.astype(jnp.bfloat16),
                      preferred_element_type=jnp.float32)
    rank = jnp.dot(on_path.astype(jnp.bfloat16), inclusive, preferred_element_type=jnp.float32)
    slot = (sel_sub % PATH).astype(jnp.float32)
    selector = jnp.where((rank - 1.0 == slot) & (on_path > 0.5), 1.0, 0.0)
    path = jnp.dot(selector.astype(jnp.bfloat16), fresh_ref[...],
                   preferred_element_type=jnp.float32).astype(path_ref.dtype)
    for r in range(req_count):
        path_ref[r] = path[r * PATH : (r + 1) * PATH]

    valid = jnp.concatenate([reach > 0.5] * group, axis=0)
    query = jnp.concatenate([q_ref[:, g * HD : (g + 1) * HD] for g in range(group)], axis=0)
    largest, totals, weighted = attend(query, fresh_ref[:, 0:HD], fresh_ref[:, HD : 2 * HD], valid, False)
    stat_lanes = lax.broadcasted_iota(jnp.int32, (rows, STAT_LANES), 1)
    stats = jnp.zeros((rows, STAT_LANES), jnp.float32)
    for g in range(group):
        part = slice(g * rows, (g + 1) * rows)
        stats = jnp.where(stat_lanes == g, largest[part], stats)
        stats = jnp.where(stat_lanes == group + g, totals[part], stats)
        part_ref[:, g * HD : (g + 1) * HD] = weighted[part]
    part_ref[:, group * HD : group * HD + STAT_LANES] = stats


def tree_partial(accepted, queries, new_kv, parents, group):
    rows, width = queries.shape
    req_count = parents.shape[0]
    row_width = new_kv.shape[1]
    offsets = TREE * jnp.arange(req_count, dtype=jnp.int32)[:, None]
    parent_rows = (parents + offsets).reshape(rows, 1)
    full = lambda shape: pl.BlockSpec(shape, lambda i, a: (0,) * len(shape))
    return pl.pallas_call(
        functools.partial(tree_kernel, group),
        out_shape=(
            jax.ShapeDtypeStruct((rows, width + STAT_LANES), jnp.float32),
            jax.ShapeDtypeStruct((req_count, PATH, row_width), jnp.bfloat16),
        ),
        grid_spec=pltpu.PrefetchScalarGridSpec(
            num_scalar_prefetch=1,
            grid=(1,),
            in_specs=[full((rows, width)), full((rows, row_width)), full((rows, 1))],
            out_specs=(full((rows, width + STAT_LANES)), full((req_count, PATH, row_width))),
        ),
    )(accepted, queries, new_kv, parent_rows)


def local_kernel(group, page_ids, lens_ref, q_ref, kv_ref, tree_ref, *rest):
    pages = rest[: len(page_ids) - 1]
    sum_ref, stat_ref = rest[-2:]
    req_count, page_size = kv_ref.shape[0], kv_ref.shape[1]
    stat_lanes = lax.broadcasted_iota(jnp.int32, (TREE, STAT_LANES), 1)
    for r in range(req_count):
        row0 = r * TREE
        query = stacked_heads(q_ref, row0, group)
        length = lens_ref[r]
        tree_stats = tree_ref[row0 : row0 + TREE, group * HD : group * HD + STAT_LANES]
        blocks = [(
            jnp.concatenate([lane_pick(tree_stats, g) for g in range(group)], axis=0),
            jnp.concatenate([lane_pick(tree_stats, group + g) for g in range(group)], axis=0),
            stacked_heads(tree_ref, row0, group),
        )]
        for page_index, page_ref in zip(page_ids, (kv_ref,) + tuple(pages)):
            positions = lax.broadcasted_iota(jnp.int32, (1, page_size), 1) + page_index * page_size
            blocks.append(attend(query, page_ref[r, :, 0:HD], page_ref[r, :, HD : 2 * HD],
                                 positions < length, False))
        top = blocks[0][0]
        for block in blocks[1:]:
            top = jnp.maximum(top, block[0])
        totals = jnp.zeros_like(top)
        weighted = jnp.zeros(blocks[0][2].shape, jnp.float32)
        for largest, part_totals, part_weighted in blocks:
            factor = jnp.exp(largest - top)
            totals = totals + factor * part_totals
            weighted = weighted + factor * part_weighted
        stats = jnp.zeros((TREE, STAT_LANES), jnp.float32)
        for g in range(group):
            rows = slice(g * TREE, (g + 1) * TREE)
            sum_ref[row0 : row0 + TREE, g * HD : (g + 1) * HD] = weighted[rows]
            stats = jnp.where(stat_lanes == g, top[rows], stats)
            stats = jnp.where(stat_lanes == group + g, totals[rows], stats)
        stat_ref[row0 : row0 + TREE, :] = stats


def local_partial(cache_lens, queries, kv_pool, tree_part, shipped, group):
    req_count, page_count, page_size, row_width = kv_pool.shape
    rows, width = queries.shape
    page_ids = (0,) + tuple(index for index, _ in shipped)
    page_spec = pl.BlockSpec((req_count, page_size, row_width), lambda i, a: (0, 0, 0))
    return pl.pallas_call(
        functools.partial(local_kernel, group, page_ids),
        out_shape=(
            jax.ShapeDtypeStruct((rows, width), jnp.float32),
            jax.ShapeDtypeStruct((rows, STAT_LANES), jnp.float32),
        ),
        grid_spec=pltpu.PrefetchScalarGridSpec(
            num_scalar_prefetch=1,
            grid=(1,),
            in_specs=[
                pl.BlockSpec((rows, width), lambda i, a: (0, 0)),
                pl.BlockSpec((req_count, None, page_size, row_width), lambda i, a: (0, 0, 0, 0)),
                pl.BlockSpec(tree_part.shape, lambda i, a: (0, 0)),
            ] + [page_spec for _ in shipped],
            out_specs=(
                pl.BlockSpec((rows, width), lambda i, a: (0, 0)),
                pl.BlockSpec((rows, STAT_LANES), lambda i, a: (0, 0)),
            ),
        ),
    )(cache_lens, queries, kv_pool, tree_part, *[page for _, page in shipped])


def holder_kernel(page_index, group, q_ref, kv_ref, order_ref, out_ref):
    req_count, page_size = kv_ref.shape[0], kv_ref.shape[1]
    rows = req_count * TREE
    extra = q_ref[rows : rows + EXTRA, :].astype(jnp.float32)
    length_row = extra[0:1, :] * 16.0 + extra[1:2, :]
    positions = (
        lax.broadcasted_iota(jnp.int32, (1, page_size), 1) + page_index * page_size
    ).astype(jnp.float32)
    stat_lanes = lax.broadcasted_iota(jnp.int32, (TREE, STAT_LANES), 1)
    for r in range(req_count):
        row0 = r * TREE
        valid = positions < lane_pick(length_row, r)
        query = stacked_heads(q_ref, row0, group)
        largest, totals, weighted = attend(
            query, kv_ref[r, :, 0:HD], kv_ref[r, :, HD : 2 * HD], valid, True
        )
        total_hi = totals.astype(jnp.bfloat16).astype(jnp.float32)
        total_lo = totals - total_hi
        stats = jnp.zeros((TREE, STAT_LANES), jnp.float32)
        for g in range(group):
            part = slice(g * TREE, (g + 1) * TREE)
            out_ref[row0 : row0 + TREE, g * HD : (g + 1) * HD] = weighted[part].astype(jnp.bfloat16)
            stats = jnp.where(stat_lanes == g, largest[part], stats)
            stats = jnp.where(stat_lanes == group + g, total_hi[part], stats)
            stats = jnp.where(stat_lanes == 2 * group + g, total_lo[part], stats)
        out_ref[row0 : row0 + TREE, group * HD : group * HD + STAT_LANES] = stats.astype(jnp.bfloat16)


def holder_partial(packed_queries, kv_pool, page_index, group, order_after):
    req_count, page_count, page_size, row_width = kv_pool.shape
    packed_rows, width = packed_queries.shape
    rows = req_count * TREE
    return pl.pallas_call(
        functools.partial(holder_kernel, page_index, group),
        out_shape=jax.ShapeDtypeStruct((rows, width + STAT_LANES), jnp.bfloat16),
        grid=(1,),
        in_specs=[
            pl.BlockSpec((packed_rows, width), lambda i: (0, 0)),
            pl.BlockSpec((req_count, None, page_size, row_width), lambda i: (0, page_index, 0, 0)),
            pl.BlockSpec((8, STAT_LANES), lambda i: (0, 0)),
        ],
        out_specs=pl.BlockSpec((rows, width + STAT_LANES), lambda i: (0, 0)),
    )(packed_queries, kv_pool, order_after)


def merge_kernel(group, count, sum_hbm, stat_hbm, *rest):
    returned = rest[:count]
    w_hbm, out_ref, sum_ref, stat_ref, w_ref, att_ref, sems = rest[count:]
    copies = [
        pltpu.make_async_copy(sum_hbm, sum_ref, sems.at[0]),
        pltpu.make_async_copy(stat_hbm, stat_ref, sems.at[1]),
        pltpu.make_async_copy(w_hbm, w_ref, sems.at[2]),
    ]
    for copy in copies:
        copy.start()
    copies[0].wait()
    copies[1].wait()
    rows = sum_ref.shape[0]
    for r in range(rows // TREE):
        row0 = r * TREE
        local_stats = stat_ref[row0 : row0 + TREE, :]
        for g in range(group):
            cols = slice(g * HD, (g + 1) * HD)
            blocks = [(lane_pick(local_stats, g), lane_pick(local_stats, group + g),
                       sum_ref[row0 : row0 + TREE, cols])]
            for part_ref in returned:
                stats = part_ref[row0 : row0 + TREE, group * HD : group * HD + STAT_LANES].astype(jnp.float32)
                totals = lane_pick(stats, group + g) + lane_pick(stats, 2 * group + g)
                blocks.append((lane_pick(stats, g), totals,
                               part_ref[row0 : row0 + TREE, cols].astype(jnp.float32)))
            top = blocks[0][0]
            for block in blocks[1:]:
                top = jnp.maximum(top, block[0])
            denominator = jnp.zeros_like(top)
            numerator = jnp.zeros((TREE, HD), jnp.float32)
            for largest, totals, weighted in blocks:
                factor = jnp.exp(largest - top)
                denominator = denominator + factor * totals
                numerator = numerator + factor * weighted
            att_ref[row0 : row0 + TREE, cols] = (numerator / denominator).astype(jnp.bfloat16)
    copies[2].wait()
    out_ref[...] = jnp.dot(
        att_ref[...], w_ref[...], preferred_element_type=jnp.float32
    ).astype(out_ref.dtype)


def merge_project(sums, stats, returned, w_out, group):
    rows, width = sums.shape
    part_width = returned[0].shape[1]
    model = w_out.shape[1]
    full = lambda shape: pl.BlockSpec(shape, lambda i: (0, 0))
    anywhere = pl.BlockSpec(memory_space=pl.ANY)
    return pl.pallas_call(
        functools.partial(merge_kernel, group, len(returned)),
        out_shape=jax.ShapeDtypeStruct((rows, model), jnp.bfloat16),
        grid=(1,),
        in_specs=[anywhere, anywhere]
        + [full((rows, part_width)) for _ in returned]
        + [anywhere],
        out_specs=full((rows, model)),
        scratch_shapes=[
            pltpu.VMEM(sums.shape, sums.dtype),
            pltpu.VMEM(stats.shape, stats.dtype),
            pltpu.VMEM(w_out.shape, w_out.dtype),
            pltpu.VMEM((rows, width), jnp.bfloat16),
            pltpu.SemaphoreType.DMA((3,)),
        ],
        compiler_params=pltpu.CompilerParams(vmem_limit_bytes=48 * 1024 * 1024),
    )(sums, stats, *returned, w_out)


def chain_reduce_scatter(product, axis):
    count = lax.axis_size(axis)
    me = lax.axis_index(axis)
    chunk = product.shape[0] // count
    pieces = product.reshape(count, chunk, product.shape[1])

    def piece(offset):
        return lax.dynamic_index_in_dim(pieces, (me + offset) % count, 0, keepdims=False)

    forward_hops = count // 2
    backward_hops = count - 1 - forward_hops
    forward = piece(forward_hops)
    backward = piece(-backward_hops) if backward_hops > 0 else None
    for step in range(1, forward_hops + 1):
        forward = shifted(forward, axis, 1)
        if backward is not None and step <= backward_hops:
            backward = shifted(backward, axis, -1)
        if step < forward_hops:
            forward = (forward.astype(jnp.float32)
                       + piece(forward_hops - step).astype(jnp.float32)).astype(jnp.bfloat16)
        if backward is not None and step < backward_hops:
            backward = (backward.astype(jnp.float32)
                        + piece(step - backward_hops).astype(jnp.float32)).astype(jnp.bfloat16)
    total = piece(0).astype(jnp.float32) + forward.astype(jnp.float32)
    if backward is not None:
        total = total + backward.astype(jnp.float32)
    return total


def pack_queries(queries, lengths):
    width = queries.shape[1]
    count = lengths.shape[0]
    pair = jnp.stack([lengths // 16, lengths % 16]).astype(jnp.bfloat16)
    extra = jnp.pad(pair, ((0, EXTRA - 2), (0, width - count)))
    return jnp.concatenate([queries, extra], axis=0)


def per_device(queries, new_kv, kv_pool, cache_lens, parents, accepted, residual, w_out, norm_gain):
    req_count, page_count, page_size, row_width = kv_pool.shape
    kv_local = row_width // (2 * HD)
    q_local = queries.shape[1] // HD
    group = q_local // kv_local

    shipped = [(p, shifted(kv_pool[:, p], "req", -p)) for p in SHIPPED_PAGES]
    visited = [p for p in range(1, page_count) if p not in SHIPPED_PAGES]
    packed_queries = pack_queries(queries, cache_lens)
    guests = [shifted(packed_queries, "req", p) for p in visited]
    tree_part, accepted_kv = tree_partial(accepted, queries, new_kv, parents, group)
    returned = []
    for page_index, guest in zip(visited, guests):
        part = holder_partial(guest, kv_pool, page_index, group, tree_part)
        returned.append(shifted(part, "req", -page_index))
    sums, stats = local_partial(cache_lens, queries, kv_pool, tree_part, shipped, group)

    product = merge_project(sums, stats, returned, w_out, group)
    summed = chain_reduce_scatter(product, "tp")
    hidden_out = (residual.astype(jnp.float32) + summed).astype(jnp.bfloat16)
    widened = hidden_out.astype(jnp.float32)
    normed = (
        widened * lax.rsqrt(jnp.mean(widened * widened, axis=-1, keepdims=True) + 1e-05) * norm_gain
    ).astype(jnp.bfloat16)
    return (hidden_out, normed, accepted_kv)


def solution(mesh):
    placed = (
        P("req", "tp"),
        P("req", "tp"),
        P("req", None, None, "tp"),
        P("req"),
        P("req", None),
        P("req"),
        P(("req", "tp"), None),
        P("tp", None),
        P(),
    )
    return jax.shard_map(
        per_device,
        mesh=mesh,
        in_specs=placed,
        out_specs=(P(("req", "tp"), None), P(("req", "tp"), None), P("req", None, "tp")),
        check_vma=False,
    )
```

```python
import functools

import jax
import jax.numpy as jnp
from jax import lax
from jax.experimental import pallas as pl
from jax.experimental.pallas import tpu as pltpu
from jax.sharding import PartitionSpec as P

HD = 128
TREE = 32
MAXD = 7
PATH = 8
EXTRA = 16
STAT_LANES = 128
SHIPPED_PAGES = (1,)


NEGATIVE = -1e30


def shifted(value, axis, steps):
    count = lax.axis_size(axis)
    pairs = [(source, (source + steps) % count) for source in range(count)]
    return lax.ppermute(value, axis, pairs)


def attend(query, key, value, valid, round_max):
    scores = lax.dot_general(
        query, key, (((1,), (1,)), ((), ())), preferred_element_type=jnp.float32
    ) * (HD ** (-0.5))
    scores = jnp.where(valid, scores, NEGATIVE)
    largest = jnp.max(scores, axis=1, keepdims=True)
    if round_max:
        largest = largest.astype(jnp.bfloat16).astype(jnp.float32)
    weights = jnp.where(valid, jnp.exp(scores - largest), 0.0)
    totals = jnp.sum(weights, axis=1, keepdims=True)
    weighted = jnp.dot(
        weights.astype(jnp.bfloat16), value, preferred_element_type=jnp.float32
    )
    return largest, totals, weighted


def lane_pick(block, lane):
    lanes = lax.broadcasted_iota(jnp.int32, block.shape, 1)
    return jnp.sum(jnp.where(lanes == lane, block, 0.0), axis=1, keepdims=True)


def stacked_heads(rows_ref, row0, group):
    parts = [rows_ref[row0 : row0 + TREE, g * HD : (g + 1) * HD] for g in range(group)]
    return jnp.concatenate(parts, axis=0)


def tree_kernel(group, acc_ref, q_ref, fresh_ref, parent_ref, part_ref, path_ref):
    rows = fresh_ref.shape[0]
    req_count = rows // TREE
    sub = lax.broadcasted_iota(jnp.int32, (rows, rows), 0)
    lane = lax.broadcasted_iota(jnp.int32, (rows, rows), 1)
    same_block = (sub // TREE) == (lane // TREE)
    reach = jnp.where((parent_ref[...] == lane) | (sub == lane), 1.0, 0.0)
    for _ in range(3):
        square = jnp.dot(reach.astype(jnp.bfloat16), reach.astype(jnp.bfloat16),
                         preferred_element_type=jnp.float32)
        reach = jnp.minimum(square, 1.0)
    inclusive = jnp.where(same_block & (sub <= lane), 1.0, 0.0).astype(jnp.bfloat16)
    sel_sub = lax.broadcasted_iota(jnp.int32, (req_count * PATH, rows), 0)
    sel_lane = lax.broadcasted_iota(jnp.int32, (req_count * PATH, rows), 1)
    chosen = jnp.zeros((req_count * PATH, rows), jnp.float32)
    for r in range(req_count):
        target = r * TREE + acc_ref[r]
        chosen = jnp.where((sel_sub // PATH == r) & (sel_lane == target), 1.0, chosen)
    on_path = jnp.dot(chosen.astype(jnp.bfloat16), reach.astype(jnp.bfloat16),
                      preferred_element_type=jnp.float32)
    rank = jnp.dot(on_path.astype(jnp.bfloat16), inclusive, preferred_element_type=jnp.float32)
    slot = (sel_sub % PATH).astype(jnp.float32)
    selector = jnp.where((rank - 1.0 == slot) & (on_path > 0.5), 1.0, 0.0)
    path = jnp.dot(selector.astype(jnp.bfloat16), fresh_ref[...],
                   preferred_element_type=jnp.float32).astype(path_ref.dtype)
    for r in range(req_count):
        path_ref[r] = path[r * PATH : (r + 1) * PATH]

    valid = jnp.concatenate([reach > 0.5] * group, axis=0)
    query = jnp.concatenate([q_ref[:, g * HD : (g + 1) * HD] for g in range(group)], axis=0)
    largest, totals, weighted = attend(query, fresh_ref[:, 0:HD], fresh_ref[:, HD : 2 * HD], valid, False)
    stat_lanes = lax.broadcasted_iota(jnp.int32, (rows, STAT_LANES), 1)
    stats = jnp.zeros((rows, STAT_LANES), jnp.float32)
    for g in range(group):
        part = slice(g * rows, (g + 1) * rows)
        stats = jnp.where(stat_lanes == g, largest[part], stats)
        stats = jnp.where(stat_lanes == group + g, totals[part], stats)
        part_ref[:, g * HD : (g + 1) * HD] = weighted[part]
    part_ref[:, group * HD : group * HD + STAT_LANES] = stats


def tree_partial(accepted, queries, new_kv, parents, group):
    rows, width = queries.shape
    req_count = parents.shape[0]
    row_width = new_kv.shape[1]
    offsets = TREE * jnp.arange(req_count, dtype=jnp.int32)[:, None]
    parent_rows = (parents + offsets).reshape(rows, 1)
    full = lambda shape: pl.BlockSpec(shape, lambda i, a: (0,) * len(shape))
    return pl.pallas_call(
        functools.partial(tree_kernel, group),
        out_shape=(
            jax.ShapeDtypeStruct((rows, width + STAT_LANES), jnp.float32),
            jax.ShapeDtypeStruct((req_count, PATH, row_width), jnp.bfloat16),
        ),
        grid_spec=pltpu.PrefetchScalarGridSpec(
            num_scalar_prefetch=1,
            grid=(1,),
            in_specs=[full((rows, width)), full((rows, row_width)), full((rows, 1))],
            out_specs=(full((rows, width + STAT_LANES)), full((req_count, PATH, row_width))),
        ),
    )(accepted, queries, new_kv, parent_rows)


def local_kernel(group, page_ids, lens_ref, q_ref, kv_ref, tree_ref, *rest):
    pages = rest[: len(page_ids) - 1]
    sum_ref, stat_ref = rest[-2:]
    req_count, page_size = kv_ref.shape[0], kv_ref.shape[1]
    stat_lanes = lax.broadcasted_iota(jnp.int32, (TREE, STAT_LANES), 1)
    for r in range(req_count):
        row0 = r * TREE
        query = stacked_heads(q_ref, row0, group)
        length = lens_ref[r]
        tree_stats = tree_ref[row0 : row0 + TREE, group * HD : group * HD + STAT_LANES]
        blocks = [(
            jnp.concatenate([lane_pick(tree_stats, g) for g in range(group)], axis=0),
            jnp.concatenate([lane_pick(tree_stats, group + g) for g in range(group)], axis=0),
            stacked_heads(tree_ref, row0, group),
        )]
        page_refs = (kv_ref,) + tuple(pages)
        if page_ids == tuple(range(len(page_ids))):
            keys = jnp.concatenate([ref[r, :, 0:HD] for ref in page_refs], axis=0)
            values = jnp.concatenate([ref[r, :, HD : 2 * HD] for ref in page_refs], axis=0)
            positions = lax.broadcasted_iota(jnp.int32, (1, page_size * len(page_refs)), 1)
            blocks.append(attend(query, keys, values, positions < length, False))
        else:
            for page_index, page_ref in zip(page_ids, page_refs):
                positions = lax.broadcasted_iota(jnp.int32, (1, page_size), 1) + page_index * page_size
                blocks.append(attend(query, page_ref[r, :, 0:HD], page_ref[r, :, HD : 2 * HD],
                                     positions < length, False))
        top = blocks[0][0]
        for block in blocks[1:]:
            top = jnp.maximum(top, block[0])
        totals = jnp.zeros_like(top)
        weighted = jnp.zeros(blocks[0][2].shape, jnp.float32)
        for largest, part_totals, part_weighted in blocks:
            factor = jnp.exp(largest - top)
            totals = totals + factor * part_totals
            weighted = weighted + factor * part_weighted
        stats = jnp.zeros((TREE, STAT_LANES), jnp.float32)
        for g in range(group):
            rows = slice(g * TREE, (g + 1) * TREE)
            sum_ref[row0 : row0 + TREE, g * HD : (g + 1) * HD] = weighted[rows]
            stats = jnp.where(stat_lanes == g, top[rows], stats)
            stats = jnp.where(stat_lanes == group + g, totals[rows], stats)
        stat_ref[row0 : row0 + TREE, :] = stats


def local_partial(cache_lens, queries, kv_pool, tree_part, shipped, group):
    req_count, page_count, page_size, row_width = kv_pool.shape
    rows, width = queries.shape
    page_ids = (0,) + tuple(index for index, _ in shipped)
    page_spec = pl.BlockSpec((req_count, page_size, row_width), lambda i, a: (0, 0, 0))
    return pl.pallas_call(
        functools.partial(local_kernel, group, page_ids),
        out_shape=(
            jax.ShapeDtypeStruct((rows, width), jnp.float32),
            jax.ShapeDtypeStruct((rows, STAT_LANES), jnp.float32),
        ),
        grid_spec=pltpu.PrefetchScalarGridSpec(
            num_scalar_prefetch=1,
            grid=(1,),
            in_specs=[
                pl.BlockSpec((rows, width), lambda i, a: (0, 0)),
                pl.BlockSpec((req_count, None, page_size, row_width), lambda i, a: (0, 0, 0, 0)),
                pl.BlockSpec(tree_part.shape, lambda i, a: (0, 0)),
            ] + [page_spec for _ in shipped],
            out_specs=(
                pl.BlockSpec((rows, width), lambda i, a: (0, 0)),
                pl.BlockSpec((rows, STAT_LANES), lambda i, a: (0, 0)),
            ),
        ),
    )(cache_lens, queries, kv_pool, tree_part, *[page for _, page in shipped])


def holder_kernel(page_index, group, q_ref, kv_ref, order_ref, out_ref):
    req_count, page_size = kv_ref.shape[0], kv_ref.shape[1]
    rows = req_count * TREE
    extra = q_ref[rows : rows + EXTRA, :].astype(jnp.float32)
    length_row = extra[0:1, :] * 16.0 + extra[1:2, :]
    positions = (
        lax.broadcasted_iota(jnp.int32, (1, page_size), 1) + page_index * page_size
    ).astype(jnp.float32)
    stat_lanes = lax.broadcasted_iota(jnp.int32, (TREE, STAT_LANES), 1)
    for r in range(req_count):
        row0 = r * TREE
        valid = positions < lane_pick(length_row, r)
        query = stacked_heads(q_ref, row0, group)
        largest, totals, weighted = attend(
            query, kv_ref[r, :, 0:HD], kv_ref[r, :, HD : 2 * HD], valid, True
        )
        total_hi = totals.astype(jnp.bfloat16).astype(jnp.float32)
        total_lo = totals - total_hi
        stats = jnp.zeros((TREE, STAT_LANES), jnp.float32)
        for g in range(group):
            part = slice(g * TREE, (g + 1) * TREE)
            out_ref[row0 : row0 + TREE, g * HD : (g + 1) * HD] = weighted[part].astype(jnp.bfloat16)
            stats = jnp.where(stat_lanes == g, largest[part], stats)
            stats = jnp.where(stat_lanes == group + g, total_hi[part], stats)
            stats = jnp.where(stat_lanes == 2 * group + g, total_lo[part], stats)
        out_ref[row0 : row0 + TREE, group * HD : group * HD + STAT_LANES] = stats.astype(jnp.bfloat16)


def holder_partial(packed_queries, kv_pool, page_index, group, order_after):
    req_count, page_count, page_size, row_width = kv_pool.shape
    packed_rows, width = packed_queries.shape
    rows = req_count * TREE
    return pl.pallas_call(
        functools.partial(holder_kernel, page_index, group),
        out_shape=jax.ShapeDtypeStruct((rows, width + STAT_LANES), jnp.bfloat16),
        grid=(1,),
        in_specs=[
            pl.BlockSpec((packed_rows, width), lambda i: (0, 0)),
            pl.BlockSpec((req_count, None, page_size, row_width), lambda i: (0, page_index, 0, 0)),
            pl.BlockSpec((8, STAT_LANES), lambda i: (0, 0)),
        ],
        out_specs=pl.BlockSpec((rows, width + STAT_LANES), lambda i: (0, 0)),
    )(packed_queries, kv_pool, order_after)


def merge_kernel(group, count, sum_hbm, stat_hbm, *rest):
    returned = rest[:count]
    w_hbm, out_ref, sum_ref, stat_ref, w_ref, att_ref, sems = rest[count:]
    copies = [
        pltpu.make_async_copy(sum_hbm, sum_ref, sems.at[0]),
        pltpu.make_async_copy(stat_hbm, stat_ref, sems.at[1]),
        pltpu.make_async_copy(w_hbm, w_ref, sems.at[2]),
    ]
    for copy in copies:
        copy.start()
    copies[0].wait()
    copies[1].wait()
    rows = sum_ref.shape[0]
    for r in range(rows // TREE):
        row0 = r * TREE
        local_stats = stat_ref[row0 : row0 + TREE, :]
        for g in range(group):
            cols = slice(g * HD, (g + 1) * HD)
            blocks = [(lane_pick(local_stats, g), lane_pick(local_stats, group + g),
                       sum_ref[row0 : row0 + TREE, cols])]
            for part_ref in returned:
                stats = part_ref[row0 : row0 + TREE, group * HD : group * HD + STAT_LANES].astype(jnp.float32)
                totals = lane_pick(stats, group + g) + lane_pick(stats, 2 * group + g)
                blocks.append((lane_pick(stats, g), totals,
                               part_ref[row0 : row0 + TREE, cols].astype(jnp.float32)))
            top = blocks[0][0]
            for block in blocks[1:]:
                top = jnp.maximum(top, block[0])
            denominator = jnp.zeros_like(top)
            numerator = jnp.zeros((TREE, HD), jnp.float32)
            for largest, totals, weighted in blocks:
                factor = jnp.exp(largest - top)
                denominator = denominator + factor * totals
                numerator = numerator + factor * weighted
            att_ref[row0 : row0 + TREE, cols] = (numerator / denominator).astype(jnp.bfloat16)
    copies[2].wait()
    out_ref[...] = jnp.dot(
        att_ref[...], w_ref[...], preferred_element_type=jnp.float32
    ).astype(out_ref.dtype)


def merge_project(sums, stats, returned, w_out, group):
    rows, width = sums.shape
    part_width = returned[0].shape[1]
    model = w_out.shape[1]
    full = lambda shape: pl.BlockSpec(shape, lambda i: (0, 0))
    anywhere = pl.BlockSpec(memory_space=pl.ANY)
    return pl.pallas_call(
        functools.partial(merge_kernel, group, len(returned)),
        out_shape=jax.ShapeDtypeStruct((rows, model), jnp.bfloat16),
        grid=(1,),
        in_specs=[anywhere, anywhere]
        + [full((rows, part_width)) for _ in returned]
        + [anywhere],
        out_specs=full((rows, model)),
        scratch_shapes=[
            pltpu.VMEM(sums.shape, sums.dtype),
            pltpu.VMEM(stats.shape, stats.dtype),
            pltpu.VMEM(w_out.shape, w_out.dtype),
            pltpu.VMEM((rows, width), jnp.bfloat16),
            pltpu.SemaphoreType.DMA((3,)),
        ],
        compiler_params=pltpu.CompilerParams(vmem_limit_bytes=48 * 1024 * 1024),
    )(sums, stats, *returned, w_out)


def chain_reduce_scatter(product, axis):
    count = lax.axis_size(axis)
    me = lax.axis_index(axis)
    chunk = product.shape[0] // count
    pieces = product.reshape(count, chunk, product.shape[1])

    def piece(offset):
        return lax.dynamic_index_in_dim(pieces, (me + offset) % count, 0, keepdims=False)

    forward_hops = count // 2
    backward_hops = count - 1 - forward_hops
    forward = piece(forward_hops)
    backward = piece(-backward_hops) if backward_hops > 0 else None
    for step in range(1, forward_hops + 1):
        forward = shifted(forward, axis, 1)
        if backward is not None and step <= backward_hops:
            backward = shifted(backward, axis, -1)
        if step < forward_hops:
            forward = (forward.astype(jnp.float32)
                       + piece(forward_hops - step).astype(jnp.float32)).astype(jnp.bfloat16)
        if backward is not None and step < backward_hops:
            backward = (backward.astype(jnp.float32)
                        + piece(step - backward_hops).astype(jnp.float32)).astype(jnp.bfloat16)
    total = piece(0).astype(jnp.float32) + forward.astype(jnp.float32)
    if backward is not None:
        total = total + backward.astype(jnp.float32)
    return total


def pack_queries(queries, lengths):
    width = queries.shape[1]
    count = lengths.shape[0]
    pair = jnp.stack([lengths // 16, lengths % 16]).astype(jnp.bfloat16)
    extra = jnp.pad(pair, ((0, EXTRA - 2), (0, width - count)))
    return jnp.concatenate([queries, extra], axis=0)


def per_device(queries, new_kv, kv_pool, cache_lens, parents, accepted, residual, w_out, norm_gain):
    req_count, page_count, page_size, row_width = kv_pool.shape
    kv_local = row_width // (2 * HD)
    q_local = queries.shape[1] // HD
    group = q_local // kv_local

    shipped = [(p, shifted(kv_pool[:, p], "req", -p)) for p in SHIPPED_PAGES]
    visited = [p for p in range(1, page_count) if p not in SHIPPED_PAGES]
    packed_queries = pack_queries(queries, cache_lens)
    guests = [shifted(packed_queries, "req", p) for p in visited]
    tree_part, accepted_kv = tree_partial(accepted, queries, new_kv, parents, group)
    returned = []
    for page_index, guest in zip(visited, guests):
        part = holder_partial(guest, kv_pool, page_index, group, tree_part)
        returned.append(shifted(part, "req", -page_index))
    sums, stats = local_partial(cache_lens, queries, kv_pool, tree_part, shipped, group)

    product = merge_project(sums, stats, returned, w_out, group)
    summed = chain_reduce_scatter(product, "tp")
    hidden_out = (residual.astype(jnp.float32) + summed).astype(jnp.bfloat16)
    widened = hidden_out.astype(jnp.float32)
    normed = (
        widened * lax.rsqrt(jnp.mean(widened * widened, axis=-1, keepdims=True) + 1e-05) * norm_gain
    ).astype(jnp.bfloat16)
    return (hidden_out, normed, accepted_kv)


def solution(mesh):
    placed = (
        P("req", "tp"),
        P("req", "tp"),
        P("req", None, None, "tp"),
        P("req"),
        P("req", None),
        P("req"),
        P(("req", "tp"), None),
        P("tp", None),
        P(),
    )
    return jax.shard_map(
        per_device,
        mesh=mesh,
        in_specs=placed,
        out_specs=(P(("req", "tp"), None), P(("req", "tp"), None), P("req", None, "tp")),
        check_vma=False,
    )
```

```python
import functools

import jax
import jax.numpy as jnp
from jax import lax
from jax.experimental import pallas as pl
from jax.experimental.pallas import tpu as pltpu
from jax.sharding import PartitionSpec as P

HD = 128
TREE = 32
MAXD = 7
PATH = 8
EXTRA = 16
STAT_LANES = 128
SHIPPED_PAGES = (1,)


NEGATIVE = -1e30


def shifted(value, axis, steps):
    count = lax.axis_size(axis)
    pairs = [(source, (source + steps) % count) for source in range(count)]
    return lax.ppermute(value, axis, pairs)


def attend(query, key, value, valid, round_max):
    scores = lax.dot_general(
        query, key, (((1,), (1,)), ((), ())), preferred_element_type=jnp.float32
    ) * (HD ** (-0.5))
    scores = jnp.where(valid, scores, NEGATIVE)
    largest = jnp.max(scores, axis=1, keepdims=True)
    if round_max:
        largest = largest.astype(jnp.bfloat16).astype(jnp.float32)
    weights = jnp.where(valid, jnp.exp(scores - largest), 0.0)
    totals = jnp.sum(weights, axis=1, keepdims=True)
    weighted = jnp.dot(
        weights.astype(jnp.bfloat16), value, preferred_element_type=jnp.float32
    )
    return largest, totals, weighted


def lane_pick(block, lane):
    lanes = lax.broadcasted_iota(jnp.int32, block.shape, 1)
    return jnp.sum(jnp.where(lanes == lane, block, 0.0), axis=1, keepdims=True)


def stacked_heads(rows_ref, row0, group):
    parts = [rows_ref[row0 : row0 + TREE, g * HD : (g + 1) * HD] for g in range(group)]
    return jnp.concatenate(parts, axis=0)


def tree_kernel(group, acc_ref, q_ref, fresh_ref, parent_ref, part_ref, path_ref):
    rows = fresh_ref.shape[0]
    req_count = rows // TREE
    sub = lax.broadcasted_iota(jnp.int32, (rows, rows), 0)
    lane = lax.broadcasted_iota(jnp.int32, (rows, rows), 1)
    same_block = (sub // TREE) == (lane // TREE)
    reach = jnp.where((parent_ref[...] == lane) | (sub == lane), 1.0, 0.0)
    for _ in range(3):
        square = jnp.dot(reach.astype(jnp.bfloat16), reach.astype(jnp.bfloat16),
                         preferred_element_type=jnp.float32)
        reach = jnp.minimum(square, 1.0)
    inclusive = jnp.where(same_block & (sub <= lane), 1.0, 0.0).astype(jnp.bfloat16)
    sel_sub = lax.broadcasted_iota(jnp.int32, (req_count * PATH, rows), 0)
    sel_lane = lax.broadcasted_iota(jnp.int32, (req_count * PATH, rows), 1)
    chosen = jnp.zeros((req_count * PATH, rows), jnp.float32)
    for r in range(req_count):
        target = r * TREE + acc_ref[r]
        chosen = jnp.where((sel_sub // PATH == r) & (sel_lane == target), 1.0, chosen)
    on_path = jnp.dot(chosen.astype(jnp.bfloat16), reach.astype(jnp.bfloat16),
                      preferred_element_type=jnp.float32)
    rank = jnp.dot(on_path.astype(jnp.bfloat16), inclusive, preferred_element_type=jnp.float32)
    slot = (sel_sub % PATH).astype(jnp.float32)
    selector = jnp.where((rank - 1.0 == slot) & (on_path > 0.5), 1.0, 0.0)
    path = jnp.dot(selector.astype(jnp.bfloat16), fresh_ref[...],
                   preferred_element_type=jnp.float32).astype(path_ref.dtype)
    for r in range(req_count):
        path_ref[r] = path[r * PATH : (r + 1) * PATH]

    valid = jnp.concatenate([reach > 0.5] * group, axis=0)
    query = jnp.concatenate([q_ref[:, g * HD : (g + 1) * HD] for g in range(group)], axis=0)
    largest, totals, weighted = attend(query, fresh_ref[:, 0:HD], fresh_ref[:, HD : 2 * HD], valid, False)
    stat_lanes = lax.broadcasted_iota(jnp.int32, (rows, STAT_LANES), 1)
    stats = jnp.zeros((rows, STAT_LANES), jnp.float32)
    for g in range(group):
        part = slice(g * rows, (g + 1) * rows)
        stats = jnp.where(stat_lanes == g, largest[part], stats)
        stats = jnp.where(stat_lanes == group + g, totals[part], stats)
        part_ref[:, g * HD : (g + 1) * HD] = weighted[part]
    part_ref[:, group * HD : group * HD + STAT_LANES] = stats


def tree_partial(accepted, queries, new_kv, parents, group):
    rows, width = queries.shape
    req_count = parents.shape[0]
    row_width = new_kv.shape[1]
    offsets = TREE * jnp.arange(req_count, dtype=jnp.int32)[:, None]
    parent_rows = (parents + offsets).reshape(rows, 1)
    full = lambda shape: pl.BlockSpec(shape, lambda i, a: (0,) * len(shape))
    return pl.pallas_call(
        functools.partial(tree_kernel, group),
        out_shape=(
            jax.ShapeDtypeStruct((rows, width + STAT_LANES), jnp.float32),
            jax.ShapeDtypeStruct((req_count, PATH, row_width), jnp.bfloat16),
        ),
        grid_spec=pltpu.PrefetchScalarGridSpec(
            num_scalar_prefetch=1,
            grid=(1,),
            in_specs=[full((rows, width)), full((rows, row_width)), full((rows, 1))],
            out_specs=(full((rows, width + STAT_LANES)), full((req_count, PATH, row_width))),
        ),
    )(accepted, queries, new_kv, parent_rows)


def local_kernel(group, page_ids, lens_ref, q_ref, kv_ref, tree_ref, *rest):
    pages = rest[: len(page_ids) - 1]
    sum_ref, stat_ref = rest[-2:]
    req_count, page_size = kv_ref.shape[0], kv_ref.shape[1]
    stat_lanes = lax.broadcasted_iota(jnp.int32, (TREE, STAT_LANES), 1)
    for r in range(req_count):
        row0 = r * TREE
        query = stacked_heads(q_ref, row0, group)
        length = lens_ref[r]
        tree_stats = tree_ref[row0 : row0 + TREE, group * HD : group * HD + STAT_LANES]
        blocks = [(
            jnp.concatenate([lane_pick(tree_stats, g) for g in range(group)], axis=0),
            jnp.concatenate([lane_pick(tree_stats, group + g) for g in range(group)], axis=0),
            stacked_heads(tree_ref, row0, group),
        )]
        page_refs = (kv_ref,) + tuple(pages)
        if page_ids == tuple(range(len(page_ids))):
            keys = jnp.concatenate([ref[r, :, 0:HD] for ref in page_refs], axis=0)
            values = jnp.concatenate([ref[r, :, HD : 2 * HD] for ref in page_refs], axis=0)
            positions = lax.broadcasted_iota(jnp.int32, (1, page_size * len(page_refs)), 1)
            blocks.append(attend(query, keys, values, positions < length, False))
        else:
            for page_index, page_ref in zip(page_ids, page_refs):
                positions = lax.broadcasted_iota(jnp.int32, (1, page_size), 1) + page_index * page_size
                blocks.append(attend(query, page_ref[r, :, 0:HD], page_ref[r, :, HD : 2 * HD],
                                     positions < length, False))
        top = blocks[0][0]
        for block in blocks[1:]:
            top = jnp.maximum(top, block[0])
        totals = jnp.zeros_like(top)
        weighted = jnp.zeros(blocks[0][2].shape, jnp.float32)
        for largest, part_totals, part_weighted in blocks:
            factor = jnp.exp(largest - top)
            totals = totals + factor * part_totals
            weighted = weighted + factor * part_weighted
        stats = jnp.zeros((TREE, STAT_LANES), jnp.float32)
        for g in range(group):
            rows = slice(g * TREE, (g + 1) * TREE)
            sum_ref[row0 : row0 + TREE, g * HD : (g + 1) * HD] = weighted[rows]
            stats = jnp.where(stat_lanes == g, top[rows], stats)
            stats = jnp.where(stat_lanes == group + g, totals[rows], stats)
        stat_ref[row0 : row0 + TREE, :] = stats


def local_partial(cache_lens, queries, kv_pool, tree_part, shipped, group):
    req_count, page_count, page_size, row_width = kv_pool.shape
    rows, width = queries.shape
    page_ids = (0,) + tuple(index for index, _ in shipped)
    page_spec = pl.BlockSpec((req_count, page_size, row_width), lambda i, a: (0, 0, 0))
    return pl.pallas_call(
        functools.partial(local_kernel, group, page_ids),
        out_shape=(
            jax.ShapeDtypeStruct((rows, width), jnp.float32),
            jax.ShapeDtypeStruct((rows, STAT_LANES), jnp.float32),
        ),
        grid_spec=pltpu.PrefetchScalarGridSpec(
            num_scalar_prefetch=1,
            grid=(1,),
            in_specs=[
                pl.BlockSpec((rows, width), lambda i, a: (0, 0)),
                pl.BlockSpec((req_count, None, page_size, row_width), lambda i, a: (0, 0, 0, 0)),
                pl.BlockSpec(tree_part.shape, lambda i, a: (0, 0)),
            ] + [page_spec for _ in shipped],
            out_specs=(
                pl.BlockSpec((rows, width), lambda i, a: (0, 0)),
                pl.BlockSpec((rows, STAT_LANES), lambda i, a: (0, 0)),
            ),
        ),
    )(cache_lens, queries, kv_pool, tree_part, *[page for _, page in shipped])


def holder_kernel(page_index, group, q_ref, kv_ref, order_ref, out_ref):
    req_count, page_size = kv_ref.shape[0], kv_ref.shape[1]
    rows = req_count * TREE
    extra = q_ref[rows : rows + EXTRA, :].astype(jnp.float32)
    length_row = extra[0:1, :] * 16.0 + extra[1:2, :]
    pair = 2 if req_count % 2 == 0 else 1
    q_rows = pair * group * TREE
    sub = lax.broadcasted_iota(jnp.int32, (q_rows, pair * page_size), 0)
    lane = lax.broadcasted_iota(jnp.int32, (q_rows, pair * page_size), 1)
    same_request = (sub // (group * TREE)) == (lane // page_size)
    positions = ((lane % page_size) + page_index * page_size).astype(jnp.float32)
    row_owner = lax.broadcasted_iota(jnp.int32, (q_rows, 1), 0) // (group * TREE)
    stat_lanes = lax.broadcasted_iota(jnp.int32, (TREE, STAT_LANES), 1)
    for r0 in range(0, req_count, pair):
        members = list(range(r0, r0 + pair))
        length = jnp.zeros((q_rows, 1), jnp.float32)
        for k, r in enumerate(members):
            length = jnp.where(row_owner == k, lane_pick(length_row, r), length)
        valid = same_request & (positions < length)
        query = jnp.concatenate([stacked_heads(q_ref, r * TREE, group) for r in members], axis=0)
        key = jnp.concatenate([kv_ref[r, :, 0:HD] for r in members], axis=0)
        value = jnp.concatenate([kv_ref[r, :, HD : 2 * HD] for r in members], axis=0)
        largest, totals, weighted = attend(query, key, value, valid, True)
        total_hi = totals.astype(jnp.bfloat16).astype(jnp.float32)
        total_lo = totals - total_hi
        for k, r in enumerate(members):
            row0 = r * TREE
            stats = jnp.zeros((TREE, STAT_LANES), jnp.float32)
            for g in range(group):
                part = slice((k * group + g) * TREE, (k * group + g + 1) * TREE)
                out_ref[row0 : row0 + TREE, g * HD : (g + 1) * HD] = weighted[part].astype(jnp.bfloat16)
                stats = jnp.where(stat_lanes == g, largest[part], stats)
                stats = jnp.where(stat_lanes == group + g, total_hi[part], stats)
                stats = jnp.where(stat_lanes == 2 * group + g, total_lo[part], stats)
            out_ref[row0 : row0 + TREE, group * HD : group * HD + STAT_LANES] = stats.astype(jnp.bfloat16)


def holder_partial(packed_queries, kv_pool, page_index, group, order_after):
    req_count, page_count, page_size, row_width = kv_pool.shape
    packed_rows, width = packed_queries.shape
    rows = req_count * TREE
    return pl.pallas_call(
        functools.partial(holder_kernel, page_index, group),
        out_shape=jax.ShapeDtypeStruct((rows, width + STAT_LANES), jnp.bfloat16),
        grid=(1,),
        in_specs=[
            pl.BlockSpec((packed_rows, width), lambda i: (0, 0)),
            pl.BlockSpec((req_count, None, page_size, row_width), lambda i: (0, page_index, 0, 0)),
            pl.BlockSpec((8, STAT_LANES), lambda i: (0, 0)),
        ],
        out_specs=pl.BlockSpec((rows, width + STAT_LANES), lambda i: (0, 0)),
    )(packed_queries, kv_pool, order_after)


def merge_kernel(group, count, sum_hbm, stat_hbm, *rest):
    returned = rest[:count]
    w_hbm, out_ref, sum_ref, stat_ref, w_ref, att_ref, sems = rest[count:]
    copies = [
        pltpu.make_async_copy(sum_hbm, sum_ref, sems.at[0]),
        pltpu.make_async_copy(stat_hbm, stat_ref, sems.at[1]),
        pltpu.make_async_copy(w_hbm, w_ref, sems.at[2]),
    ]
    for copy in copies:
        copy.start()
    copies[0].wait()
    copies[1].wait()
    rows = sum_ref.shape[0]
    for r in range(rows // TREE):
        row0 = r * TREE
        local_stats = stat_ref[row0 : row0 + TREE, :]
        for g in range(group):
            cols = slice(g * HD, (g + 1) * HD)
            blocks = [(lane_pick(local_stats, g), lane_pick(local_stats, group + g),
                       sum_ref[row0 : row0 + TREE, cols])]
            for part_ref in returned:
                stats = part_ref[row0 : row0 + TREE, group * HD : group * HD + STAT_LANES].astype(jnp.float32)
                totals = lane_pick(stats, group + g) + lane_pick(stats, 2 * group + g)
                blocks.append((lane_pick(stats, g), totals,
                               part_ref[row0 : row0 + TREE, cols].astype(jnp.float32)))
            top = blocks[0][0]
            for block in blocks[1:]:
                top = jnp.maximum(top, block[0])
            denominator = jnp.zeros_like(top)
            numerator = jnp.zeros((TREE, HD), jnp.float32)
            for largest, totals, weighted in blocks:
                factor = jnp.exp(largest - top)
                denominator = denominator + factor * totals
                numerator = numerator + factor * weighted
            att_ref[row0 : row0 + TREE, cols] = (numerator / denominator).astype(jnp.bfloat16)
    copies[2].wait()
    out_ref[...] = jnp.dot(
        att_ref[...], w_ref[...], preferred_element_type=jnp.float32
    ).astype(out_ref.dtype)


def merge_project(sums, stats, returned, w_out, group):
    rows, width = sums.shape
    part_width = returned[0].shape[1]
    model = w_out.shape[1]
    full = lambda shape: pl.BlockSpec(shape, lambda i: (0, 0))
    anywhere = pl.BlockSpec(memory_space=pl.ANY)
    return pl.pallas_call(
        functools.partial(merge_kernel, group, len(returned)),
        out_shape=jax.ShapeDtypeStruct((rows, model), jnp.bfloat16),
        grid=(1,),
        in_specs=[anywhere, anywhere]
        + [full((rows, part_width)) for _ in returned]
        + [anywhere],
        out_specs=full((rows, model)),
        scratch_shapes=[
            pltpu.VMEM(sums.shape, sums.dtype),
            pltpu.VMEM(stats.shape, stats.dtype),
            pltpu.VMEM(w_out.shape, w_out.dtype),
            pltpu.VMEM((rows, width), jnp.bfloat16),
            pltpu.SemaphoreType.DMA((3,)),
        ],
        compiler_params=pltpu.CompilerParams(vmem_limit_bytes=48 * 1024 * 1024),
    )(sums, stats, *returned, w_out)


def chain_reduce_scatter(product, axis):
    count = lax.axis_size(axis)
    me = lax.axis_index(axis)
    chunk = product.shape[0] // count
    pieces = product.reshape(count, chunk, product.shape[1])

    def piece(offset):
        return lax.dynamic_index_in_dim(pieces, (me + offset) % count, 0, keepdims=False)

    forward_hops = count // 2
    backward_hops = count - 1 - forward_hops
    forward = piece(forward_hops)
    backward = piece(-backward_hops) if backward_hops > 0 else None
    for step in range(1, forward_hops + 1):
        forward = shifted(forward, axis, 1)
        if backward is not None and step <= backward_hops:
            backward = shifted(backward, axis, -1)
        if step < forward_hops:
            forward = (forward.astype(jnp.float32)
                       + piece(forward_hops - step).astype(jnp.float32)).astype(jnp.bfloat16)
        if backward is not None and step < backward_hops:
            backward = (backward.astype(jnp.float32)
                        + piece(step - backward_hops).astype(jnp.float32)).astype(jnp.bfloat16)
    total = piece(0).astype(jnp.float32) + forward.astype(jnp.float32)
    if backward is not None:
        total = total + backward.astype(jnp.float32)
    return total


def pack_queries(queries, lengths):
    width = queries.shape[1]
    count = lengths.shape[0]
    pair = jnp.stack([lengths // 16, lengths % 16]).astype(jnp.bfloat16)
    extra = jnp.pad(pair, ((0, EXTRA - 2), (0, width - count)))
    return jnp.concatenate([queries, extra], axis=0)


def per_device(queries, new_kv, kv_pool, cache_lens, parents, accepted, residual, w_out, norm_gain):
    req_count, page_count, page_size, row_width = kv_pool.shape
    kv_local = row_width // (2 * HD)
    q_local = queries.shape[1] // HD
    group = q_local // kv_local

    shipped = [(p, shifted(kv_pool[:, p], "req", -p)) for p in SHIPPED_PAGES]
    visited = [p for p in range(1, page_count) if p not in SHIPPED_PAGES]
    packed_queries = pack_queries(queries, cache_lens)
    guests = [shifted(packed_queries, "req", p) for p in visited]
    tree_part, accepted_kv = tree_partial(accepted, queries, new_kv, parents, group)
    returned = []
    for page_index, guest in zip(visited, guests):
        part = holder_partial(guest, kv_pool, page_index, group, tree_part)
        returned.append(shifted(part, "req", -page_index))
    sums, stats = local_partial(cache_lens, queries, kv_pool, tree_part, shipped, group)

    product = merge_project(sums, stats, returned, w_out, group)
    summed = chain_reduce_scatter(product, "tp")
    hidden_out = (residual.astype(jnp.float32) + summed).astype(jnp.bfloat16)
    widened = hidden_out.astype(jnp.float32)
    normed = (
        widened * lax.rsqrt(jnp.mean(widened * widened, axis=-1, keepdims=True) + 1e-05) * norm_gain
    ).astype(jnp.bfloat16)
    return (hidden_out, normed, accepted_kv)


def solution(mesh):
    placed = (
        P("req", "tp"),
        P("req", "tp"),
        P("req", None, None, "tp"),
        P("req"),
        P("req", None),
        P("req"),
        P(("req", "tp"), None),
        P("tp", None),
        P(),
    )
    return jax.shard_map(
        per_device,
        mesh=mesh,
        in_specs=placed,
        out_specs=(P(("req", "tp"), None), P(("req", "tp"), None), P("req", None, "tp")),
        check_vma=False,
    )
```

```python
import functools

import jax
import jax.numpy as jnp
from jax import lax
from jax.experimental import pallas as pl
from jax.experimental.pallas import tpu as pltpu
from jax.sharding import PartitionSpec as P

HD = 128
TREE = 32
MAXD = 7
PATH = 8
EXTRA = 16
STAT_LANES = 128
SHIPPED_PAGES = (1,)


NEGATIVE = -1e30


def shifted(value, axis, steps):
    count = lax.axis_size(axis)
    pairs = [(source, (source + steps) % count) for source in range(count)]
    return lax.ppermute(value, axis, pairs)


def attend(query, key, value, valid, round_max):
    scores = lax.dot_general(
        query, key, (((1,), (1,)), ((), ())), preferred_element_type=jnp.float32
    ) * (HD ** (-0.5))
    scores = jnp.where(valid, scores, NEGATIVE)
    largest = jnp.max(scores, axis=1, keepdims=True)
    if round_max:
        largest = largest.astype(jnp.bfloat16).astype(jnp.float32)
    weights = jnp.where(valid, jnp.exp(scores - largest), 0.0)
    totals = jnp.sum(weights, axis=1, keepdims=True)
    weighted = jnp.dot(
        weights.astype(jnp.bfloat16), value, preferred_element_type=jnp.float32
    )
    return largest, totals, weighted


def lane_pick(block, lane):
    lanes = lax.broadcasted_iota(jnp.int32, block.shape, 1)
    return jnp.sum(jnp.where(lanes == lane, block, 0.0), axis=1, keepdims=True)


def stacked_heads(rows_ref, row0, group):
    parts = [rows_ref[row0 : row0 + TREE, g * HD : (g + 1) * HD] for g in range(group)]
    return jnp.concatenate(parts, axis=0)


def tree_kernel(group, acc_ref, q_ref, fresh_ref, parent_ref, part_ref, path_ref):
    rows = fresh_ref.shape[0]
    req_count = rows // TREE
    sub = lax.broadcasted_iota(jnp.int32, (rows, rows), 0)
    lane = lax.broadcasted_iota(jnp.int32, (rows, rows), 1)
    same_block = (sub // TREE) == (lane // TREE)
    reach = jnp.where((parent_ref[...] == lane) | (sub == lane), 1.0, 0.0)
    for _ in range(3):
        square = jnp.dot(reach.astype(jnp.bfloat16), reach.astype(jnp.bfloat16),
                         preferred_element_type=jnp.float32)
        reach = jnp.minimum(square, 1.0)
    inclusive = jnp.where(same_block & (sub <= lane), 1.0, 0.0).astype(jnp.bfloat16)
    sel_sub = lax.broadcasted_iota(jnp.int32, (req_count * PATH, rows), 0)
    sel_lane = lax.broadcasted_iota(jnp.int32, (req_count * PATH, rows), 1)
    chosen = jnp.zeros((req_count * PATH, rows), jnp.float32)
    for r in range(req_count):
        target = r * TREE + acc_ref[r]
        chosen = jnp.where((sel_sub // PATH == r) & (sel_lane == target), 1.0, chosen)
    on_path = jnp.dot(chosen.astype(jnp.bfloat16), reach.astype(jnp.bfloat16),
                      preferred_element_type=jnp.float32)
    rank = jnp.dot(on_path.astype(jnp.bfloat16), inclusive, preferred_element_type=jnp.float32)
    slot = (sel_sub % PATH).astype(jnp.float32)
    selector = jnp.where((rank - 1.0 == slot) & (on_path > 0.5), 1.0, 0.0)
    path = jnp.dot(selector.astype(jnp.bfloat16), fresh_ref[...],
                   preferred_element_type=jnp.float32).astype(path_ref.dtype)
    for r in range(req_count):
        path_ref[r] = path[r * PATH : (r + 1) * PATH]

    valid = jnp.concatenate([reach > 0.5] * group, axis=0)
    query = jnp.concatenate([q_ref[:, g * HD : (g + 1) * HD] for g in range(group)], axis=0)
    largest, totals, weighted = attend(query, fresh_ref[:, 0:HD], fresh_ref[:, HD : 2 * HD], valid, False)
    stat_lanes = lax.broadcasted_iota(jnp.int32, (rows, STAT_LANES), 1)
    stats = jnp.zeros((rows, STAT_LANES), jnp.float32)
    for g in range(group):
        part = slice(g * rows, (g + 1) * rows)
        stats = jnp.where(stat_lanes == g, largest[part], stats)
        stats = jnp.where(stat_lanes == group + g, totals[part], stats)
        part_ref[:, g * HD : (g + 1) * HD] = weighted[part]
    part_ref[:, group * HD : group * HD + STAT_LANES] = stats


def tree_partial(accepted, queries, new_kv, parents, group):
    rows, width = queries.shape
    req_count = parents.shape[0]
    row_width = new_kv.shape[1]
    offsets = TREE * jnp.arange(req_count, dtype=jnp.int32)[:, None]
    parent_rows = (parents + offsets).reshape(rows, 1)
    full = lambda shape: pl.BlockSpec(shape, lambda i, a: (0,) * len(shape))
    return pl.pallas_call(
        functools.partial(tree_kernel, group),
        out_shape=(
            jax.ShapeDtypeStruct((rows, width + STAT_LANES), jnp.float32),
            jax.ShapeDtypeStruct((req_count, PATH, row_width), jnp.bfloat16),
        ),
        grid_spec=pltpu.PrefetchScalarGridSpec(
            num_scalar_prefetch=1,
            grid=(1,),
            in_specs=[full((rows, width)), full((rows, row_width)), full((rows, 1))],
            out_specs=(full((rows, width + STAT_LANES)), full((req_count, PATH, row_width))),
        ),
    )(accepted, queries, new_kv, parent_rows)


def local_kernel(group, page_ids, lens_ref, q_ref, kv_ref, tree_ref, *rest):
    pages = rest[: len(page_ids) - 1]
    sum_ref, stat_ref = rest[-2:]
    req_count, page_size = kv_ref.shape[0], kv_ref.shape[1]
    page_refs = (kv_ref,) + tuple(pages)
    joined = page_ids == tuple(range(len(page_ids)))
    pair = 2 if (joined and req_count % 2 == 0) else 1
    span = page_size * len(page_refs)
    q_rows = pair * group * TREE
    stat_lanes = lax.broadcasted_iota(jnp.int32, (TREE, STAT_LANES), 1)
    row_owner = lax.broadcasted_iota(jnp.int32, (q_rows, 1), 0) // (group * TREE)
    for r0 in range(0, req_count, pair):
        members = list(range(r0, r0 + pair))
        query = jnp.concatenate([stacked_heads(q_ref, r * TREE, group) for r in members], axis=0)
        tree_rows = []
        for r in members:
            tree_rows.append(tree_ref[r * TREE : (r + 1) * TREE, group * HD : group * HD + STAT_LANES])
        m1 = jnp.concatenate([lane_pick(t, g) for t in tree_rows for g in range(group)], axis=0)
        l1 = jnp.concatenate([lane_pick(t, group + g) for t in tree_rows for g in range(group)], axis=0)
        a1 = jnp.concatenate([stacked_heads(tree_ref, r * TREE, group) for r in members], axis=0)
        blocks = [(m1, l1, a1)]
        if joined:
            length = jnp.zeros((q_rows, 1), jnp.int32)
            for k, r in enumerate(members):
                length = jnp.where(row_owner == k, lens_ref[r], length)
            sub = lax.broadcasted_iota(jnp.int32, (q_rows, pair * span), 0)
            lane = lax.broadcasted_iota(jnp.int32, (q_rows, pair * span), 1)
            valid = ((sub // (group * TREE)) == (lane // span)) & ((lane % span) < length)
            keys = jnp.concatenate([ref[r, :, 0:HD] for r in members for ref in page_refs], axis=0)
            values = jnp.concatenate([ref[r, :, HD : 2 * HD] for r in members for ref in page_refs], axis=0)
            blocks.append(attend(query, keys, values, valid, False))
        else:
            r = r0
            length = lens_ref[r]
            for page_index, page_ref in zip(page_ids, page_refs):
                positions = lax.broadcasted_iota(jnp.int32, (1, page_size), 1) + page_index * page_size
                blocks.append(attend(query, page_ref[r, :, 0:HD], page_ref[r, :, HD : 2 * HD],
                                     positions < length, False))
        top = blocks[0][0]
        for block in blocks[1:]:
            top = jnp.maximum(top, block[0])
        totals = jnp.zeros_like(top)
        weighted = jnp.zeros(blocks[0][2].shape, jnp.float32)
        for largest, part_totals, part_weighted in blocks:
            factor = jnp.exp(largest - top)
            totals = totals + factor * part_totals
            weighted = weighted + factor * part_weighted
        for k, r in enumerate(members):
            row0 = r * TREE
            stats = jnp.zeros((TREE, STAT_LANES), jnp.float32)
            for g in range(group):
                part = slice((k * group + g) * TREE, (k * group + g + 1) * TREE)
                sum_ref[row0 : row0 + TREE, g * HD : (g + 1) * HD] = weighted[part]
                stats = jnp.where(stat_lanes == g, top[part], stats)
                stats = jnp.where(stat_lanes == group + g, totals[part], stats)
            stat_ref[row0 : row0 + TREE, :] = stats


def local_partial(cache_lens, queries, kv_pool, tree_part, shipped, group):
    req_count, page_count, page_size, row_width = kv_pool.shape
    rows, width = queries.shape
    page_ids = (0,) + tuple(index for index, _ in shipped)
    page_spec = pl.BlockSpec((req_count, page_size, row_width), lambda i, a: (0, 0, 0))
    return pl.pallas_call(
        functools.partial(local_kernel, group, page_ids),
        out_shape=(
            jax.ShapeDtypeStruct((rows, width), jnp.float32),
            jax.ShapeDtypeStruct((rows, STAT_LANES), jnp.float32),
        ),
        grid_spec=pltpu.PrefetchScalarGridSpec(
            num_scalar_prefetch=1,
            grid=(1,),
            in_specs=[
                pl.BlockSpec((rows, width), lambda i, a: (0, 0)),
                pl.BlockSpec((req_count, None, page_size, row_width), lambda i, a: (0, 0, 0, 0)),
                pl.BlockSpec(tree_part.shape, lambda i, a: (0, 0)),
            ] + [page_spec for _ in shipped],
            out_specs=(
                pl.BlockSpec((rows, width), lambda i, a: (0, 0)),
                pl.BlockSpec((rows, STAT_LANES), lambda i, a: (0, 0)),
            ),
        ),
    )(cache_lens, queries, kv_pool, tree_part, *[page for _, page in shipped])


def holder_kernel(page_index, group, q_ref, kv_ref, order_ref, out_ref):
    req_count, page_size = kv_ref.shape[0], kv_ref.shape[1]
    rows = req_count * TREE
    extra = q_ref[rows : rows + EXTRA, :].astype(jnp.float32)
    length_row = extra[0:1, :] * 16.0 + extra[1:2, :]
    pair = 2 if req_count % 2 == 0 else 1
    q_rows = pair * group * TREE
    sub = lax.broadcasted_iota(jnp.int32, (q_rows, pair * page_size), 0)
    lane = lax.broadcasted_iota(jnp.int32, (q_rows, pair * page_size), 1)
    same_request = (sub // (group * TREE)) == (lane // page_size)
    positions = ((lane % page_size) + page_index * page_size).astype(jnp.float32)
    row_owner = lax.broadcasted_iota(jnp.int32, (q_rows, 1), 0) // (group * TREE)
    stat_lanes = lax.broadcasted_iota(jnp.int32, (TREE, STAT_LANES), 1)
    for r0 in range(0, req_count, pair):
        members = list(range(r0, r0 + pair))
        length = jnp.zeros((q_rows, 1), jnp.float32)
        for k, r in enumerate(members):
            length = jnp.where(row_owner == k, lane_pick(length_row, r), length)
        valid = same_request & (positions < length)
        query = jnp.concatenate([stacked_heads(q_ref, r * TREE, group) for r in members], axis=0)
        key = jnp.concatenate([kv_ref[r, :, 0:HD] for r in members], axis=0)
        value = jnp.concatenate([kv_ref[r, :, HD : 2 * HD] for r in members], axis=0)
        largest, totals, weighted = attend(query, key, value, valid, True)
        total_hi = totals.astype(jnp.bfloat16).astype(jnp.float32)
        total_lo = totals - total_hi
        for k, r in enumerate(members):
            row0 = r * TREE
            stats = jnp.zeros((TREE, STAT_LANES), jnp.float32)
            for g in range(group):
                part = slice((k * group + g) * TREE, (k * group + g + 1) * TREE)
                out_ref[row0 : row0 + TREE, g * HD : (g + 1) * HD] = weighted[part].astype(jnp.bfloat16)
                stats = jnp.where(stat_lanes == g, largest[part], stats)
                stats = jnp.where(stat_lanes == group + g, total_hi[part], stats)
                stats = jnp.where(stat_lanes == 2 * group + g, total_lo[part], stats)
            out_ref[row0 : row0 + TREE, group * HD : group * HD + STAT_LANES] = stats.astype(jnp.bfloat16)


def holder_partial(packed_queries, kv_pool, page_index, group, order_after):
    req_count, page_count, page_size, row_width = kv_pool.shape
    packed_rows, width = packed_queries.shape
    rows = req_count * TREE
    return pl.pallas_call(
        functools.partial(holder_kernel, page_index, group),
        out_shape=jax.ShapeDtypeStruct((rows, width + STAT_LANES), jnp.bfloat16),
        grid=(1,),
        in_specs=[
            pl.BlockSpec((packed_rows, width), lambda i: (0, 0)),
            pl.BlockSpec((req_count, None, page_size, row_width), lambda i: (0, page_index, 0, 0)),
            pl.BlockSpec((8, STAT_LANES), lambda i: (0, 0)),
        ],
        out_specs=pl.BlockSpec((rows, width + STAT_LANES), lambda i: (0, 0)),
    )(packed_queries, kv_pool, order_after)


def merge_kernel(group, count, sum_hbm, stat_hbm, *rest):
    returned = rest[:count]
    w_hbm, out_ref, sum_ref, stat_ref, w_ref, att_ref, sems = rest[count:]
    copies = [
        pltpu.make_async_copy(sum_hbm, sum_ref, sems.at[0]),
        pltpu.make_async_copy(stat_hbm, stat_ref, sems.at[1]),
        pltpu.make_async_copy(w_hbm, w_ref, sems.at[2]),
    ]
    for copy in copies:
        copy.start()
    copies[0].wait()
    copies[1].wait()
    rows = sum_ref.shape[0]
    for r in range(rows // TREE):
        row0 = r * TREE
        local_stats = stat_ref[row0 : row0 + TREE, :]
        for g in range(group):
            cols = slice(g * HD, (g + 1) * HD)
            blocks = [(lane_pick(local_stats, g), lane_pick(local_stats, group + g),
                       sum_ref[row0 : row0 + TREE, cols])]
            for part_ref in returned:
                stats = part_ref[row0 : row0 + TREE, group * HD : group * HD + STAT_LANES].astype(jnp.float32)
                totals = lane_pick(stats, group + g) + lane_pick(stats, 2 * group + g)
                blocks.append((lane_pick(stats, g), totals,
                               part_ref[row0 : row0 + TREE, cols].astype(jnp.float32)))
            top = blocks[0][0]
            for block in blocks[1:]:
                top = jnp.maximum(top, block[0])
            denominator = jnp.zeros_like(top)
            numerator = jnp.zeros((TREE, HD), jnp.float32)
            for largest, totals, weighted in blocks:
                factor = jnp.exp(largest - top)
                denominator = denominator + factor * totals
                numerator = numerator + factor * weighted
            att_ref[row0 : row0 + TREE, cols] = (numerator / denominator).astype(jnp.bfloat16)
    copies[2].wait()
    out_ref[...] = jnp.dot(
        att_ref[...], w_ref[...], preferred_element_type=jnp.float32
    ).astype(out_ref.dtype)


def merge_project(sums, stats, returned, w_out, group):
    rows, width = sums.shape
    part_width = returned[0].shape[1]
    model = w_out.shape[1]
    full = lambda shape: pl.BlockSpec(shape, lambda i: (0, 0))
    anywhere = pl.BlockSpec(memory_space=pl.ANY)
    return pl.pallas_call(
        functools.partial(merge_kernel, group, len(returned)),
        out_shape=jax.ShapeDtypeStruct((rows, model), jnp.bfloat16),
        grid=(1,),
        in_specs=[anywhere, anywhere]
        + [full((rows, part_width)) for _ in returned]
        + [anywhere],
        out_specs=full((rows, model)),
        scratch_shapes=[
            pltpu.VMEM(sums.shape, sums.dtype),
            pltpu.VMEM(stats.shape, stats.dtype),
            pltpu.VMEM(w_out.shape, w_out.dtype),
            pltpu.VMEM((rows, width), jnp.bfloat16),
            pltpu.SemaphoreType.DMA((3,)),
        ],
        compiler_params=pltpu.CompilerParams(vmem_limit_bytes=48 * 1024 * 1024),
    )(sums, stats, *returned, w_out)


def chain_reduce_scatter(product, axis):
    count = lax.axis_size(axis)
    me = lax.axis_index(axis)
    chunk = product.shape[0] // count
    pieces = product.reshape(count, chunk, product.shape[1])

    def piece(offset):
        return lax.dynamic_index_in_dim(pieces, (me + offset) % count, 0, keepdims=False)

    forward_hops = count // 2
    backward_hops = count - 1 - forward_hops
    forward = piece(forward_hops)
    backward = piece(-backward_hops) if backward_hops > 0 else None
    for step in range(1, forward_hops + 1):
        forward = shifted(forward, axis, 1)
        if backward is not None and step <= backward_hops:
            backward = shifted(backward, axis, -1)
        if step < forward_hops:
            forward = (forward.astype(jnp.float32)
                       + piece(forward_hops - step).astype(jnp.float32)).astype(jnp.bfloat16)
        if backward is not None and step < backward_hops:
            backward = (backward.astype(jnp.float32)
                        + piece(step - backward_hops).astype(jnp.float32)).astype(jnp.bfloat16)
    total = piece(0).astype(jnp.float32) + forward.astype(jnp.float32)
    if backward is not None:
        total = total + backward.astype(jnp.float32)
    return total


def pack_queries(queries, lengths):
    width = queries.shape[1]
    count = lengths.shape[0]
    pair = jnp.stack([lengths // 16, lengths % 16]).astype(jnp.bfloat16)
    extra = jnp.pad(pair, ((0, EXTRA - 2), (0, width - count)))
    return jnp.concatenate([queries, extra], axis=0)


def per_device(queries, new_kv, kv_pool, cache_lens, parents, accepted, residual, w_out, norm_gain):
    req_count, page_count, page_size, row_width = kv_pool.shape
    kv_local = row_width // (2 * HD)
    q_local = queries.shape[1] // HD
    group = q_local // kv_local

    shipped = [(p, shifted(kv_pool[:, p], "req", -p)) for p in SHIPPED_PAGES]
    visited = [p for p in range(1, page_count) if p not in SHIPPED_PAGES]
    packed_queries = pack_queries(queries, cache_lens)
    guests = [shifted(packed_queries, "req", p) for p in visited]
    tree_part, accepted_kv = tree_partial(accepted, queries, new_kv, parents, group)
    returned = []
    for page_index, guest in zip(visited, guests):
        part = holder_partial(guest, kv_pool, page_index, group, tree_part)
        returned.append(shifted(part, "req", -page_index))
    sums, stats = local_partial(cache_lens, queries, kv_pool, tree_part, shipped, group)

    product = merge_project(sums, stats, returned, w_out, group)
    summed = chain_reduce_scatter(product, "tp")
    hidden_out = (residual.astype(jnp.float32) + summed).astype(jnp.bfloat16)
    widened = hidden_out.astype(jnp.float32)
    normed = (
        widened * lax.rsqrt(jnp.mean(widened * widened, axis=-1, keepdims=True) + 1e-05) * norm_gain
    ).astype(jnp.bfloat16)
    return (hidden_out, normed, accepted_kv)


def solution(mesh):
    placed = (
        P("req", "tp"),
        P("req", "tp"),
        P("req", None, None, "tp"),
        P("req"),
        P("req", None),
        P("req"),
        P(("req", "tp"), None),
        P("tp", None),
        P(),
    )
    return jax.shard_map(
        per_device,
        mesh=mesh,
        in_specs=placed,
        out_specs=(P(("req", "tp"), None), P(("req", "tp"), None), P("req", None, "tp")),
        check_vma=False,
    )
```

```python
import functools

import jax
import jax.numpy as jnp
from jax import lax
from jax.experimental import pallas as pl
from jax.experimental.pallas import tpu as pltpu
from jax.sharding import PartitionSpec as P

HD = 128
TREE = 32
MAXD = 7
PATH = 8
EXTRA = 16
STAT_LANES = 128
SHIPPED_PAGES = (1,)


NEGATIVE = -1e30


def shifted(value, axis, steps):
    count = lax.axis_size(axis)
    pairs = [(source, (source + steps) % count) for source in range(count)]
    return lax.ppermute(value, axis, pairs)


def attend(query, key, value, valid, round_max):
    scores = lax.dot_general(
        query, key, (((1,), (1,)), ((), ())), preferred_element_type=jnp.float32
    ) * (HD ** (-0.5))
    scores = jnp.where(valid, scores, NEGATIVE)
    largest = jnp.max(scores, axis=1, keepdims=True)
    if round_max:
        largest = largest.astype(jnp.bfloat16).astype(jnp.float32)
    weights = jnp.where(valid, jnp.exp(scores - largest), 0.0)
    totals = jnp.sum(weights, axis=1, keepdims=True)
    weighted = jnp.dot(
        weights.astype(jnp.bfloat16), value, preferred_element_type=jnp.float32
    )
    return largest, totals, weighted


def lane_pick(block, lane):
    lanes = lax.broadcasted_iota(jnp.int32, block.shape, 1)
    return jnp.sum(jnp.where(lanes == lane, block, 0.0), axis=1, keepdims=True)


def stacked_heads(rows_ref, row0, group):
    parts = [rows_ref[row0 : row0 + TREE, g * HD : (g + 1) * HD] for g in range(group)]
    return jnp.concatenate(parts, axis=0)


def tree_kernel(group, acc_ref, q_ref, fresh_ref, parent_ref, part_ref, path_ref):
    rows = fresh_ref.shape[0]
    req_count = rows // TREE
    sub = lax.broadcasted_iota(jnp.int32, (rows, rows), 0)
    lane = lax.broadcasted_iota(jnp.int32, (rows, rows), 1)
    same_block = (sub // TREE) == (lane // TREE)
    reach = jnp.where((parent_ref[...] == lane) | (sub == lane), 1.0, 0.0)
    for _ in range(3):
        square = jnp.dot(reach.astype(jnp.bfloat16), reach.astype(jnp.bfloat16),
                         preferred_element_type=jnp.float32)
        reach = jnp.minimum(square, 1.0)
    inclusive = jnp.where(same_block & (sub <= lane), 1.0, 0.0).astype(jnp.bfloat16)
    sel_sub = lax.broadcasted_iota(jnp.int32, (req_count * PATH, rows), 0)
    sel_lane = lax.broadcasted_iota(jnp.int32, (req_count * PATH, rows), 1)
    chosen = jnp.zeros((req_count * PATH, rows), jnp.float32)
    for r in range(req_count):
        target = r * TREE + acc_ref[r]
        chosen = jnp.where((sel_sub // PATH == r) & (sel_lane == target), 1.0, chosen)
    on_path = jnp.dot(chosen.astype(jnp.bfloat16), reach.astype(jnp.bfloat16),
                      preferred_element_type=jnp.float32)
    rank = jnp.dot(on_path.astype(jnp.bfloat16), inclusive, preferred_element_type=jnp.float32)
    slot = (sel_sub % PATH).astype(jnp.float32)
    selector = jnp.where((rank - 1.0 == slot) & (on_path > 0.5), 1.0, 0.0)
    path = jnp.dot(selector.astype(jnp.bfloat16), fresh_ref[...],
                   preferred_element_type=jnp.float32).astype(path_ref.dtype)
    for r in range(req_count):
        path_ref[r] = path[r * PATH : (r + 1) * PATH]

    valid = jnp.concatenate([reach > 0.5] * group, axis=0)
    query = jnp.concatenate([q_ref[:, g * HD : (g + 1) * HD] for g in range(group)], axis=0)
    largest, totals, weighted = attend(query, fresh_ref[:, 0:HD], fresh_ref[:, HD : 2 * HD], valid, False)
    stat_lanes = lax.broadcasted_iota(jnp.int32, (rows, STAT_LANES), 1)
    stats = jnp.zeros((rows, STAT_LANES), jnp.float32)
    for g in range(group):
        part = slice(g * rows, (g + 1) * rows)
        stats = jnp.where(stat_lanes == g, largest[part], stats)
        stats = jnp.where(stat_lanes == group + g, totals[part], stats)
        part_ref[:, g * HD : (g + 1) * HD] = weighted[part]
    part_ref[:, group * HD : group * HD + STAT_LANES] = stats


def tree_partial(accepted, queries, new_kv, parents, group):
    rows, width = queries.shape
    req_count = parents.shape[0]
    row_width = new_kv.shape[1]
    offsets = TREE * jnp.arange(req_count, dtype=jnp.int32)[:, None]
    parent_rows = (parents + offsets).reshape(rows, 1)
    full = lambda shape: pl.BlockSpec(shape, lambda i, a: (0,) * len(shape))
    return pl.pallas_call(
        functools.partial(tree_kernel, group),
        out_shape=(
            jax.ShapeDtypeStruct((rows, width + STAT_LANES), jnp.float32),
            jax.ShapeDtypeStruct((req_count, PATH, row_width), jnp.bfloat16),
        ),
        grid_spec=pltpu.PrefetchScalarGridSpec(
            num_scalar_prefetch=1,
            grid=(1,),
            in_specs=[full((rows, width)), full((rows, row_width)), full((rows, 1))],
            out_specs=(full((rows, width + STAT_LANES)), full((req_count, PATH, row_width))),
        ),
    )(accepted, queries, new_kv, parent_rows)


def local_kernel(group, page_ids, lens_ref, q_ref, kv_ref, tree_ref, *rest):
    pages = rest[: len(page_ids) - 1]
    sum_ref, stat_ref = rest[-2:]
    req_count, page_size = kv_ref.shape[0], kv_ref.shape[1]
    page_refs = (kv_ref,) + tuple(pages)
    joined = page_ids == tuple(range(len(page_ids)))
    pair = 2 if (joined and req_count % 2 == 0) else 1
    span = page_size * len(page_refs)
    q_rows = pair * group * TREE
    stat_lanes = lax.broadcasted_iota(jnp.int32, (TREE, STAT_LANES), 1)
    row_owner = lax.broadcasted_iota(jnp.int32, (q_rows, 1), 0) // (group * TREE)
    for r0 in range(0, req_count, pair):
        members = list(range(r0, r0 + pair))
        query = jnp.concatenate([stacked_heads(q_ref, r * TREE, group) for r in members], axis=0)
        tree_rows = []
        for r in members:
            tree_rows.append(tree_ref[r * TREE : (r + 1) * TREE, group * HD : group * HD + STAT_LANES])
        m1 = jnp.concatenate([lane_pick(t, g) for t in tree_rows for g in range(group)], axis=0)
        l1 = jnp.concatenate([lane_pick(t, group + g) for t in tree_rows for g in range(group)], axis=0)
        a1 = jnp.concatenate([stacked_heads(tree_ref, r * TREE, group) for r in members], axis=0)
        blocks = [(m1, l1, a1)]
        if joined:
            length = jnp.zeros((q_rows, 1), jnp.int32)
            for k, r in enumerate(members):
                length = jnp.where(row_owner == k, lens_ref[r], length)
            sub = lax.broadcasted_iota(jnp.int32, (q_rows, pair * span), 0)
            lane = lax.broadcasted_iota(jnp.int32, (q_rows, pair * span), 1)
            valid = ((sub // (group * TREE)) == (lane // span)) & ((lane % span) < length)
            keys = jnp.concatenate([ref[r, :, 0:HD] for r in members for ref in page_refs], axis=0)
            values = jnp.concatenate([ref[r, :, HD : 2 * HD] for r in members for ref in page_refs], axis=0)
            blocks.append(attend(query, keys, values, valid, False))
        else:
            r = r0
            length = lens_ref[r]
            for page_index, page_ref in zip(page_ids, page_refs):
                positions = lax.broadcasted_iota(jnp.int32, (1, page_size), 1) + page_index * page_size
                blocks.append(attend(query, page_ref[r, :, 0:HD], page_ref[r, :, HD : 2 * HD],
                                     positions < length, False))
        top = blocks[0][0]
        for block in blocks[1:]:
            top = jnp.maximum(top, block[0])
        totals = jnp.zeros_like(top)
        weighted = jnp.zeros(blocks[0][2].shape, jnp.float32)
        for largest, part_totals, part_weighted in blocks:
            factor = jnp.exp(largest - top)
            totals = totals + factor * part_totals
            weighted = weighted + factor * part_weighted
        for k, r in enumerate(members):
            row0 = r * TREE
            stats = jnp.zeros((TREE, STAT_LANES), jnp.float32)
            for g in range(group):
                part = slice((k * group + g) * TREE, (k * group + g + 1) * TREE)
                sum_ref[row0 : row0 + TREE, g * HD : (g + 1) * HD] = weighted[part]
                stats = jnp.where(stat_lanes == g, top[part], stats)
                stats = jnp.where(stat_lanes == group + g, totals[part], stats)
            stat_ref[row0 : row0 + TREE, :] = stats


def local_partial(cache_lens, queries, kv_pool, tree_part, shipped, group):
    req_count, page_count, page_size, row_width = kv_pool.shape
    rows, width = queries.shape
    page_ids = (0,) + tuple(index for index, _ in shipped)
    page_spec = pl.BlockSpec((req_count, page_size, row_width), lambda i, a: (0, 0, 0))
    return pl.pallas_call(
        functools.partial(local_kernel, group, page_ids),
        out_shape=(
            jax.ShapeDtypeStruct((rows, width), jnp.float32),
            jax.ShapeDtypeStruct((rows, STAT_LANES), jnp.float32),
        ),
        grid_spec=pltpu.PrefetchScalarGridSpec(
            num_scalar_prefetch=1,
            grid=(1,),
            in_specs=[
                pl.BlockSpec((rows, width), lambda i, a: (0, 0)),
                pl.BlockSpec((req_count, None, page_size, row_width), lambda i, a: (0, 0, 0, 0)),
                pl.BlockSpec(tree_part.shape, lambda i, a: (0, 0)),
            ] + [page_spec for _ in shipped],
            out_specs=(
                pl.BlockSpec((rows, width), lambda i, a: (0, 0)),
                pl.BlockSpec((rows, STAT_LANES), lambda i, a: (0, 0)),
            ),
        ),
    )(cache_lens, queries, kv_pool, tree_part, *[page for _, page in shipped])


def holder_kernel(page_index, group, q_ref, kv_ref, order_ref, out_ref):
    req_count, page_size = kv_ref.shape[0], kv_ref.shape[1]
    rows = req_count * TREE
    extra = q_ref[rows : rows + EXTRA, :].astype(jnp.float32)
    length_row = extra[0:1, :] * 16.0 + extra[1:2, :]
    pair = 4 if req_count % 4 == 0 else 1
    q_rows = pair * group * TREE
    sub = lax.broadcasted_iota(jnp.int32, (q_rows, pair * page_size), 0)
    lane = lax.broadcasted_iota(jnp.int32, (q_rows, pair * page_size), 1)
    same_request = (sub // (group * TREE)) == (lane // page_size)
    positions = ((lane % page_size) + page_index * page_size).astype(jnp.float32)
    row_owner = lax.broadcasted_iota(jnp.int32, (q_rows, 1), 0) // (group * TREE)
    stat_lanes = lax.broadcasted_iota(jnp.int32, (TREE, STAT_LANES), 1)
    for r0 in range(0, req_count, pair):
        members = list(range(r0, r0 + pair))
        length = jnp.zeros((q_rows, 1), jnp.float32)
        for k, r in enumerate(members):
            length = jnp.where(row_owner == k, lane_pick(length_row, r), length)
        valid = same_request & (positions < length)
        query = jnp.concatenate([stacked_heads(q_ref, r * TREE, group) for r in members], axis=0)
        key = jnp.concatenate([kv_ref[r, :, 0:HD] for r in members], axis=0)
        value = jnp.concatenate([kv_ref[r, :, HD : 2 * HD] for r in members], axis=0)
        largest, totals, weighted = attend(query, key, value, valid, True)
        total_hi = totals.astype(jnp.bfloat16).astype(jnp.float32)
        total_lo = totals - total_hi
        for k, r in enumerate(members):
            row0 = r * TREE
            stats = jnp.zeros((TREE, STAT_LANES), jnp.float32)
            for g in range(group):
                part = slice((k * group + g) * TREE, (k * group + g + 1) * TREE)
                out_ref[row0 : row0 + TREE, g * HD : (g + 1) * HD] = weighted[part].astype(jnp.bfloat16)
                stats = jnp.where(stat_lanes == g, largest[part], stats)
                stats = jnp.where(stat_lanes == group + g, total_hi[part], stats)
                stats = jnp.where(stat_lanes == 2 * group + g, total_lo[part], stats)
            out_ref[row0 : row0 + TREE, group * HD : group * HD + STAT_LANES] = stats.astype(jnp.bfloat16)


def holder_partial(packed_queries, kv_pool, page_index, group, order_after):
    req_count, page_count, page_size, row_width = kv_pool.shape
    packed_rows, width = packed_queries.shape
    rows = req_count * TREE
    return pl.pallas_call(
        functools.partial(holder_kernel, page_index, group),
        out_shape=jax.ShapeDtypeStruct((rows, width + STAT_LANES), jnp.bfloat16),
        grid=(1,),
        in_specs=[
            pl.BlockSpec((packed_rows, width), lambda i: (0, 0)),
            pl.BlockSpec((req_count, None, page_size, row_width), lambda i: (0, page_index, 0, 0)),
            pl.BlockSpec((8, STAT_LANES), lambda i: (0, 0)),
        ],
        out_specs=pl.BlockSpec((rows, width + STAT_LANES), lambda i: (0, 0)),
    )(packed_queries, kv_pool, order_after)


def merge_kernel(group, count, sum_hbm, stat_hbm, *rest):
    returned = rest[:count]
    w_hbm, out_ref, sum_ref, stat_ref, w_ref, att_ref, sems = rest[count:]
    copies = [
        pltpu.make_async_copy(sum_hbm, sum_ref, sems.at[0]),
        pltpu.make_async_copy(stat_hbm, stat_ref, sems.at[1]),
        pltpu.make_async_copy(w_hbm, w_ref, sems.at[2]),
    ]
    for copy in copies:
        copy.start()
    copies[0].wait()
    copies[1].wait()
    rows = sum_ref.shape[0]
    for r in range(rows // TREE):
        row0 = r * TREE
        local_stats = stat_ref[row0 : row0 + TREE, :]
        for g in range(group):
            cols = slice(g * HD, (g + 1) * HD)
            blocks = [(lane_pick(local_stats, g), lane_pick(local_stats, group + g),
                       sum_ref[row0 : row0 + TREE, cols])]
            for part_ref in returned:
                stats = part_ref[row0 : row0 + TREE, group * HD : group * HD + STAT_LANES].astype(jnp.float32)
                totals = lane_pick(stats, group + g) + lane_pick(stats, 2 * group + g)
                blocks.append((lane_pick(stats, g), totals,
                               part_ref[row0 : row0 + TREE, cols].astype(jnp.float32)))
            top = blocks[0][0]
            for block in blocks[1:]:
                top = jnp.maximum(top, block[0])
            denominator = jnp.zeros_like(top)
            numerator = jnp.zeros((TREE, HD), jnp.float32)
            for largest, totals, weighted in blocks:
                factor = jnp.exp(largest - top)
                denominator = denominator + factor * totals
                numerator = numerator + factor * weighted
            att_ref[row0 : row0 + TREE, cols] = (numerator / denominator).astype(jnp.bfloat16)
    copies[2].wait()
    out_ref[...] = jnp.dot(
        att_ref[...], w_ref[...], preferred_element_type=jnp.float32
    ).astype(out_ref.dtype)


def merge_project(sums, stats, returned, w_out, group):
    rows, width = sums.shape
    part_width = returned[0].shape[1]
    model = w_out.shape[1]
    full = lambda shape: pl.BlockSpec(shape, lambda i: (0, 0))
    anywhere = pl.BlockSpec(memory_space=pl.ANY)
    return pl.pallas_call(
        functools.partial(merge_kernel, group, len(returned)),
        out_shape=jax.ShapeDtypeStruct((rows, model), jnp.bfloat16),
        grid=(1,),
        in_specs=[anywhere, anywhere]
        + [full((rows, part_width)) for _ in returned]
        + [anywhere],
        out_specs=full((rows, model)),
        scratch_shapes=[
            pltpu.VMEM(sums.shape, sums.dtype),
            pltpu.VMEM(stats.shape, stats.dtype),
            pltpu.VMEM(w_out.shape, w_out.dtype),
            pltpu.VMEM((rows, width), jnp.bfloat16),
            pltpu.SemaphoreType.DMA((3,)),
        ],
        compiler_params=pltpu.CompilerParams(vmem_limit_bytes=48 * 1024 * 1024),
    )(sums, stats, *returned, w_out)


def chain_reduce_scatter(product, axis):
    count = lax.axis_size(axis)
    me = lax.axis_index(axis)
    chunk = product.shape[0] // count
    pieces = product.reshape(count, chunk, product.shape[1])

    def piece(offset):
        return lax.dynamic_index_in_dim(pieces, (me + offset) % count, 0, keepdims=False)

    forward_hops = count // 2
    backward_hops = count - 1 - forward_hops
    forward = piece(forward_hops)
    backward = piece(-backward_hops) if backward_hops > 0 else None
    for step in range(1, forward_hops + 1):
        forward = shifted(forward, axis, 1)
        if backward is not None and step <= backward_hops:
            backward = shifted(backward, axis, -1)
        if step < forward_hops:
            forward = (forward.astype(jnp.float32)
                       + piece(forward_hops - step).astype(jnp.float32)).astype(jnp.bfloat16)
        if backward is not None and step < backward_hops:
            backward = (backward.astype(jnp.float32)
                        + piece(step - backward_hops).astype(jnp.float32)).astype(jnp.bfloat16)
    total = piece(0).astype(jnp.float32) + forward.astype(jnp.float32)
    if backward is not None:
        total = total + backward.astype(jnp.float32)
    return total


def pack_queries(queries, lengths):
    width = queries.shape[1]
    count = lengths.shape[0]
    pair = jnp.stack([lengths // 16, lengths % 16]).astype(jnp.bfloat16)
    extra = jnp.pad(pair, ((0, EXTRA - 2), (0, width - count)))
    return jnp.concatenate([queries, extra], axis=0)


def per_device(queries, new_kv, kv_pool, cache_lens, parents, accepted, residual, w_out, norm_gain):
    req_count, page_count, page_size, row_width = kv_pool.shape
    kv_local = row_width // (2 * HD)
    q_local = queries.shape[1] // HD
    group = q_local // kv_local

    shipped = [(p, shifted(kv_pool[:, p], "req", -p)) for p in SHIPPED_PAGES]
    visited = [p for p in range(1, page_count) if p not in SHIPPED_PAGES]
    packed_queries = pack_queries(queries, cache_lens)
    guests = [shifted(packed_queries, "req", p) for p in visited]
    tree_part, accepted_kv = tree_partial(accepted, queries, new_kv, parents, group)
    returned = []
    for page_index, guest in zip(visited, guests):
        part = holder_partial(guest, kv_pool, page_index, group, tree_part)
        returned.append(shifted(part, "req", -page_index))
    sums, stats = local_partial(cache_lens, queries, kv_pool, tree_part, shipped, group)

    product = merge_project(sums, stats, returned, w_out, group)
    summed = chain_reduce_scatter(product, "tp")
    hidden_out = (residual.astype(jnp.float32) + summed).astype(jnp.bfloat16)
    widened = hidden_out.astype(jnp.float32)
    normed = (
        widened * lax.rsqrt(jnp.mean(widened * widened, axis=-1, keepdims=True) + 1e-05) * norm_gain
    ).astype(jnp.bfloat16)
    return (hidden_out, normed, accepted_kv)


def solution(mesh):
    placed = (
        P("req", "tp"),
        P("req", "tp"),
        P("req", None, None, "tp"),
        P("req"),
        P("req", None),
        P("req"),
        P(("req", "tp"), None),
        P("tp", None),
        P(),
    )
    return jax.shard_map(
        per_device,
        mesh=mesh,
        in_specs=placed,
        out_specs=(P(("req", "tp"), None), P(("req", "tp"), None), P("req", None, "tp")),
        check_vma=False,
    )
```

```python
import functools

import jax
import jax.numpy as jnp
from jax import lax
from jax.experimental import pallas as pl
from jax.experimental.pallas import tpu as pltpu
from jax.sharding import PartitionSpec as P

HD = 128
TREE = 32
MAXD = 7
PATH = 8
EXTRA = 16
STAT_LANES = 128
SHIPPED_PAGES = (1,)


NEGATIVE = -1e30


def shifted(value, axis, steps):
    count = lax.axis_size(axis)
    pairs = [(source, (source + steps) % count) for source in range(count)]
    return lax.ppermute(value, axis, pairs)


def attend(query, key, value, valid, round_max):
    scores = lax.dot_general(
        query, key, (((1,), (1,)), ((), ())), preferred_element_type=jnp.float32
    ) * (HD ** (-0.5))
    scores = jnp.where(valid, scores, NEGATIVE)
    largest = jnp.max(scores, axis=1, keepdims=True)
    if round_max:
        largest = largest.astype(jnp.bfloat16).astype(jnp.float32)
    weights = jnp.where(valid, jnp.exp(scores - largest), 0.0)
    totals = jnp.sum(weights, axis=1, keepdims=True)
    weighted = jnp.dot(
        weights.astype(jnp.bfloat16), value, preferred_element_type=jnp.float32
    )
    return largest, totals, weighted


def lane_pick(block, lane):
    lanes = lax.broadcasted_iota(jnp.int32, block.shape, 1)
    return jnp.sum(jnp.where(lanes == lane, block, 0.0), axis=1, keepdims=True)


def stacked_heads(rows_ref, row0, group):
    parts = [rows_ref[row0 : row0 + TREE, g * HD : (g + 1) * HD] for g in range(group)]
    return jnp.concatenate(parts, axis=0)


def tree_kernel(group, acc_ref, q_ref, fresh_ref, parent_ref, part_ref, path_ref):
    rows = fresh_ref.shape[0]
    req_count = rows // TREE
    sub = lax.broadcasted_iota(jnp.int32, (rows, rows), 0)
    lane = lax.broadcasted_iota(jnp.int32, (rows, rows), 1)
    same_block = (sub // TREE) == (lane // TREE)
    reach = jnp.where((parent_ref[...] == lane) | (sub == lane), 1.0, 0.0)
    for _ in range(3):
        square = jnp.dot(reach.astype(jnp.bfloat16), reach.astype(jnp.bfloat16),
                         preferred_element_type=jnp.float32)
        reach = jnp.minimum(square, 1.0)
    inclusive = jnp.where(same_block & (sub <= lane), 1.0, 0.0).astype(jnp.bfloat16)
    sel_sub = lax.broadcasted_iota(jnp.int32, (req_count * PATH, rows), 0)
    sel_lane = lax.broadcasted_iota(jnp.int32, (req_count * PATH, rows), 1)
    chosen = jnp.zeros((req_count * PATH, rows), jnp.float32)
    for r in range(req_count):
        target = r * TREE + acc_ref[r]
        chosen = jnp.where((sel_sub // PATH == r) & (sel_lane == target), 1.0, chosen)
    on_path = jnp.dot(chosen.astype(jnp.bfloat16), reach.astype(jnp.bfloat16),
                      preferred_element_type=jnp.float32)
    rank = jnp.dot(on_path.astype(jnp.bfloat16), inclusive, preferred_element_type=jnp.float32)
    slot = (sel_sub % PATH).astype(jnp.float32)
    selector = jnp.where((rank - 1.0 == slot) & (on_path > 0.5), 1.0, 0.0)
    path = jnp.dot(selector.astype(jnp.bfloat16), fresh_ref[...],
                   preferred_element_type=jnp.float32).astype(path_ref.dtype)
    for r in range(req_count):
        path_ref[r] = path[r * PATH : (r + 1) * PATH]

    valid = jnp.concatenate([reach > 0.5] * group, axis=0)
    query = jnp.concatenate([q_ref[:, g * HD : (g + 1) * HD] for g in range(group)], axis=0)
    largest, totals, weighted = attend(query, fresh_ref[:, 0:HD], fresh_ref[:, HD : 2 * HD], valid, False)
    stat_lanes = lax.broadcasted_iota(jnp.int32, (rows, STAT_LANES), 1)
    stats = jnp.zeros((rows, STAT_LANES), jnp.float32)
    for g in range(group):
        part = slice(g * rows, (g + 1) * rows)
        stats = jnp.where(stat_lanes == g, largest[part], stats)
        stats = jnp.where(stat_lanes == group + g, totals[part], stats)
        part_ref[:, g * HD : (g + 1) * HD] = weighted[part]
    part_ref[:, group * HD : group * HD + STAT_LANES] = stats


def tree_partial(accepted, queries, new_kv, parents, group):
    rows, width = queries.shape
    req_count = parents.shape[0]
    row_width = new_kv.shape[1]
    offsets = TREE * jnp.arange(req_count, dtype=jnp.int32)[:, None]
    parent_rows = (parents + offsets).reshape(rows, 1)
    full = lambda shape: pl.BlockSpec(shape, lambda i, a: (0,) * len(shape))
    return pl.pallas_call(
        functools.partial(tree_kernel, group),
        out_shape=(
            jax.ShapeDtypeStruct((rows, width + STAT_LANES), jnp.float32),
            jax.ShapeDtypeStruct((req_count, PATH, row_width), jnp.bfloat16),
        ),
        grid_spec=pltpu.PrefetchScalarGridSpec(
            num_scalar_prefetch=1,
            grid=(1,),
            in_specs=[full((rows, width)), full((rows, row_width)), full((rows, 1))],
            out_specs=(full((rows, width + STAT_LANES)), full((req_count, PATH, row_width))),
        ),
    )(accepted, queries, new_kv, parent_rows)


def local_kernel(group, page_ids, lens_ref, q_ref, kv_ref, tree_ref, *rest):
    pages = rest[: len(page_ids) - 1]
    sum_ref, stat_ref = rest[-2:]
    req_count, page_size = kv_ref.shape[0], kv_ref.shape[1]
    page_refs = (kv_ref,) + tuple(pages)
    joined = page_ids == tuple(range(len(page_ids)))
    pair = 2 if (joined and req_count % 2 == 0) else 1
    span = page_size * len(page_refs)
    q_rows = pair * group * TREE
    stat_lanes = lax.broadcasted_iota(jnp.int32, (TREE, STAT_LANES), 1)
    row_owner = lax.broadcasted_iota(jnp.int32, (q_rows, 1), 0) // (group * TREE)
    for r0 in range(0, req_count, pair):
        members = list(range(r0, r0 + pair))
        query = jnp.concatenate([stacked_heads(q_ref, r * TREE, group) for r in members], axis=0)
        tree_rows = []
        for r in members:
            tree_rows.append(tree_ref[r * TREE : (r + 1) * TREE, group * HD : group * HD + STAT_LANES])
        m1 = jnp.concatenate([lane_pick(t, g) for t in tree_rows for g in range(group)], axis=0)
        l1 = jnp.concatenate([lane_pick(t, group + g) for t in tree_rows for g in range(group)], axis=0)
        a1 = jnp.concatenate([stacked_heads(tree_ref, r * TREE, group) for r in members], axis=0)
        blocks = [(m1, l1, a1)]
        if joined:
            length = jnp.zeros((q_rows, 1), jnp.int32)
            for k, r in enumerate(members):
                length = jnp.where(row_owner == k, lens_ref[r], length)
            sub = lax.broadcasted_iota(jnp.int32, (q_rows, pair * span), 0)
            lane = lax.broadcasted_iota(jnp.int32, (q_rows, pair * span), 1)
            valid = ((sub // (group * TREE)) == (lane // span)) & ((lane % span) < length)
            keys = jnp.concatenate([ref[r, :, 0:HD] for r in members for ref in page_refs], axis=0)
            values = jnp.concatenate([ref[r, :, HD : 2 * HD] for r in members for ref in page_refs], axis=0)
            blocks.append(attend(query, keys, values, valid, False))
        else:
            r = r0
            length = lens_ref[r]
            for page_index, page_ref in zip(page_ids, page_refs):
                positions = lax.broadcasted_iota(jnp.int32, (1, page_size), 1) + page_index * page_size
                blocks.append(attend(query, page_ref[r, :, 0:HD], page_ref[r, :, HD : 2 * HD],
                                     positions < length, False))
        top = blocks[0][0]
        for block in blocks[1:]:
            top = jnp.maximum(top, block[0])
        totals = jnp.zeros_like(top)
        weighted = jnp.zeros(blocks[0][2].shape, jnp.float32)
        for largest, part_totals, part_weighted in blocks:
            factor = jnp.exp(largest - top)
            totals = totals + factor * part_totals
            weighted = weighted + factor * part_weighted
        for k, r in enumerate(members):
            row0 = r * TREE
            stats = jnp.zeros((TREE, STAT_LANES), jnp.float32)
            for g in range(group):
                part = slice((k * group + g) * TREE, (k * group + g + 1) * TREE)
                sum_ref[row0 : row0 + TREE, g * HD : (g + 1) * HD] = weighted[part]
                stats = jnp.where(stat_lanes == g, top[part], stats)
                stats = jnp.where(stat_lanes == group + g, totals[part], stats)
            stat_ref[row0 : row0 + TREE, :] = stats


def local_partial(cache_lens, queries, kv_pool, tree_part, shipped, group):
    req_count, page_count, page_size, row_width = kv_pool.shape
    rows, width = queries.shape
    page_ids = (0,) + tuple(index for index, _ in shipped)
    page_spec = pl.BlockSpec((req_count, page_size, row_width), lambda i, a: (0, 0, 0))
    return pl.pallas_call(
        functools.partial(local_kernel, group, page_ids),
        out_shape=(
            jax.ShapeDtypeStruct((rows, width), jnp.float32),
            jax.ShapeDtypeStruct((rows, STAT_LANES), jnp.float32),
        ),
        grid_spec=pltpu.PrefetchScalarGridSpec(
            num_scalar_prefetch=1,
            grid=(1,),
            in_specs=[
                pl.BlockSpec((rows, width), lambda i, a: (0, 0)),
                pl.BlockSpec((req_count, None, page_size, row_width), lambda i, a: (0, 0, 0, 0)),
                pl.BlockSpec(tree_part.shape, lambda i, a: (0, 0)),
            ] + [page_spec for _ in shipped],
            out_specs=(
                pl.BlockSpec((rows, width), lambda i, a: (0, 0)),
                pl.BlockSpec((rows, STAT_LANES), lambda i, a: (0, 0)),
            ),
        ),
    )(cache_lens, queries, kv_pool, tree_part, *[page for _, page in shipped])


def holder_kernel(page_index, group, q_ref, kv_ref, order_ref, out_ref):
    req_count, page_size = kv_ref.shape[0], kv_ref.shape[1]
    rows = req_count * TREE
    extra = q_ref[rows : rows + EXTRA, :].astype(jnp.float32)
    length_row = extra[0:1, :] * 16.0 + extra[1:2, :]
    pair = 2 if req_count % 2 == 0 else 1
    q_rows = pair * group * TREE
    sub = lax.broadcasted_iota(jnp.int32, (q_rows, pair * page_size), 0)
    lane = lax.broadcasted_iota(jnp.int32, (q_rows, pair * page_size), 1)
    same_request = (sub // (group * TREE)) == (lane // page_size)
    positions = ((lane % page_size) + page_index * page_size).astype(jnp.float32)
    row_owner = lax.broadcasted_iota(jnp.int32, (q_rows, 1), 0) // (group * TREE)
    stat_lanes = lax.broadcasted_iota(jnp.int32, (TREE, STAT_LANES), 1)
    for r0 in range(0, req_count, pair):
        members = list(range(r0, r0 + pair))
        length = jnp.zeros((q_rows, 1), jnp.float32)
        for k, r in enumerate(members):
            length = jnp.where(row_owner == k, lane_pick(length_row, r), length)
        valid = same_request & (positions < length)
        query = jnp.concatenate([stacked_heads(q_ref, r * TREE, group) for r in members], axis=0)
        key = jnp.concatenate([kv_ref[r, :, 0:HD] for r in members], axis=0)
        value = jnp.concatenate([kv_ref[r, :, HD : 2 * HD] for r in members], axis=0)
        largest, totals, weighted = attend(query, key, value, valid, True)
        total_hi = totals.astype(jnp.bfloat16).astype(jnp.float32)
        total_lo = totals - total_hi
        for k, r in enumerate(members):
            row0 = r * TREE
            stats = jnp.zeros((TREE, STAT_LANES), jnp.float32)
            for g in range(group):
                part = slice((k * group + g) * TREE, (k * group + g + 1) * TREE)
                out_ref[row0 : row0 + TREE, g * HD : (g + 1) * HD] = weighted[part].astype(jnp.bfloat16)
                stats = jnp.where(stat_lanes == g, largest[part], stats)
                stats = jnp.where(stat_lanes == group + g, total_hi[part], stats)
                stats = jnp.where(stat_lanes == 2 * group + g, total_lo[part], stats)
            out_ref[row0 : row0 + TREE, group * HD : group * HD + STAT_LANES] = stats.astype(jnp.bfloat16)


def holder_partial(packed_queries, kv_pool, page_index, group, order_after):
    req_count, page_count, page_size, row_width = kv_pool.shape
    packed_rows, width = packed_queries.shape
    rows = req_count * TREE
    return pl.pallas_call(
        functools.partial(holder_kernel, page_index, group),
        out_shape=jax.ShapeDtypeStruct((rows, width + STAT_LANES), jnp.bfloat16),
        grid=(1,),
        in_specs=[
            pl.BlockSpec((packed_rows, width), lambda i: (0, 0)),
            pl.BlockSpec((req_count, None, page_size, row_width), lambda i: (0, page_index, 0, 0)),
            pl.BlockSpec((8, STAT_LANES), lambda i: (0, 0)),
        ],
        out_specs=pl.BlockSpec((rows, width + STAT_LANES), lambda i: (0, 0)),
    )(packed_queries, kv_pool, order_after)


def merge_kernel(group, count, sum_hbm, stat_hbm, *rest):
    returned = rest[:count]
    w_hbm, out_ref, sum_ref, stat_ref, w_ref, att_ref, sems = rest[count:]
    copies = [
        pltpu.make_async_copy(sum_hbm, sum_ref, sems.at[0]),
        pltpu.make_async_copy(stat_hbm, stat_ref, sems.at[1]),
        pltpu.make_async_copy(w_hbm, w_ref, sems.at[2]),
    ]
    for copy in copies:
        copy.start()
    copies[0].wait()
    copies[1].wait()
    rows = sum_ref.shape[0]
    for r in range(rows // TREE):
        row0 = r * TREE
        local_stats = stat_ref[row0 : row0 + TREE, :]
        for g in range(group):
            cols = slice(g * HD, (g + 1) * HD)
            blocks = [(lane_pick(local_stats, g), lane_pick(local_stats, group + g),
                       sum_ref[row0 : row0 + TREE, cols])]
            for part_ref in returned:
                stats = part_ref[row0 : row0 + TREE, group * HD : group * HD + STAT_LANES].astype(jnp.float32)
                totals = lane_pick(stats, group + g) + lane_pick(stats, 2 * group + g)
                blocks.append((lane_pick(stats, g), totals,
                               part_ref[row0 : row0 + TREE, cols].astype(jnp.float32)))
            top = blocks[0][0]
            for block in blocks[1:]:
                top = jnp.maximum(top, block[0])
            denominator = jnp.zeros_like(top)
            numerator = jnp.zeros((TREE, HD), jnp.float32)
            for largest, totals, weighted in blocks:
                factor = jnp.exp(largest - top)
                denominator = denominator + factor * totals
                numerator = numerator + factor * weighted
            att_ref[row0 : row0 + TREE, cols] = (numerator / denominator).astype(jnp.bfloat16)
    copies[2].wait()
    out_ref[...] = jnp.dot(
        att_ref[...], w_ref[...], preferred_element_type=jnp.float32
    ).astype(out_ref.dtype)


def merge_project(sums, stats, returned, w_out, group):
    rows, width = sums.shape
    part_width = returned[0].shape[1]
    model = w_out.shape[1]
    full = lambda shape: pl.BlockSpec(shape, lambda i: (0, 0))
    anywhere = pl.BlockSpec(memory_space=pl.ANY)
    return pl.pallas_call(
        functools.partial(merge_kernel, group, len(returned)),
        out_shape=jax.ShapeDtypeStruct((rows, model), jnp.bfloat16),
        grid=(1,),
        in_specs=[anywhere, anywhere]
        + [full((rows, part_width)) for _ in returned]
        + [anywhere],
        out_specs=full((rows, model)),
        scratch_shapes=[
            pltpu.VMEM(sums.shape, sums.dtype),
            pltpu.VMEM(stats.shape, stats.dtype),
            pltpu.VMEM(w_out.shape, w_out.dtype),
            pltpu.VMEM((rows, width), jnp.bfloat16),
            pltpu.SemaphoreType.DMA((3,)),
        ],
        compiler_params=pltpu.CompilerParams(vmem_limit_bytes=48 * 1024 * 1024),
    )(sums, stats, *returned, w_out)


def chain_reduce_scatter(product, axis):
    count = lax.axis_size(axis)
    me = lax.axis_index(axis)
    chunk = product.shape[0] // count
    pieces = product.reshape(count, chunk, product.shape[1])

    doubled = jnp.concatenate([pieces, pieces], axis=0)
    rotated = lax.dynamic_slice_in_dim(doubled, me, count, 0)

    def piece(offset):
        return rotated[offset % count]

    forward_hops = count // 2
    backward_hops = count - 1 - forward_hops
    forward = piece(forward_hops)
    backward = piece(-backward_hops) if backward_hops > 0 else None
    for step in range(1, forward_hops + 1):
        forward = shifted(forward, axis, 1)
        if backward is not None and step <= backward_hops:
            backward = shifted(backward, axis, -1)
        if step < forward_hops:
            forward = (forward.astype(jnp.float32)
                       + piece(forward_hops - step).astype(jnp.float32)).astype(jnp.bfloat16)
        if backward is not None and step < backward_hops:
            backward = (backward.astype(jnp.float32)
                        + piece(step - backward_hops).astype(jnp.float32)).astype(jnp.bfloat16)
    total = piece(0).astype(jnp.float32) + forward.astype(jnp.float32)
    if backward is not None:
        total = total + backward.astype(jnp.float32)
    return total


def pack_queries(queries, lengths):
    width = queries.shape[1]
    count = lengths.shape[0]
    pair = jnp.stack([lengths // 16, lengths % 16]).astype(jnp.bfloat16)
    extra = jnp.pad(pair, ((0, EXTRA - 2), (0, width - count)))
    return jnp.concatenate([queries, extra], axis=0)


def per_device(queries, new_kv, kv_pool, cache_lens, parents, accepted, residual, w_out, norm_gain):
    req_count, page_count, page_size, row_width = kv_pool.shape
    kv_local = row_width // (2 * HD)
    q_local = queries.shape[1] // HD
    group = q_local // kv_local

    shipped = [(p, shifted(kv_pool[:, p], "req", -p)) for p in SHIPPED_PAGES]
    visited = [p for p in range(1, page_count) if p not in SHIPPED_PAGES]
    packed_queries = pack_queries(queries, cache_lens)
    guests = [shifted(packed_queries, "req", p) for p in visited]
    tree_part, accepted_kv = tree_partial(accepted, queries, new_kv, parents, group)
    returned = []
    for page_index, guest in zip(visited, guests):
        part = holder_partial(guest, kv_pool, page_index, group, tree_part)
        returned.append(shifted(part, "req", -page_index))
    sums, stats = local_partial(cache_lens, queries, kv_pool, tree_part, shipped, group)

    product = merge_project(sums, stats, returned, w_out, group)
    summed = chain_reduce_scatter(product, "tp")
    hidden_out = (residual.astype(jnp.float32) + summed).astype(jnp.bfloat16)
    widened = hidden_out.astype(jnp.float32)
    normed = (
        widened * lax.rsqrt(jnp.mean(widened * widened, axis=-1, keepdims=True) + 1e-05) * norm_gain
    ).astype(jnp.bfloat16)
    return (hidden_out, normed, accepted_kv)


def solution(mesh):
    placed = (
        P("req", "tp"),
        P("req", "tp"),
        P("req", None, None, "tp"),
        P("req"),
        P("req", None),
        P("req"),
        P(("req", "tp"), None),
        P("tp", None),
        P(),
    )
    return jax.shard_map(
        per_device,
        mesh=mesh,
        in_specs=placed,
        out_specs=(P(("req", "tp"), None), P(("req", "tp"), None), P("req", None, "tp")),
        check_vma=False,
    )
```
